32 devices in a mesh: req: 2 (over x), ctx: 8 (over z, core), exp: 2 (over y).
Axes of the slice: x: 2, y: 2, z: 4, core: 2. Of those that a mesh axis runs over, the one named last changes fastest.
Arguments:
- query_states: bfloat16 [2, 512, 1024], P('req', 'ctx', 'exp'), may hold values from -6 to 6
- key_states: bfloat16 [2, 512, 1024], P('req', 'ctx', 'exp'), may hold values from -6 to 6
- value_states: bfloat16 [2, 512, 1024], P('req', 'ctx', 'exp'), may hold values from -6 to 6
- residual: bfloat16 [2, 512, 2048], P('req', ('ctx', 'exp')), may hold values from -6 to 6
- out_weight: bfloat16 [2048, 1024], P('ctx', 'exp'), may hold values from -0.1875 to 0.1875
- norm_gain: float32 [2048], replicated, may hold values from 0.1 to 1.9
- gate_weight: bfloat16 [8, 2048, 704], P('ctx', None, 'exp'), may hold values from -0.125 to 0.125
- up_weight: bfloat16 [8, 2048, 704], P('ctx', None, 'exp'), may hold values from -0.125 to 0.125
- down_weight: bfloat16 [8, 704, 2048], P('ctx', 'exp'), may hold values from -0.21875 to 0.21875
- routes: int32 [2, 512, 4], P('req', 'ctx'), may hold values from 0 to 7, all different within a row; in each aligned block of 64 rows (0 to 63, 64 to 127, ..., all dimensions but the last counted through in order) at most 48 rows name the same one
- route_weights: float32 [2, 512, 4], P('req', 'ctx'), may hold values from 0.1 to 1
- prompt_lengths: int32 [2], P('req'), may hold values from 128 to 512, as said below
Outputs:
- layer_out: bfloat16 [2, 512, 2048], P('req', ('ctx', 'exp'))
- cache_keys: bfloat16 [2, 512, 1024], P('req', 'ctx', 'exp')
- cache_values: bfloat16 [2, 512, 1024], P('req', 'ctx', 'exp')
The draws below stay inside these ranges and needn't reach their ends.
Inputs may be any that keep to these rules, and one draw needn't show every extreme that they name: `routes`: each row names 4 different experts; in each aligned block of 64 rows of a request no expert is named by more than 48 rows, a bound that some block reaches. `prompt_lengths`: one request has exactly 512 tokens.
All inputs are finite; a program needn't handle non-finite values.
Results may differ from the reference program's by a relative error of at most 0.019.
Values may be sent and summed in bfloat16 or wider, within the bound.
No kernel may reach another device: no remote copies, remote signals or barrier semaphores. Data moves between devices by JAX's collectives and lax.ppermute only.
A program may use at most 64 MiB of HBM per device.

```python
import math
import jax
import jax.numpy as jnp
import numpy as np
from jax import lax

D = 2048
HEADS = 8
HD = 128
FF = 704
TOP = 4
TOK_DEV = 64
SEQ = 512
REQS = 2
EXPERTS = 8
CAP = 48
N_CTX = 8


def draw_query_states(key, part):
    noise_vals = 1.3 * jax.random.truncated_normal(jax.random.fold_in(key, 1), -4.0, 4.0, (REQS, SEQ, HEADS, HD), jnp.float32)
    return noise_vals.reshape(REQS, SEQ, HEADS * HD).astype(jnp.bfloat16)


def draw_key_states(key, part):
    noise_vals = 1.3 * jax.random.truncated_normal(jax.random.fold_in(key, 2), -4.0, 4.0, (REQS, SEQ, HEADS, HD), jnp.float32)
    return noise_vals.reshape(REQS, SEQ, HEADS * HD).astype(jnp.bfloat16)


def draw_prompt_lengths(key, part):
    length_draw = jax.random.randint(jax.random.fold_in(key, 3), (REQS,), SEQ // 4, SEQ + 1, dtype=jnp.int32)
    length_draw = jnp.where(jnp.arange(REQS, dtype=jnp.int32) == 0, SEQ, length_draw).astype(jnp.int32)
    return jax.random.permutation(jax.random.fold_in(key, 4), length_draw)


def levels(own_key, shape, cuts, smallest, high):
    level = 1.0
    for position, shards_of in cuts:
        steps = jax.random.uniform(jax.random.fold_in(jax.random.fold_in(own_key, 6), position), (shards_of,), jnp.float32, smallest / len(cuts), high / len(cuts))
        level = level * jnp.repeat(jnp.exp(steps), shape[position] // shards_of).reshape((-1,) + (1,) * (len(shape) - 1 - position))
    return level


def deal_out(rng, own, number, rows, count, top, reach, skew):
    order = jax.random.permutation(rng, count)
    heavy_load, ordinary = shares(count, rows * top, reach, skew, True), shares(count, rows * top, reach, skew, False)
    places = jnp.arange(count)

    def named(sizes, offset_by):
        used = int((sizes > 0).sum())
        fixed = max(1, used // 4)
        passed = fixed + (places - fixed + offset_by * (used - fixed)) % max(1, count - fixed)
        return jnp.zeros((count,), jnp.int32).at[order[jnp.where(places < fixed, places, passed)]].set(jnp.asarray(sizes, jnp.int32))

    sizes = jnp.where(number % 4 == 0, named(heavy_load, number // 4), named(ordinary, number - number // 4 - 1))
    mixed = jax.random.permutation(jax.random.fold_in(own, 3), count)
    donor, receiver = mixed[0:count // 2 * 2:2], mixed[1:count // 2 * 2:2]
    margin = jnp.minimum(sizes[donor] - 1, reach - sizes[receiver]) // 2
    margin = jnp.where((donor == order[0]) | (receiver == order[0]) | (sizes[receiver] == 0), 0, jnp.maximum(margin, 0))
    passed = jax.random.randint(jax.random.fold_in(own, 4), (count // 2,), 0, 1 << 20) % (margin + 1)
    sizes = sizes.at[donor].add(-passed).at[receiver].add(passed)
    items = jnp.searchsorted(jnp.cumsum(sizes), jnp.arange(rows * top), side="right").astype(jnp.int32)
    table = items.reshape(top, rows).T
    table = table[jax.random.permutation(jax.random.fold_in(own, 1), rows)]
    offset_by = jax.random.randint(jax.random.fold_in(own, 2), (rows, 1), 0, top)
    return jnp.take_along_axis(table, (jnp.arange(top)[None, :] + offset_by) % top, axis=1)


def shares(number_of, total, reach, skew, full):
    weights = [(1 << 20) // math.isqrt(standing ** skew) + 1 for standing in range(1, number_of + 1)]
    largest = reach if full else min(reach, max(-(-total // number_of), total * weights[0] // sum(weights)))
    least = 1 if total - largest >= number_of - 1 else 0
    holding, spare = [largest] + [least] * (number_of - 1), total - largest - least * (number_of - 1)
    while spare > 0:
        movable = [i for i in range(1, number_of) if holding[i] < largest] or [i for i in range(1, number_of) if holding[i] < reach]
        whole, left = sum([weights[i] for i in movable]), spare
        for i in movable:
            more = min(reach - holding[i], max(1, left * weights[i] // whole), spare)
            holding[i] = holding[i] + more
            spare = spare - more
    return np.array(holding)


def gaussian(rng, dims, width, limit, split=(), kind=jnp.bfloat16):
    level = levels(rng, dims, split, -0.22, 0.18) if split else 1.0
    result = jax.random.normal(rng, dims, jnp.float32) * width * level
    return jnp.minimum(jnp.maximum(result, -limit), limit).astype(kind)


def setup_inputs(seed: int = 0) -> dict:
    key_list = jax.random.split(jax.random.key(seed), 13)
    query_states = draw_query_states(jax.random.fold_in(key_list[12], 71), 0)
    key_states = draw_key_states(jax.random.fold_in(key_list[12], 71), 0)
    value_states = gaussian(key_list[2], (REQS, SEQ, HEADS * HD), 1.0, 6.0, ((0, 2), (1, 8), (2, 2)))
    residual = gaussian(key_list[3], (REQS, SEQ, D), 1.0, 6.0, ((0, 2), (1, 16)))
    out_weight = gaussian(key_list[4], (D, HEADS * HD), (HEADS * HD) ** -0.5, 0.1875, ((0, 8), (1, 2)))
    norm_gain = jnp.clip(1.0 + 0.18 * jax.random.normal(key_list[5], (D,), jnp.float32), 0.1, 1.9)
    gate_weight = gaussian(key_list[6], (EXPERTS, D, FF), D ** -0.5, 0.125, ((0, 8), (2, 2)))
    up_weight = gaussian(key_list[7], (EXPERTS, D, FF), D ** -0.5, 0.125, ((0, 8), (2, 2)))
    down_weight = gaussian(key_list[8], (EXPERTS, FF, D), FF ** -0.5, 0.21875, ((0, 8), (1, 2)))
    routes_keys = jax.random.split(jax.random.fold_in(key_list[9], 1), REQS * SEQ // TOK_DEV)
    routes_turns = jax.random.permutation(jax.random.fold_in(key_list[9], 3), REQS * SEQ // TOK_DEV)
    routes = jax.vmap(lambda own, number: deal_out(jax.random.fold_in(key_list[9], 2), own, number, TOK_DEV, EXPERTS, TOP, CAP, 2))(routes_keys, routes_turns).reshape((REQS, SEQ, TOP))
    route_weights = jnp.clip(jnp.exp(math.log(1.0) - 2.3025851 * jax.random.uniform(key_list[10], (REQS, SEQ, TOP), jnp.float32) ** levels(key_list[10], (REQS, SEQ, TOP), ((0, 2), (1, 8)), -0.2, 0.2)), 0.1, 1.0)
    prompt_lengths = draw_prompt_lengths(jax.random.fold_in(key_list[12], 71), 0)
    return {"query_states": query_states, "key_states": key_states, "value_states": value_states, "residual": residual, "out_weight": out_weight, "norm_gain": norm_gain, "gate_weight": gate_weight, "up_weight": up_weight, "down_weight": down_weight, "routes": routes, "route_weights": route_weights, "prompt_lengths": prompt_lengths}


EPS = 1e-06
NEG = -1e+30

def row_positions(row_ids, half_block, n_groups):
    block_ids = row_ids // half_block
    device = block_ids // 2
    target = jnp.where(block_ids % 2 == 0, device, 2 * n_groups - 1 - device)
    return (target * half_block + row_ids % half_block).astype(jnp.int32)

def position_rows(spot_ids, half_block, n_groups):
    block_ids = spot_ids // half_block
    is_lower = block_ids < n_groups
    device = jnp.where(is_lower, block_ids, 2 * n_groups - 1 - block_ids)
    upper_half = jnp.where(is_lower, 0, 1)
    return ((device * 2 + upper_half) * half_block + spot_ids % half_block).astype(jnp.int32)

def slot_tables(route_block, weight_block, experts, capacity):
    tok_here, top_here = route_block.shape
    flat_ids = route_block.reshape(tok_here * top_here)
    hit_table = (flat_ids[:, None] == jnp.arange(experts, dtype=jnp.int32)[None, :]).astype(jnp.int32)
    before = jnp.cumsum(hit_table, axis=0) - hit_table
    slot_rank = lax.optimization_barrier(jnp.sum(before * hit_table, axis=1))
    slot_index = (flat_ids * capacity + slot_rank).astype(jnp.int32)
    slot_match = (jnp.arange(experts * capacity, dtype=jnp.int32)[:, None] == slot_index[None, :]).astype(jnp.float32)
    slot_match = slot_match.reshape(experts * capacity, tok_here, top_here)
    dispatch = lax.optimization_barrier(jnp.sum(slot_match, axis=2))
    combine = jnp.transpose(lax.optimization_barrier(jnp.sum(slot_match * weight_block[None, :, :].astype(jnp.float32), axis=2)))
    return (dispatch, combine)

def expert_ffn(token_rows, gate_matrix, up_matrix, down_matrix):
    gate_act = jnp.dot(token_rows, gate_matrix, preferred_element_type=jnp.float32)
    up_act = jnp.dot(token_rows, up_matrix, preferred_element_type=jnp.float32)
    hidden = (jax.nn.silu(gate_act) * up_act).astype(jnp.bfloat16)
    return jnp.dot(hidden, down_matrix, preferred_element_type=jnp.float32)

def attend_head(packed):
    query_head, key_head, value_head, length = packed
    spot_ids = jnp.arange(SEQ, dtype=jnp.int32)
    logits = jnp.dot(query_head, key_head.T, preferred_element_type=jnp.float32) * HD ** (-0.5)
    visible = (spot_ids[None, :] <= spot_ids[:, None]) & (spot_ids[None, :] < length)
    logits = jnp.where(visible, logits, NEG)
    row_max = lax.optimization_barrier(jnp.max(logits, axis=1, keepdims=True))
    weights = jnp.where(visible, jnp.exp(logits - row_max), 0.0)
    row_sum = lax.optimization_barrier(jnp.sum(weights, axis=1, keepdims=True))
    mixed = jnp.dot(weights.astype(jnp.bfloat16), value_head, preferred_element_type=jnp.float32)
    return (mixed / row_sum).astype(jnp.bfloat16)

def split_heads(states):
    return states.reshape(REQS, SEQ, HEADS, HD).transpose(0, 2, 1, 3).reshape(REQS * HEADS, SEQ, HD)

def reference(query_states, key_states, value_states, residual, out_weight, norm_gain, gate_weight, up_weight, down_weight, routes, route_weights, prompt_lengths):
    half_block = TOK_DEV // 2
    spot_ids = jnp.arange(SEQ, dtype=jnp.int32)
    rows_of = position_rows(spot_ids, half_block, N_CTX)
    pos_of = row_positions(spot_ids, half_block, N_CTX)
    query_pos = query_states[:, rows_of]
    key_pos = key_states[:, rows_of]
    value_pos = value_states[:, rows_of]
    lengths_rep = jnp.repeat(prompt_lengths, HEADS).astype(jnp.int32)
    mixed = lax.map(attend_head, (split_heads(query_pos), split_heads(key_pos), split_heads(value_pos), lengths_rep))
    mixed = mixed.reshape(REQS, HEADS, SEQ, HD).transpose(0, 2, 1, 3).reshape(REQS, SEQ, HEADS * HD)
    mixed_rows = mixed[:, pos_of]
    attn_proj = jnp.dot(mixed_rows.reshape(REQS * SEQ, HEADS * HD), out_weight.T, preferred_element_type=jnp.float32)
    stream = (residual.reshape(REQS * SEQ, D).astype(jnp.float32) + attn_proj).astype(jnp.bfloat16)
    stream_f = stream.astype(jnp.float32)
    mean_sq = lax.optimization_barrier(jnp.mean(stream_f * stream_f, axis=1, keepdims=True))
    normed = (stream_f * lax.rsqrt(mean_sq + EPS) * norm_gain).astype(jnp.bfloat16)
    normed = normed.reshape(REQS, SEQ, D)

    def block_tables(route_block, weight_block):
        return slot_tables(route_block, weight_block, EXPERTS, CAP)

    def run_expert(packed):
        return expert_ffn(packed[0], packed[1], packed[2], packed[3])

    def one_request(packed):
        normed_req, routes_req, weights_req = packed
        dispatch, combine = jax.vmap(block_tables)(routes_req.reshape(N_CTX, TOK_DEV, TOP), weights_req.reshape(N_CTX, TOK_DEV, TOP))
        sent = jnp.einsum('bst,btd->bsd', dispatch, normed_req.reshape(N_CTX, TOK_DEV, D).astype(jnp.float32), precision=lax.Precision.HIGHEST).astype(jnp.bfloat16)
        by_expert = sent.reshape(N_CTX, EXPERTS, CAP, D).transpose(1, 0, 2, 3).reshape(EXPERTS, N_CTX * CAP, D)
        produced = lax.map(run_expert, (by_expert, gate_weight, up_weight, down_weight))
        returned = produced.reshape(EXPERTS, N_CTX, CAP, D).transpose(1, 0, 2, 3).reshape(N_CTX, EXPERTS * CAP, D)
        moe = jnp.einsum('bts,bsd->btd', combine, returned, precision=lax.Precision.HIGHEST)
        return moe.reshape(SEQ, D)
    moe_all = lax.map(one_request, (normed, routes, route_weights))
    layer_out = (stream.reshape(REQS, SEQ, D).astype(jnp.float32) + moe_all).astype(jnp.bfloat16)
    return (layer_out, key_pos, value_pos)
```

```python
import jax
import jax.numpy as jnp
from jax import lax
from jax.sharding import PartitionSpec as P

D = 2048
HD = 128
TOP = 4


EPS = 1e-06
NEG = -1e30


def row_positions(row_ids, half_block, n_groups):
    block_ids = row_ids // half_block
    device = block_ids // 2
    target = jnp.where(block_ids % 2 == 0, device, 2 * n_groups - 1 - device)
    return target * half_block + row_ids % half_block


def slot_tables(route_block, weight_block, experts, capacity):
    tok_here, top_here = route_block.shape
    flat_ids = route_block.reshape(tok_here * top_here)
    hit_table = (flat_ids[:, None] == jnp.arange(experts, dtype=jnp.int32)[None, :]).astype(
        jnp.int32
    )
    before = jnp.cumsum(hit_table, axis=0) - hit_table
    slot_rank = jnp.sum(before * hit_table, axis=1)
    slot_index = flat_ids * capacity + slot_rank
    slot_match = (
        jnp.arange(experts * capacity, dtype=jnp.int32)[:, None] == slot_index[None, :]
    ).astype(jnp.float32)
    slot_match = slot_match.reshape(experts * capacity, tok_here, top_here)
    dispatch = jnp.sum(slot_match, axis=2)
    combine = jnp.transpose(jnp.sum(slot_match * weight_block[None, :, :], axis=2))
    return (dispatch, combine)


def expert_ffn(token_rows, gate_matrix, up_matrix, down_matrix):
    gate_act = jnp.dot(token_rows, gate_matrix, preferred_element_type=jnp.float32)
    up_act = jnp.dot(token_rows, up_matrix, preferred_element_type=jnp.float32)
    hidden = (jax.nn.silu(gate_act) * up_act).astype(jnp.bfloat16)
    return jnp.dot(hidden, down_matrix, preferred_element_type=jnp.float32)


def exp_swap(x):
    return lax.ppermute(x, "exp", perm=[(0, 1), (1, 0)])


def exp_reduce_rows(parts):
    if lax.axis_size("exp") != 2:
        return lax.psum_scatter(
            parts.astype(jnp.bfloat16), "exp", scatter_dimension=0, tiled=True
        ).astype(jnp.float32)
    half = parts.shape[0] // 2
    first = lax.axis_index("exp") == 0
    lower = parts[:half]
    upper = parts[half:]
    mine = jnp.where(first, lower, upper)
    theirs = jnp.where(first, upper, lower)
    got = exp_swap(theirs.astype(jnp.bfloat16))
    return mine + got.astype(jnp.float32)


def exp_gather_rows(rows):
    if lax.axis_size("exp") != 2:
        return lax.all_gather(rows, "exp", axis=0, tiled=True)
    got = exp_swap(rows)
    first = lax.axis_index("exp") == 0
    return jnp.where(
        first, jnp.concatenate([rows, got], axis=0), jnp.concatenate([got, rows], axis=0)
    )


def local(
    query_states,
    key_states,
    value_states,
    residual,
    out_weight,
    norm_gain,
    gate_weight,
    up_weight,
    down_weight,
    routes,
    route_weights,
    prompt_lengths,
):
    n_ctx = lax.axis_size("ctx")
    my_ctx = lax.axis_index("ctx")
    tok_here = query_states.shape[1]
    feat_width = query_states.shape[2]
    heads_dev = feat_width // HD
    half_block = tok_here // 2
    score_scale = HD ** (-0.5)
    length = prompt_lengths[0]
    local_ids = jnp.arange(tok_here, dtype=jnp.int32)
    query_pos = row_positions(my_ctx * tok_here + local_ids, half_block, n_ctx)
    decode_pos = my_ctx * tok_here + local_ids
    query_three = query_states[0].reshape(tok_here, heads_dev, HD)
    run_max = jnp.full((heads_dev, tok_here), NEG, jnp.float32)
    kv_here = jnp.concatenate([key_states[0], value_states[0]], axis=1)
    kv_all = lax.all_gather(kv_here, "ctx", axis=0, tiled=True)
    key_two = kv_all[:, :feat_width]
    value_two = kv_all[:, feat_width:]
    row_count = key_two.shape[0]
    key_pos = row_positions(jnp.arange(row_count, dtype=jnp.int32), half_block, n_ctx)
    pick_rows = (decode_pos[:, None] == key_pos[None, :]).astype(jnp.bfloat16)
    kept_keys = jnp.dot(pick_rows, key_two, preferred_element_type=jnp.float32)
    kept_values = jnp.dot(pick_rows, value_two, preferred_element_type=jnp.float32)
    old_max = run_max
    key_heads = key_two.reshape(row_count, heads_dev, HD)
    value_heads = value_two.reshape(row_count, heads_dev, HD)
    logits = (
        jnp.einsum("qhd,khd->hqk", query_three, key_heads, preferred_element_type=jnp.float32)
        * score_scale
    )
    visible = (key_pos[None, :] <= query_pos[:, None]) & (key_pos[None, :] < length)
    logits = jnp.where(visible[None], logits, NEG)
    new_max = jnp.maximum(old_max, jnp.max(logits, axis=2))
    weights = jnp.where(visible[None], jnp.exp(logits - new_max[:, :, None]), 0.0)
    new_sum = jnp.sum(weights, axis=2)
    gained = jnp.einsum(
        "hqk,khd->hqd",
        weights.astype(jnp.bfloat16),
        value_heads,
        preferred_element_type=jnp.float32,
    )
    inner_state = (new_max, new_sum, gained)
    run_max, run_sum, run_out, kept_keys, kept_values = inner_state + (kept_keys, kept_values)
    mixed = (run_out / run_sum[:, :, None]).astype(jnp.bfloat16)
    mixed = jnp.transpose(mixed, (1, 0, 2)).reshape(tok_here, feat_width)
    out_parts = jnp.einsum(
        "tc,oc->to",
        mixed,
        lax.all_gather(out_weight, "ctx", axis=0, tiled=True),
        preferred_element_type=jnp.float32,
    )
    head_total = exp_reduce_rows(out_parts)
    stream = (residual[0].astype(jnp.float32) + head_total).astype(jnp.bfloat16)
    stream_f = stream.astype(jnp.float32)
    mean_sq = jnp.mean(stream_f * stream_f, axis=1, keepdims=True)
    normed = (stream_f * lax.rsqrt(mean_sq + EPS) * norm_gain).astype(jnp.bfloat16)
    all_normed = exp_gather_rows(normed)
    capacity = min(tok_here, 2 * max(1, 3 * tok_here * TOP // (4 * n_ctx)))
    dispatch, combine = slot_tables(routes[0], route_weights[0], n_ctx, capacity)
    send_rows = jnp.dot(
        dispatch.astype(jnp.bfloat16), all_normed, preferred_element_type=jnp.float32
    ).astype(jnp.bfloat16)
    send_rows = send_rows.reshape(n_ctx, capacity, D)
    arrived = lax.all_to_all(send_rows, "ctx", split_axis=0, concat_axis=0, tiled=True)
    slot_count = arrived.shape[1]
    flat_rows = arrived.reshape(n_ctx * slot_count, D)
    produced = expert_ffn(flat_rows, gate_weight[0], up_weight[0], down_weight[0]).reshape(
        n_ctx, slot_count, D
    )
    served = lax.all_to_all(
        produced.astype(jnp.bfloat16), "ctx", split_axis=0, concat_axis=0, tiled=True
    ).astype(produced.dtype)
    results = served.reshape(n_ctx * capacity, D)
    moe_part = jnp.dot(
        combine, results, precision=lax.Precision.HIGHEST, preferred_element_type=jnp.float32
    )
    moe_rows = exp_reduce_rows(moe_part)
    layer_out = (stream.astype(jnp.float32) + moe_rows).astype(jnp.bfloat16)
    return (
        layer_out[None],
        kept_keys.astype(jnp.bfloat16)[None],
        kept_values.astype(jnp.bfloat16)[None],
    )


def solution(mesh):
    return jax.shard_map(
        local,
        mesh=mesh,
        in_specs=(
            P("req", "ctx", "exp"),
            P("req", "ctx", "exp"),
            P("req", "ctx", "exp"),
            P("req", ("ctx", "exp"), None),
            P("ctx", "exp"),
            P(),
            P("ctx", None, "exp"),
            P("ctx", None, "exp"),
            P("ctx", "exp", None),
            P("req", "ctx", None),
            P("req", "ctx", None),
            P("req"),
        ),
        out_specs=(P("req", ("ctx", "exp"), None), P("req", "ctx", "exp"), P("req", "ctx", "exp")),
        check_vma=False,
    )
```

```python
import jax
import jax.numpy as jnp
from jax import lax
from jax.sharding import PartitionSpec as P

D = 2048
HD = 128
TOP = 4


EPS = 1e-06
NEG = -1e30


def row_positions(row_ids, half_block, n_groups):
    block_ids = row_ids // half_block
    device = block_ids // 2
    target = jnp.where(block_ids % 2 == 0, device, 2 * n_groups - 1 - device)
    return target * half_block + row_ids % half_block


def slot_tables(route_block, weight_block, experts, capacity):
    tok_here, top_here = route_block.shape
    flat_ids = route_block.reshape(tok_here * top_here)
    hit_table = (flat_ids[:, None] == jnp.arange(experts, dtype=jnp.int32)[None, :]).astype(
        jnp.int32
    )
    before = jnp.cumsum(hit_table, axis=0) - hit_table
    slot_rank = jnp.sum(before * hit_table, axis=1)
    slot_index = flat_ids * capacity + slot_rank
    slot_match = (
        jnp.arange(experts * capacity, dtype=jnp.int32)[:, None] == slot_index[None, :]
    ).astype(jnp.float32)
    slot_match = slot_match.reshape(experts * capacity, tok_here, top_here)
    dispatch = jnp.sum(slot_match, axis=2)
    combine = jnp.transpose(jnp.sum(slot_match * weight_block[None, :, :], axis=2))
    return (dispatch, combine)


def expert_ffn(token_rows, gate_matrix, up_matrix, down_matrix):
    gate_act = jnp.dot(token_rows, gate_matrix, preferred_element_type=jnp.float32)
    up_act = jnp.dot(token_rows, up_matrix, preferred_element_type=jnp.float32)
    hidden = (jax.nn.silu(gate_act) * up_act).astype(jnp.bfloat16)
    return jnp.dot(hidden, down_matrix, preferred_element_type=jnp.float32)


def exp_swap(x):
    return lax.ppermute(x, "exp", perm=[(0, 1), (1, 0)])


def exp_reduce_rows(parts):
    if lax.axis_size("exp") != 2:
        return lax.psum_scatter(
            parts.astype(jnp.bfloat16), "exp", scatter_dimension=0, tiled=True
        ).astype(jnp.float32)
    half = parts.shape[0] // 2
    first = lax.axis_index("exp") == 0
    lower = parts[:half]
    upper = parts[half:]
    mine = jnp.where(first, lower, upper)
    theirs = jnp.where(first, upper, lower)
    got = exp_swap(theirs.astype(jnp.bfloat16))
    return mine + got.astype(jnp.float32)


def exp_gather_rows(rows):
    if lax.axis_size("exp") != 2:
        return lax.all_gather(rows, "exp", axis=0, tiled=True)
    got = exp_swap(rows)
    first = lax.axis_index("exp") == 0
    return jnp.where(
        first, jnp.concatenate([rows, got], axis=0), jnp.concatenate([got, rows], axis=0)
    )


def local(
    query_states,
    key_states,
    value_states,
    residual,
    out_weight,
    norm_gain,
    gate_weight,
    up_weight,
    down_weight,
    routes,
    route_weights,
    prompt_lengths,
):
    n_ctx = lax.axis_size("ctx")
    my_ctx = lax.axis_index("ctx")
    tok_here = query_states.shape[1]
    feat_width = query_states.shape[2]
    heads_dev = feat_width // HD
    half_block = tok_here // 2
    score_scale = HD ** (-0.5)
    length = prompt_lengths[0]
    local_ids = jnp.arange(tok_here, dtype=jnp.int32)
    query_pos = row_positions(my_ctx * tok_here + local_ids, half_block, n_ctx)
    decode_pos = my_ctx * tok_here + local_ids
    query_three = query_states[0].reshape(tok_here, heads_dev, HD)
    run_max = jnp.full((heads_dev, tok_here), NEG, jnp.float32)
    key_two = lax.all_gather(key_states, "ctx", axis=1, tiled=True)[0]
    value_two = lax.all_gather(value_states, "ctx", axis=1, tiled=True)[0]
    row_count = key_two.shape[0]
    key_pos = row_positions(jnp.arange(row_count, dtype=jnp.int32), half_block, n_ctx)
    pick_rows = (decode_pos[:, None] == key_pos[None, :]).astype(jnp.bfloat16)
    kept_keys = jnp.dot(pick_rows, key_two, preferred_element_type=jnp.float32)
    kept_values = jnp.dot(pick_rows, value_two, preferred_element_type=jnp.float32)
    old_max = run_max
    key_heads = key_two.reshape(row_count, heads_dev, HD)
    value_heads = value_two.reshape(row_count, heads_dev, HD)
    logits = (
        jnp.einsum("qhd,khd->hqk", query_three, key_heads, preferred_element_type=jnp.float32)
        * score_scale
    )
    visible = (key_pos[None, :] <= query_pos[:, None]) & (key_pos[None, :] < length)
    logits = jnp.where(visible[None], logits, NEG)
    new_max = jnp.maximum(old_max, jnp.max(logits, axis=2))
    weights = jnp.where(visible[None], jnp.exp(logits - new_max[:, :, None]), 0.0)
    new_sum = jnp.sum(weights, axis=2)
    gained = jnp.einsum(
        "hqk,khd->hqd",
        weights.astype(jnp.bfloat16),
        value_heads,
        preferred_element_type=jnp.float32,
    )
    inner_state = (new_max, new_sum, gained)
    run_max, run_sum, run_out, kept_keys, kept_values = inner_state + (kept_keys, kept_values)
    mixed = (run_out / run_sum[:, :, None]).astype(jnp.bfloat16)
    mixed = jnp.transpose(mixed, (1, 0, 2)).reshape(tok_here, feat_width)
    out_parts = jnp.einsum(
        "tc,oc->to",
        mixed,
        lax.all_gather(out_weight, "ctx", axis=0, tiled=True),
        preferred_element_type=jnp.float32,
    )
    head_total = exp_reduce_rows(out_parts)
    stream = (residual[0].astype(jnp.float32) + head_total).astype(jnp.bfloat16)
    stream_f = stream.astype(jnp.float32)
    mean_sq = jnp.mean(stream_f * stream_f, axis=1, keepdims=True)
    normed = (stream_f * lax.rsqrt(mean_sq + EPS) * norm_gain).astype(jnp.bfloat16)
    all_normed = exp_gather_rows(normed)
    capacity = min(tok_here, 2 * max(1, 3 * tok_here * TOP // (4 * n_ctx)))
    dispatch, combine = slot_tables(routes[0], route_weights[0], n_ctx, capacity)
    send_rows = jnp.dot(
        dispatch.astype(jnp.bfloat16), all_normed, preferred_element_type=jnp.float32
    ).astype(jnp.bfloat16)
    send_rows = send_rows.reshape(n_ctx, capacity, D)
    arrived = lax.all_to_all(send_rows, "ctx", split_axis=0, concat_axis=0, tiled=True)
    slot_count = arrived.shape[1]
    flat_rows = arrived.reshape(n_ctx * slot_count, D)
    produced = expert_ffn(flat_rows, gate_weight[0], up_weight[0], down_weight[0]).reshape(
        n_ctx, slot_count, D
    )
    served = lax.all_to_all(
        produced.astype(jnp.bfloat16), "ctx", split_axis=0, concat_axis=0, tiled=True
    ).astype(produced.dtype)
    results = served.reshape(n_ctx * capacity, D)
    moe_part = jnp.dot(
        combine, results, precision=lax.Precision.HIGHEST, preferred_element_type=jnp.float32
    )
    moe_rows = exp_reduce_rows(moe_part)
    layer_out = (stream.astype(jnp.float32) + moe_rows).astype(jnp.bfloat16)
    return (
        layer_out[None],
        kept_keys.astype(jnp.bfloat16)[None],
        kept_values.astype(jnp.bfloat16)[None],
    )


def solution(mesh):
    return jax.shard_map(
        local,
        mesh=mesh,
        in_specs=(
            P("req", "ctx", "exp"),
            P("req", "ctx", "exp"),
            P("req", "ctx", "exp"),
            P("req", ("ctx", "exp"), None),
            P("ctx", "exp"),
            P(),
            P("ctx", None, "exp"),
            P("ctx", None, "exp"),
            P("ctx", "exp", None),
            P("req", "ctx", None),
            P("req", "ctx", None),
            P("req"),
        ),
        out_specs=(P("req", ("ctx", "exp"), None), P("req", "ctx", "exp"), P("req", "ctx", "exp")),
        check_vma=False,
    )
```

```python
import jax
import jax.numpy as jnp
from jax import lax
from jax.sharding import PartitionSpec as P

D = 2048
HD = 128
TOP = 4


EPS = 1e-06
NEG = -1e30


def row_positions(row_ids, half_block, n_groups):
    block_ids = row_ids // half_block
    device = block_ids // 2
    target = jnp.where(block_ids % 2 == 0, device, 2 * n_groups - 1 - device)
    return target * half_block + row_ids % half_block


def slot_tables(route_block, weight_block, experts, capacity):
    tok_here, top_here = route_block.shape
    flat_ids = route_block.reshape(tok_here * top_here)
    hit_table = (flat_ids[:, None] == jnp.arange(experts, dtype=jnp.int32)[None, :]).astype(
        jnp.int32
    )
    before = jnp.cumsum(hit_table, axis=0) - hit_table
    slot_rank = jnp.sum(before * hit_table, axis=1)
    slot_index = flat_ids * capacity + slot_rank
    slot_match = (
        jnp.arange(experts * capacity, dtype=jnp.int32)[:, None] == slot_index[None, :]
    ).astype(jnp.float32)
    slot_match = slot_match.reshape(experts * capacity, tok_here, top_here)
    dispatch = jnp.sum(slot_match, axis=2)
    combine = jnp.transpose(jnp.sum(slot_match * weight_block[None, :, :], axis=2))
    return (dispatch, combine)


def expert_ffn(token_rows, gate_matrix, up_matrix, down_matrix):
    gate_act = jnp.dot(token_rows, gate_matrix, preferred_element_type=jnp.float32)
    up_act = jnp.dot(token_rows, up_matrix, preferred_element_type=jnp.float32)
    hidden = (jax.nn.silu(gate_act) * up_act).astype(jnp.bfloat16)
    return jnp.dot(hidden, down_matrix, preferred_element_type=jnp.float32)


def exp_swap(x):
    return lax.ppermute(x, "exp", perm=[(0, 1), (1, 0)])


def exp_reduce_rows(parts):
    if lax.axis_size("exp") != 2:
        return lax.psum_scatter(
            parts.astype(jnp.bfloat16), "exp", scatter_dimension=0, tiled=True
        ).astype(jnp.float32)
    half = parts.shape[0] // 2
    first = lax.axis_index("exp") == 0
    lower = parts[:half]
    upper = parts[half:]
    mine = jnp.where(first, lower, upper)
    theirs = jnp.where(first, upper, lower)
    got = exp_swap(theirs.astype(jnp.bfloat16))
    return mine + got.astype(jnp.float32)


def exp_gather_rows(rows):
    if lax.axis_size("exp") != 2:
        return lax.all_gather(rows, "exp", axis=0, tiled=True)
    got = exp_swap(rows)
    first = lax.axis_index("exp") == 0
    return jnp.where(
        first, jnp.concatenate([rows, got], axis=0), jnp.concatenate([got, rows], axis=0)
    )


def moe_whole_rows(normed, dispatch, combine, gate_matrix, up_matrix, down_matrix, n_ctx, capacity):
    all_normed = lax.all_gather(normed, "exp", axis=0, tiled=True)
    send_rows = jnp.dot(
        dispatch.astype(jnp.bfloat16), all_normed, preferred_element_type=jnp.float32
    ).astype(jnp.bfloat16)
    send_rows = send_rows.reshape(n_ctx, capacity, D)
    arrived = lax.all_to_all(send_rows, "ctx", split_axis=0, concat_axis=0, tiled=True)
    flat_rows = arrived.reshape(n_ctx * capacity, D)
    produced = expert_ffn(flat_rows, gate_matrix, up_matrix, down_matrix).reshape(
        n_ctx, capacity, D
    )
    served = lax.all_to_all(
        produced.astype(jnp.bfloat16), "ctx", split_axis=0, concat_axis=0, tiled=True
    )
    results = served.reshape(n_ctx * capacity, D).astype(jnp.float32)
    moe_part = jnp.dot(
        combine, results, precision=lax.Precision.HIGHEST, preferred_element_type=jnp.float32
    )
    return lax.psum_scatter(
        moe_part.astype(jnp.bfloat16), "exp", scatter_dimension=0, tiled=True
    ).astype(jnp.float32)


def halves(x, first, axis):
    size = x.shape[axis] // 2
    lower = lax.slice_in_dim(x, 0, size, axis=axis)
    upper = lax.slice_in_dim(x, size, 2 * size, axis=axis)
    return jnp.where(first, lower, upper), jnp.where(first, upper, lower)


def join(mine, theirs, first, axis):
    return jnp.where(
        first,
        jnp.concatenate([mine, theirs], axis=axis),
        jnp.concatenate([theirs, mine], axis=axis),
    )


def moe_column_halves(normed, dispatch, combine, gate_matrix, up_matrix, down_matrix, n_ctx, capacity):
    my_exp = lax.axis_index("exp")
    first = my_exp == 0
    half_d = normed.shape[1] // 2
    my_cols, other_cols = halves(normed, first, 1)
    tokens_cols = join(my_cols, exp_swap(other_cols), first, 0)
    send_rows = jnp.dot(
        dispatch.astype(jnp.bfloat16), tokens_cols, preferred_element_type=jnp.float32
    ).astype(jnp.bfloat16)
    arrived = lax.all_to_all(
        send_rows.reshape(n_ctx, capacity, half_d), "ctx", split_axis=0, concat_axis=0, tiled=True
    ).reshape(n_ctx * capacity, half_d)
    partner_cols = exp_swap(arrived)
    my_start = my_exp * half_d
    other_start = (1 - my_exp) * half_d
    gate_mine = lax.dynamic_slice_in_dim(gate_matrix, my_start, half_d, axis=0)
    gate_other = lax.dynamic_slice_in_dim(gate_matrix, other_start, half_d, axis=0)
    up_mine = lax.dynamic_slice_in_dim(up_matrix, my_start, half_d, axis=0)
    up_other = lax.dynamic_slice_in_dim(up_matrix, other_start, half_d, axis=0)
    gate_act = jnp.dot(arrived, gate_mine, preferred_element_type=jnp.float32) + jnp.dot(
        partner_cols, gate_other, preferred_element_type=jnp.float32
    )
    up_act = jnp.dot(arrived, up_mine, preferred_element_type=jnp.float32) + jnp.dot(
        partner_cols, up_other, preferred_element_type=jnp.float32
    )
    hidden = (jax.nn.silu(gate_act) * up_act).astype(jnp.bfloat16)
    down_other = lax.dynamic_slice_in_dim(down_matrix, other_start, half_d, axis=1)
    down_mine = lax.dynamic_slice_in_dim(down_matrix, my_start, half_d, axis=1)
    out_other = jnp.dot(hidden, down_other, preferred_element_type=jnp.float32)
    got_other = exp_swap(out_other.astype(jnp.bfloat16))
    out_mine = jnp.dot(hidden, down_mine, preferred_element_type=jnp.float32)
    summed = (out_mine + got_other.astype(jnp.float32)).astype(jnp.bfloat16)
    served = lax.all_to_all(
        summed.reshape(n_ctx, capacity, half_d), "ctx", split_axis=0, concat_axis=0, tiled=True
    ).reshape(n_ctx * capacity, half_d)
    moe_half = jnp.dot(
        combine,
        served.astype(jnp.float32),
        precision=lax.Precision.HIGHEST,
        preferred_element_type=jnp.float32,
    )
    my_tok, other_tok = halves(moe_half, first, 0)
    got_tok = exp_swap(other_tok.astype(jnp.bfloat16)).astype(jnp.float32)
    return join(my_tok, got_tok, first, 1)


def local(
    query_states,
    key_states,
    value_states,
    residual,
    out_weight,
    norm_gain,
    gate_weight,
    up_weight,
    down_weight,
    routes,
    route_weights,
    prompt_lengths,
):
    n_ctx = lax.axis_size("ctx")
    my_ctx = lax.axis_index("ctx")
    tok_here = query_states.shape[1]
    feat_width = query_states.shape[2]
    heads_dev = feat_width // HD
    half_block = tok_here // 2
    score_scale = HD ** (-0.5)
    length = prompt_lengths[0]
    local_ids = jnp.arange(tok_here, dtype=jnp.int32)
    query_pos = row_positions(my_ctx * tok_here + local_ids, half_block, n_ctx)
    decode_pos = my_ctx * tok_here + local_ids
    query_three = query_states[0].reshape(tok_here, heads_dev, HD)
    run_max = jnp.full((heads_dev, tok_here), NEG, jnp.float32)
    key_two = lax.all_gather(key_states, "ctx", axis=1, tiled=True)[0]
    value_two = lax.all_gather(value_states, "ctx", axis=1, tiled=True)[0]
    row_count = key_two.shape[0]
    key_pos = row_positions(jnp.arange(row_count, dtype=jnp.int32), half_block, n_ctx)
    pick_rows = (decode_pos[:, None] == key_pos[None, :]).astype(jnp.bfloat16)
    kept_keys = jnp.dot(pick_rows, key_two, preferred_element_type=jnp.float32)
    kept_values = jnp.dot(pick_rows, value_two, preferred_element_type=jnp.float32)
    old_max = run_max
    key_heads = key_two.reshape(row_count, heads_dev, HD)
    value_heads = value_two.reshape(row_count, heads_dev, HD)
    logits = (
        jnp.einsum("qhd,khd->hqk", query_three, key_heads, preferred_element_type=jnp.float32)
        * score_scale
    )
    visible = (key_pos[None, :] <= query_pos[:, None]) & (key_pos[None, :] < length)
    logits = jnp.where(visible[None], logits, NEG)
    new_max = jnp.maximum(old_max, jnp.max(logits, axis=2))
    weights = jnp.where(visible[None], jnp.exp(logits - new_max[:, :, None]), 0.0)
    new_sum = jnp.sum(weights, axis=2)
    gained = jnp.einsum(
        "hqk,khd->hqd",
        weights.astype(jnp.bfloat16),
        value_heads,
        preferred_element_type=jnp.float32,
    )
    inner_state = (new_max, new_sum, gained)
    run_max, run_sum, run_out, kept_keys, kept_values = inner_state + (kept_keys, kept_values)
    mixed = (run_out / run_sum[:, :, None]).astype(jnp.bfloat16)
    mixed = jnp.transpose(mixed, (1, 0, 2)).reshape(tok_here, feat_width)
    out_parts = jnp.einsum(
        "tc,oc->to",
        mixed,
        lax.all_gather(out_weight, "ctx", axis=0, tiled=True),
        preferred_element_type=jnp.float32,
    )
    head_total = exp_reduce_rows(out_parts)
    stream = (residual[0].astype(jnp.float32) + head_total).astype(jnp.bfloat16)
    stream_f = stream.astype(jnp.float32)
    mean_sq = jnp.mean(stream_f * stream_f, axis=1, keepdims=True)
    normed = (stream_f * lax.rsqrt(mean_sq + EPS) * norm_gain).astype(jnp.bfloat16)
    capacity = min(tok_here, 2 * max(1, 3 * tok_here * TOP // (4 * n_ctx)))
    dispatch, combine = slot_tables(routes[0], route_weights[0], n_ctx, capacity)
    if lax.axis_size("exp") == 2:
        moe_rows = moe_column_halves(
            normed, dispatch, combine, gate_weight[0], up_weight[0], down_weight[0], n_ctx, capacity
        )
    else:
        moe_rows = moe_whole_rows(
            normed, dispatch, combine, gate_weight[0], up_weight[0], down_weight[0], n_ctx, capacity
        )
    layer_out = (stream.astype(jnp.float32) + moe_rows).astype(jnp.bfloat16)
    return (
        layer_out[None],
        kept_keys.astype(jnp.bfloat16)[None],
        kept_values.astype(jnp.bfloat16)[None],
    )


def solution(mesh):
    return jax.shard_map(
        local,
        mesh=mesh,
        in_specs=(
            P("req", "ctx", "exp"),
            P("req", "ctx", "exp"),
            P("req", "ctx", "exp"),
            P("req", ("ctx", "exp"), None),
            P("ctx", "exp"),
            P(),
            P("ctx", None, "exp"),
            P("ctx", None, "exp"),
            P("ctx", "exp", None),
            P("req", "ctx", None),
            P("req", "ctx", None),
            P("req"),
        ),
        out_specs=(P("req", ("ctx", "exp"), None), P("req", "ctx", "exp"), P("req", "ctx", "exp")),
        check_vma=False,
    )
```

```python
import jax
import jax.numpy as jnp
from jax import lax
from jax.sharding import PartitionSpec as P

D = 2048
HD = 128
TOP = 4


EPS = 1e-06
NEG = -1e30


def row_positions(row_ids, half_block, n_groups):
    block_ids = row_ids // half_block
    device = block_ids // 2
    target = jnp.where(block_ids % 2 == 0, device, 2 * n_groups - 1 - device)
    return target * half_block + row_ids % half_block


def slot_tables(route_block, weight_block, experts, capacity):
    tok_here, top_here = route_block.shape
    flat_ids = route_block.reshape(tok_here * top_here)
    hit_table = (flat_ids[:, None] == jnp.arange(experts, dtype=jnp.int32)[None, :]).astype(
        jnp.int32
    )
    before = jnp.cumsum(hit_table, axis=0) - hit_table
    slot_rank = jnp.sum(before * hit_table, axis=1)
    slot_index = flat_ids * capacity + slot_rank
    slot_match = (
        jnp.arange(experts * capacity, dtype=jnp.int32)[:, None] == slot_index[None, :]
    ).astype(jnp.float32)
    slot_match = slot_match.reshape(experts * capacity, tok_here, top_here)
    dispatch = jnp.sum(slot_match, axis=2)
    combine = jnp.transpose(jnp.sum(slot_match * weight_block[None, :, :], axis=2))
    return (dispatch, combine)


def expert_ffn(token_rows, gate_matrix, up_matrix, down_matrix):
    gate_act = jnp.dot(token_rows, gate_matrix, preferred_element_type=jnp.float32)
    up_act = jnp.dot(token_rows, up_matrix, preferred_element_type=jnp.float32)
    hidden = (jax.nn.silu(gate_act) * up_act).astype(jnp.bfloat16)
    return jnp.dot(hidden, down_matrix, preferred_element_type=jnp.float32)


def exp_swap(x):
    return lax.ppermute(x, "exp", perm=[(0, 1), (1, 0)])


def exp_reduce_rows(parts):
    if lax.axis_size("exp") != 2:
        return lax.psum_scatter(
            parts.astype(jnp.bfloat16), "exp", scatter_dimension=0, tiled=True
        ).astype(jnp.float32)
    half = parts.shape[0] // 2
    first = lax.axis_index("exp") == 0
    lower = parts[:half]
    upper = parts[half:]
    mine = jnp.where(first, lower, upper)
    theirs = jnp.where(first, upper, lower)
    got = exp_swap(theirs.astype(jnp.bfloat16))
    return mine + got.astype(jnp.float32)


def exp_gather_rows(rows):
    if lax.axis_size("exp") != 2:
        return lax.all_gather(rows, "exp", axis=0, tiled=True)
    got = exp_swap(rows)
    first = lax.axis_index("exp") == 0
    return jnp.where(
        first, jnp.concatenate([rows, got], axis=0), jnp.concatenate([got, rows], axis=0)
    )


def moe_whole_rows(normed, dispatch, combine, gate_matrix, up_matrix, down_matrix, n_ctx, capacity):
    all_normed = lax.all_gather(normed, "exp", axis=0, tiled=True)
    send_rows = jnp.dot(
        dispatch.astype(jnp.bfloat16), all_normed, preferred_element_type=jnp.float32
    ).astype(jnp.bfloat16)
    send_rows = send_rows.reshape(n_ctx, capacity, D)
    arrived = lax.all_to_all(send_rows, "ctx", split_axis=0, concat_axis=0, tiled=True)
    flat_rows = arrived.reshape(n_ctx * capacity, D)
    produced = expert_ffn(flat_rows, gate_matrix, up_matrix, down_matrix).reshape(
        n_ctx, capacity, D
    )
    served = lax.all_to_all(
        produced.astype(jnp.bfloat16), "ctx", split_axis=0, concat_axis=0, tiled=True
    )
    results = served.reshape(n_ctx * capacity, D).astype(jnp.float32)
    moe_part = jnp.dot(
        combine, results, precision=lax.Precision.HIGHEST, preferred_element_type=jnp.float32
    )
    return lax.psum_scatter(
        moe_part.astype(jnp.bfloat16), "exp", scatter_dimension=0, tiled=True
    ).astype(jnp.float32)


def halves(x, first, axis):
    size = x.shape[axis] // 2
    lower = lax.slice_in_dim(x, 0, size, axis=axis)
    upper = lax.slice_in_dim(x, size, 2 * size, axis=axis)
    return jnp.where(first, lower, upper), jnp.where(first, upper, lower)


def join(mine, theirs, first, axis):
    return jnp.where(
        first,
        jnp.concatenate([mine, theirs], axis=axis),
        jnp.concatenate([theirs, mine], axis=axis),
    )


def moe_column_halves(normed, dispatch, combine, gate_matrix, up_matrix, down_matrix, n_ctx, capacity):
    my_exp = lax.axis_index("exp")
    first = my_exp == 0
    half_d = normed.shape[1] // 2
    my_cols, other_cols = halves(normed, first, 1)
    tokens_cols = join(my_cols, exp_swap(other_cols), first, 0)
    send_rows = jnp.dot(
        dispatch.astype(jnp.bfloat16), tokens_cols, preferred_element_type=jnp.float32
    ).astype(jnp.bfloat16)
    send_rows = send_rows.reshape(n_ctx, capacity, half_d)
    my_start = my_exp * half_d
    other_start = (1 - my_exp) * half_d
    gate_mine = lax.dynamic_slice_in_dim(gate_matrix, my_start, half_d, axis=0)
    gate_other = lax.dynamic_slice_in_dim(gate_matrix, other_start, half_d, axis=0)
    up_mine = lax.dynamic_slice_in_dim(up_matrix, my_start, half_d, axis=0)
    up_other = lax.dynamic_slice_in_dim(up_matrix, other_start, half_d, axis=0)
    down_other = lax.dynamic_slice_in_dim(down_matrix, other_start, half_d, axis=1)
    down_mine = lax.dynamic_slice_in_dim(down_matrix, my_start, half_d, axis=1)
    n_chunks = 2 if capacity % 2 == 0 else 1
    chunk = capacity // n_chunks
    combine_slots = combine.reshape(combine.shape[0], n_ctx, capacity)
    moe_half = None
    for k in range(n_chunks):
        part = send_rows[:, k * chunk : (k + 1) * chunk]
        arrived = lax.all_to_all(part, "ctx", split_axis=0, concat_axis=0, tiled=True).reshape(
            n_ctx * chunk, half_d
        )
        partner_cols = exp_swap(arrived)
        gate_act = jnp.dot(arrived, gate_mine, preferred_element_type=jnp.float32) + jnp.dot(
            partner_cols, gate_other, preferred_element_type=jnp.float32
        )
        up_act = jnp.dot(arrived, up_mine, preferred_element_type=jnp.float32) + jnp.dot(
            partner_cols, up_other, preferred_element_type=jnp.float32
        )
        hidden = (jax.nn.silu(gate_act) * up_act).astype(jnp.bfloat16)
        out_other = jnp.dot(hidden, down_other, preferred_element_type=jnp.float32)
        got_other = exp_swap(out_other.astype(jnp.bfloat16))
        out_mine = jnp.dot(hidden, down_mine, preferred_element_type=jnp.float32)
        summed = (out_mine + got_other.astype(jnp.float32)).astype(jnp.bfloat16)
        served = lax.all_to_all(
            summed.reshape(n_ctx, chunk, half_d), "ctx", split_axis=0, concat_axis=0, tiled=True
        ).reshape(n_ctx * chunk, half_d)
        weights_k = combine_slots[:, :, k * chunk : (k + 1) * chunk].reshape(-1, n_ctx * chunk)
        term = jnp.dot(
            weights_k,
            served.astype(jnp.float32),
            precision=lax.Precision.HIGHEST,
            preferred_element_type=jnp.float32,
        )
        moe_half = term if moe_half is None else moe_half + term
    my_tok, other_tok = halves(moe_half, first, 0)
    got_tok = exp_swap(other_tok.astype(jnp.bfloat16)).astype(jnp.float32)
    return join(my_tok, got_tok, first, 1)


def local(
    query_states,
    key_states,
    value_states,
    residual,
    out_weight,
    norm_gain,
    gate_weight,
    up_weight,
    down_weight,
    routes,
    route_weights,
    prompt_lengths,
):
    n_ctx = lax.axis_size("ctx")
    my_ctx = lax.axis_index("ctx")
    tok_here = query_states.shape[1]
    feat_width = query_states.shape[2]
    heads_dev = feat_width // HD
    half_block = tok_here // 2
    score_scale = HD ** (-0.5)
    length = prompt_lengths[0]
    local_ids = jnp.arange(tok_here, dtype=jnp.int32)
    query_pos = row_positions(my_ctx * tok_here + local_ids, half_block, n_ctx)
    decode_pos = my_ctx * tok_here + local_ids
    query_three = query_states[0].reshape(tok_here, heads_dev, HD)
    run_max = jnp.full((heads_dev, tok_here), NEG, jnp.float32)
    key_two = lax.all_gather(key_states, "ctx", axis=1, tiled=True)[0]
    value_two = lax.all_gather(value_states, "ctx", axis=1, tiled=True)[0]
    row_count = key_two.shape[0]
    key_pos = row_positions(jnp.arange(row_count, dtype=jnp.int32), half_block, n_ctx)
    pick_rows = (decode_pos[:, None] == key_pos[None, :]).astype(jnp.bfloat16)
    kept_keys = jnp.dot(pick_rows, key_two, preferred_element_type=jnp.float32)
    kept_values = jnp.dot(pick_rows, value_two, preferred_element_type=jnp.float32)
    old_max = run_max
    key_heads = key_two.reshape(row_count, heads_dev, HD)
    value_heads = value_two.reshape(row_count, heads_dev, HD)
    logits = (
        jnp.einsum("qhd,khd->hqk", query_three, key_heads, preferred_element_type=jnp.float32)
        * score_scale
    )
    visible = (key_pos[None, :] <= query_pos[:, None]) & (key_pos[None, :] < length)
    logits = jnp.where(visible[None], logits, NEG)
    new_max = jnp.maximum(old_max, jnp.max(logits, axis=2))
    weights = jnp.where(visible[None], jnp.exp(logits - new_max[:, :, None]), 0.0)
    new_sum = jnp.sum(weights, axis=2)
    gained = jnp.einsum(
        "hqk,khd->hqd",
        weights.astype(jnp.bfloat16),
        value_heads,
        preferred_element_type=jnp.float32,
    )
    inner_state = (new_max, new_sum, gained)
    run_max, run_sum, run_out, kept_keys, kept_values = inner_state + (kept_keys, kept_values)
    mixed = (run_out / run_sum[:, :, None]).astype(jnp.bfloat16)
    mixed = jnp.transpose(mixed, (1, 0, 2)).reshape(tok_here, feat_width)
    out_parts = jnp.einsum(
        "tc,oc->to",
        mixed,
        lax.all_gather(out_weight, "ctx", axis=0, tiled=True),
        preferred_element_type=jnp.float32,
    )
    head_total = exp_reduce_rows(out_parts)
    stream = (residual[0].astype(jnp.float32) + head_total).astype(jnp.bfloat16)
    stream_f = stream.astype(jnp.float32)
    mean_sq = jnp.mean(stream_f * stream_f, axis=1, keepdims=True)
    normed = (stream_f * lax.rsqrt(mean_sq + EPS) * norm_gain).astype(jnp.bfloat16)
    capacity = min(tok_here, 2 * max(1, 3 * tok_here * TOP // (4 * n_ctx)))
    dispatch, combine = slot_tables(routes[0], route_weights[0], n_ctx, capacity)
    if lax.axis_size("exp") == 2:
        moe_rows = moe_column_halves(
            normed, dispatch, combine, gate_weight[0], up_weight[0], down_weight[0], n_ctx, capacity
        )
    else:
        moe_rows = moe_whole_rows(
            normed, dispatch, combine, gate_weight[0], up_weight[0], down_weight[0], n_ctx, capacity
        )
    layer_out = (stream.astype(jnp.float32) + moe_rows).astype(jnp.bfloat16)
    return (
        layer_out[None],
        kept_keys.astype(jnp.bfloat16)[None],
        kept_values.astype(jnp.bfloat16)[None],
    )


def solution(mesh):
    return jax.shard_map(
        local,
        mesh=mesh,
        in_specs=(
            P("req", "ctx", "exp"),
            P("req", "ctx", "exp"),
            P("req", "ctx", "exp"),
            P("req", ("ctx", "exp"), None),
            P("ctx", "exp"),
            P(),
            P("ctx", None, "exp"),
            P("ctx", None, "exp"),
            P("ctx", "exp", None),
            P("req", "ctx", None),
            P("req", "ctx", None),
            P("req"),
        ),
        out_specs=(P("req", ("ctx", "exp"), None), P("req", "ctx", "exp"), P("req", "ctx", "exp")),
        check_vma=False,
    )
```

```python
import jax
import jax.numpy as jnp
from jax import lax
from jax.sharding import PartitionSpec as P

D = 2048
HD = 128
TOP = 4


EPS = 1e-06
NEG = -1e30


def row_positions(row_ids, half_block, n_groups):
    block_ids = row_ids // half_block
    device = block_ids // 2
    target = jnp.where(block_ids % 2 == 0, device, 2 * n_groups - 1 - device)
    return target * half_block + row_ids % half_block


def slot_tables(route_block, weight_block, experts, capacity):
    tok_here, top_here = route_block.shape
    flat_ids = route_block.reshape(tok_here * top_here)
    hit_table = (flat_ids[:, None] == jnp.arange(experts, dtype=jnp.int32)[None, :]).astype(
        jnp.int32
    )
    before = jnp.cumsum(hit_table, axis=0) - hit_table
    slot_rank = jnp.sum(before * hit_table, axis=1)
    slot_index = flat_ids * capacity + slot_rank
    slot_match = (
        jnp.arange(experts * capacity, dtype=jnp.int32)[:, None] == slot_index[None, :]
    ).astype(jnp.float32)
    slot_match = slot_match.reshape(experts * capacity, tok_here, top_here)
    dispatch = jnp.sum(slot_match, axis=2)
    combine = jnp.transpose(jnp.sum(slot_match * weight_block[None, :, :], axis=2))
    return (dispatch, combine)


def expert_ffn(token_rows, gate_matrix, up_matrix, down_matrix):
    gate_act = jnp.dot(token_rows, gate_matrix, preferred_element_type=jnp.float32)
    up_act = jnp.dot(token_rows, up_matrix, preferred_element_type=jnp.float32)
    hidden = (jax.nn.silu(gate_act) * up_act).astype(jnp.bfloat16)
    return jnp.dot(hidden, down_matrix, preferred_element_type=jnp.float32)


def exp_swap(x):
    return lax.ppermute(x, "exp", perm=[(0, 1), (1, 0)])


def exp_reduce_rows(parts):
    if lax.axis_size("exp") != 2:
        return lax.psum_scatter(
            parts.astype(jnp.bfloat16), "exp", scatter_dimension=0, tiled=True
        ).astype(jnp.float32)
    half = parts.shape[0] // 2
    first = lax.axis_index("exp") == 0
    lower = parts[:half]
    upper = parts[half:]
    mine = jnp.where(first, lower, upper)
    theirs = jnp.where(first, upper, lower)
    got = exp_swap(theirs.astype(jnp.bfloat16))
    return mine + got.astype(jnp.float32)


def exp_gather_rows(rows):
    if lax.axis_size("exp") != 2:
        return lax.all_gather(rows, "exp", axis=0, tiled=True)
    got = exp_swap(rows)
    first = lax.axis_index("exp") == 0
    return jnp.where(
        first, jnp.concatenate([rows, got], axis=0), jnp.concatenate([got, rows], axis=0)
    )


def moe_whole_rows(normed, dispatch, combine, gate_matrix, up_matrix, down_matrix, n_ctx, capacity):
    all_normed = lax.all_gather(normed, "exp", axis=0, tiled=True)
    send_rows = jnp.dot(
        dispatch.astype(jnp.bfloat16), all_normed, preferred_element_type=jnp.float32
    ).astype(jnp.bfloat16)
    send_rows = send_rows.reshape(n_ctx, capacity, D)
    arrived = lax.all_to_all(send_rows, "ctx", split_axis=0, concat_axis=0, tiled=True)
    flat_rows = arrived.reshape(n_ctx * capacity, D)
    produced = expert_ffn(flat_rows, gate_matrix, up_matrix, down_matrix).reshape(
        n_ctx, capacity, D
    )
    served = lax.all_to_all(
        produced.astype(jnp.bfloat16), "ctx", split_axis=0, concat_axis=0, tiled=True
    )
    results = served.reshape(n_ctx * capacity, D).astype(jnp.float32)
    moe_part = jnp.dot(
        combine, results, precision=lax.Precision.HIGHEST, preferred_element_type=jnp.float32
    )
    return lax.psum_scatter(
        moe_part.astype(jnp.bfloat16), "exp", scatter_dimension=0, tiled=True
    ).astype(jnp.float32)


def halves(x, first, axis):
    size = x.shape[axis] // 2
    lower = lax.slice_in_dim(x, 0, size, axis=axis)
    upper = lax.slice_in_dim(x, size, 2 * size, axis=axis)
    return jnp.where(first, lower, upper), jnp.where(first, upper, lower)


def join(mine, theirs, first, axis):
    return jnp.where(
        first,
        jnp.concatenate([mine, theirs], axis=axis),
        jnp.concatenate([theirs, mine], axis=axis),
    )


def moe_column_halves(normed, dispatch, combine, gate_matrix, up_matrix, down_matrix, n_ctx, capacity):
    my_exp = lax.axis_index("exp")
    first = my_exp == 0
    half_d = normed.shape[1] // 2
    my_cols, other_cols = halves(normed, first, 1)
    tokens_cols = join(my_cols, exp_swap(other_cols), first, 0)
    send_rows = jnp.dot(
        dispatch.astype(jnp.bfloat16), tokens_cols, preferred_element_type=jnp.float32
    ).astype(jnp.bfloat16)
    send_rows = send_rows.reshape(n_ctx, capacity, half_d)
    my_start = my_exp * half_d
    other_start = (1 - my_exp) * half_d
    gate_mine = lax.dynamic_slice_in_dim(gate_matrix, my_start, half_d, axis=0)
    gate_other = lax.dynamic_slice_in_dim(gate_matrix, other_start, half_d, axis=0)
    up_mine = lax.dynamic_slice_in_dim(up_matrix, my_start, half_d, axis=0)
    up_other = lax.dynamic_slice_in_dim(up_matrix, other_start, half_d, axis=0)
    down_other = lax.dynamic_slice_in_dim(down_matrix, other_start, half_d, axis=1)
    down_mine = lax.dynamic_slice_in_dim(down_matrix, my_start, half_d, axis=1)
    n_chunks = 2 if capacity % 2 == 0 else 1
    chunk = capacity // n_chunks
    combine_slots = combine.reshape(combine.shape[0], n_ctx, capacity)
    moe_half = None
    for k in range(n_chunks):
        part = send_rows[:, k * chunk : (k + 1) * chunk]
        arrived = lax.all_to_all(part, "ctx", split_axis=0, concat_axis=0, tiled=True).reshape(
            n_ctx * chunk, half_d
        )
        partner_cols = exp_swap(arrived)
        gate_act = jnp.dot(arrived, gate_mine, preferred_element_type=jnp.float32) + jnp.dot(
            partner_cols, gate_other, preferred_element_type=jnp.float32
        )
        up_act = jnp.dot(arrived, up_mine, preferred_element_type=jnp.float32) + jnp.dot(
            partner_cols, up_other, preferred_element_type=jnp.float32
        )
        hidden = (jax.nn.silu(gate_act) * up_act).astype(jnp.bfloat16)
        out_other = jnp.dot(hidden, down_other, preferred_element_type=jnp.float32)
        got_other = exp_swap(out_other.astype(jnp.bfloat16))
        out_mine = jnp.dot(hidden, down_mine, preferred_element_type=jnp.float32)
        summed = (out_mine + got_other.astype(jnp.float32)).astype(jnp.bfloat16)
        served = lax.all_to_all(
            summed.reshape(n_ctx, chunk, half_d), "ctx", split_axis=0, concat_axis=0, tiled=True
        ).reshape(n_ctx * chunk, half_d)
        weights_k = combine_slots[:, :, k * chunk : (k + 1) * chunk].reshape(-1, n_ctx * chunk)
        term = jnp.dot(
            weights_k,
            served.astype(jnp.float32),
            precision=lax.Precision.HIGHEST,
            preferred_element_type=jnp.float32,
        )
        moe_half = term if moe_half is None else moe_half + term
    my_tok, other_tok = halves(moe_half, first, 0)
    got_tok = exp_swap(other_tok.astype(jnp.bfloat16)).astype(jnp.float32)
    return join(my_tok, got_tok, first, 1)


def ctx_gather_blocks(rows, n_ctx, my_ctx):
    n_chip = n_ctx // 2
    my_chip = my_ctx // 2
    my_core = my_ctx % 2
    stack = [rows]
    for shift in range(1, n_chip):
        perm = [(i, ((i // 2 + shift) % n_chip) * 2 + i % 2) for i in range(n_ctx)]
        stack.append(lax.ppermute(rows, "ctx", perm=perm))
    own = jnp.stack(stack)
    partner = lax.ppermute(own, "ctx", perm=[(i, i ^ 1) for i in range(n_ctx)])
    shifts = jnp.arange(n_chip, dtype=jnp.int32)
    chips = (my_chip - shifts) % n_chip
    src_ctx = jnp.concatenate([chips * 2 + my_core, chips * 2 + (1 - my_core)])
    return jnp.concatenate([own, partner]), src_ctx


def local(
    query_states,
    key_states,
    value_states,
    residual,
    out_weight,
    norm_gain,
    gate_weight,
    up_weight,
    down_weight,
    routes,
    route_weights,
    prompt_lengths,
):
    n_ctx = lax.axis_size("ctx")
    my_ctx = lax.axis_index("ctx")
    tok_here = query_states.shape[1]
    feat_width = query_states.shape[2]
    heads_dev = feat_width // HD
    half_block = tok_here // 2
    score_scale = HD ** (-0.5)
    length = prompt_lengths[0]
    local_ids = jnp.arange(tok_here, dtype=jnp.int32)
    query_pos = row_positions(my_ctx * tok_here + local_ids, half_block, n_ctx)
    decode_pos = my_ctx * tok_here + local_ids
    query_three = query_states[0].reshape(tok_here, heads_dev, HD)
    run_max = jnp.full((heads_dev, tok_here), NEG, jnp.float32)
    kv_here = jnp.concatenate([key_states[0], value_states[0]], axis=1)
    kv_blocks, src_ctx = ctx_gather_blocks(kv_here, n_ctx, my_ctx)
    kv_all = kv_blocks.reshape(n_ctx * tok_here, 2 * feat_width)
    key_two = kv_all[:, :feat_width]
    value_two = kv_all[:, feat_width:]
    row_count = key_two.shape[0]
    row_ids = (src_ctx[:, None] * tok_here + local_ids[None, :]).reshape(row_count)
    key_pos = row_positions(row_ids, half_block, n_ctx)
    pick_rows = (decode_pos[:, None] == key_pos[None, :]).astype(jnp.bfloat16)
    kept_keys = jnp.dot(pick_rows, key_two, preferred_element_type=jnp.float32)
    kept_values = jnp.dot(pick_rows, value_two, preferred_element_type=jnp.float32)
    old_max = run_max
    key_heads = key_two.reshape(row_count, heads_dev, HD)
    value_heads = value_two.reshape(row_count, heads_dev, HD)
    logits = (
        jnp.einsum("qhd,khd->hqk", query_three, key_heads, preferred_element_type=jnp.float32)
        * score_scale
    )
    visible = (key_pos[None, :] <= query_pos[:, None]) & (key_pos[None, :] < length)
    logits = jnp.where(visible[None], logits, NEG)
    new_max = jnp.maximum(old_max, jnp.max(logits, axis=2))
    weights = jnp.where(visible[None], jnp.exp(logits - new_max[:, :, None]), 0.0)
    new_sum = jnp.sum(weights, axis=2)
    gained = jnp.einsum(
        "hqk,khd->hqd",
        weights.astype(jnp.bfloat16),
        value_heads,
        preferred_element_type=jnp.float32,
    )
    inner_state = (new_max, new_sum, gained)
    run_max, run_sum, run_out, kept_keys, kept_values = inner_state + (kept_keys, kept_values)
    mixed = (run_out / run_sum[:, :, None]).astype(jnp.bfloat16)
    mixed = jnp.transpose(mixed, (1, 0, 2)).reshape(tok_here, feat_width)
    out_parts = jnp.einsum(
        "tc,oc->to",
        mixed,
        lax.all_gather(out_weight, "ctx", axis=0, tiled=True),
        preferred_element_type=jnp.float32,
    )
    head_total = exp_reduce_rows(out_parts)
    stream = (residual[0].astype(jnp.float32) + head_total).astype(jnp.bfloat16)
    stream_f = stream.astype(jnp.float32)
    mean_sq = jnp.mean(stream_f * stream_f, axis=1, keepdims=True)
    normed = (stream_f * lax.rsqrt(mean_sq + EPS) * norm_gain).astype(jnp.bfloat16)
    capacity = min(tok_here, 2 * max(1, 3 * tok_here * TOP // (4 * n_ctx)))
    dispatch, combine = slot_tables(routes[0], route_weights[0], n_ctx, capacity)
    if lax.axis_size("exp") == 2:
        moe_rows = moe_column_halves(
            normed, dispatch, combine, gate_weight[0], up_weight[0], down_weight[0], n_ctx, capacity
        )
    else:
        moe_rows = moe_whole_rows(
            normed, dispatch, combine, gate_weight[0], up_weight[0], down_weight[0], n_ctx, capacity
        )
    layer_out = (stream.astype(jnp.float32) + moe_rows).astype(jnp.bfloat16)
    return (
        layer_out[None],
        kept_keys.astype(jnp.bfloat16)[None],
        kept_values.astype(jnp.bfloat16)[None],
    )


def solution(mesh):
    return jax.shard_map(
        local,
        mesh=mesh,
        in_specs=(
            P("req", "ctx", "exp"),
            P("req", "ctx", "exp"),
            P("req", "ctx", "exp"),
            P("req", ("ctx", "exp"), None),
            P("ctx", "exp"),
            P(),
            P("ctx", None, "exp"),
            P("ctx", None, "exp"),
            P("ctx", "exp", None),
            P("req", "ctx", None),
            P("req", "ctx", None),
            P("req"),
        ),
        out_specs=(P("req", ("ctx", "exp"), None), P("req", "ctx", "exp"), P("req", "ctx", "exp")),
        check_vma=False,
    )
```

```python
import jax
import jax.numpy as jnp
from jax import lax
from jax.sharding import PartitionSpec as P

D = 2048
HD = 128
TOP = 4


EPS = 1e-06
NEG = -1e30


def row_positions(row_ids, half_block, n_groups):
    block_ids = row_ids // half_block
    device = block_ids // 2
    target = jnp.where(block_ids % 2 == 0, device, 2 * n_groups - 1 - device)
    return target * half_block + row_ids % half_block


def slot_tables(route_block, weight_block, experts, capacity):
    tok_here, top_here = route_block.shape
    flat_ids = route_block.reshape(tok_here * top_here)
    hit_table = (flat_ids[:, None] == jnp.arange(experts, dtype=jnp.int32)[None, :]).astype(
        jnp.int32
    )
    before = jnp.cumsum(hit_table, axis=0) - hit_table
    slot_rank = jnp.sum(before * hit_table, axis=1)
    slot_index = flat_ids * capacity + slot_rank
    slot_match = (
        jnp.arange(experts * capacity, dtype=jnp.int32)[:, None] == slot_index[None, :]
    ).astype(jnp.float32)
    slot_match = slot_match.reshape(experts * capacity, tok_here, top_here)
    dispatch = jnp.sum(slot_match, axis=2)
    combine = jnp.transpose(jnp.sum(slot_match * weight_block[None, :, :], axis=2))
    return (dispatch, combine)


def expert_ffn(token_rows, gate_matrix, up_matrix, down_matrix):
    gate_act = jnp.dot(token_rows, gate_matrix, preferred_element_type=jnp.float32)
    up_act = jnp.dot(token_rows, up_matrix, preferred_element_type=jnp.float32)
    hidden = (jax.nn.silu(gate_act) * up_act).astype(jnp.bfloat16)
    return jnp.dot(hidden, down_matrix, preferred_element_type=jnp.float32)


def exp_swap(x):
    return lax.ppermute(x, "exp", perm=[(0, 1), (1, 0)])


def exp_reduce_rows(parts):
    if lax.axis_size("exp") != 2:
        return lax.psum_scatter(
            parts.astype(jnp.bfloat16), "exp", scatter_dimension=0, tiled=True
        ).astype(jnp.float32)
    half = parts.shape[0] // 2
    first = lax.axis_index("exp") == 0
    lower = parts[:half]
    upper = parts[half:]
    mine = jnp.where(first, lower, upper)
    theirs = jnp.where(first, upper, lower)
    got = exp_swap(theirs.astype(jnp.bfloat16))
    return mine + got.astype(jnp.float32)


def exp_gather_rows(rows):
    if lax.axis_size("exp") != 2:
        return lax.all_gather(rows, "exp", axis=0, tiled=True)
    got = exp_swap(rows)
    first = lax.axis_index("exp") == 0
    return jnp.where(
        first, jnp.concatenate([rows, got], axis=0), jnp.concatenate([got, rows], axis=0)
    )


def moe_whole_rows(normed, dispatch, combine, gate_matrix, up_matrix, down_matrix, n_ctx, capacity):
    all_normed = lax.all_gather(normed, "exp", axis=0, tiled=True)
    send_rows = jnp.dot(
        dispatch.astype(jnp.bfloat16), all_normed, preferred_element_type=jnp.float32
    ).astype(jnp.bfloat16)
    send_rows = send_rows.reshape(n_ctx, capacity, D)
    arrived = lax.all_to_all(send_rows, "ctx", split_axis=0, concat_axis=0, tiled=True)
    flat_rows = arrived.reshape(n_ctx * capacity, D)
    produced = expert_ffn(flat_rows, gate_matrix, up_matrix, down_matrix).reshape(
        n_ctx, capacity, D
    )
    served = lax.all_to_all(
        produced.astype(jnp.bfloat16), "ctx", split_axis=0, concat_axis=0, tiled=True
    )
    results = served.reshape(n_ctx * capacity, D).astype(jnp.float32)
    moe_part = jnp.dot(
        combine, results, precision=lax.Precision.HIGHEST, preferred_element_type=jnp.float32
    )
    return lax.psum_scatter(
        moe_part.astype(jnp.bfloat16), "exp", scatter_dimension=0, tiled=True
    ).astype(jnp.float32)


def halves(x, first, axis):
    size = x.shape[axis] // 2
    lower = lax.slice_in_dim(x, 0, size, axis=axis)
    upper = lax.slice_in_dim(x, size, 2 * size, axis=axis)
    return jnp.where(first, lower, upper), jnp.where(first, upper, lower)


def join(mine, theirs, first, axis):
    return jnp.where(
        first,
        jnp.concatenate([mine, theirs], axis=axis),
        jnp.concatenate([theirs, mine], axis=axis),
    )


def moe_column_halves(normed, dispatch, combine, gate_matrix, up_matrix, down_matrix, n_ctx, capacity):
    my_exp = lax.axis_index("exp")
    first = my_exp == 0
    half_d = normed.shape[1] // 2
    my_cols, other_cols = halves(normed, first, 1)
    tokens_cols = join(my_cols, exp_swap(other_cols), first, 0)
    send_rows = jnp.dot(
        dispatch.astype(jnp.bfloat16), tokens_cols, preferred_element_type=jnp.float32
    ).astype(jnp.bfloat16)
    send_rows = send_rows.reshape(n_ctx, capacity, half_d)
    my_start = my_exp * half_d
    other_start = (1 - my_exp) * half_d
    gate_mine = lax.dynamic_slice_in_dim(gate_matrix, my_start, half_d, axis=0)
    gate_other = lax.dynamic_slice_in_dim(gate_matrix, other_start, half_d, axis=0)
    up_mine = lax.dynamic_slice_in_dim(up_matrix, my_start, half_d, axis=0)
    up_other = lax.dynamic_slice_in_dim(up_matrix, other_start, half_d, axis=0)
    down_other = lax.dynamic_slice_in_dim(down_matrix, other_start, half_d, axis=1)
    down_mine = lax.dynamic_slice_in_dim(down_matrix, my_start, half_d, axis=1)
    n_chunks = 2 if capacity % 2 == 0 else 1
    chunk = capacity // n_chunks
    combine_slots = combine.reshape(combine.shape[0], n_ctx, capacity)
    moe_half = None
    for k in range(n_chunks):
        part = send_rows[:, k * chunk : (k + 1) * chunk]
        arrived = lax.all_to_all(part, "ctx", split_axis=0, concat_axis=0, tiled=True).reshape(
            n_ctx * chunk, half_d
        )
        partner_cols = exp_swap(arrived)
        gate_act = jnp.dot(arrived, gate_mine, preferred_element_type=jnp.float32) + jnp.dot(
            partner_cols, gate_other, preferred_element_type=jnp.float32
        )
        up_act = jnp.dot(arrived, up_mine, preferred_element_type=jnp.float32) + jnp.dot(
            partner_cols, up_other, preferred_element_type=jnp.float32
        )
        hidden = (jax.nn.silu(gate_act) * up_act).astype(jnp.bfloat16)
        out_other = jnp.dot(hidden, down_other, preferred_element_type=jnp.float32)
        got_other = exp_swap(out_other.astype(jnp.bfloat16))
        out_mine = jnp.dot(hidden, down_mine, preferred_element_type=jnp.float32)
        summed = (out_mine + got_other.astype(jnp.float32)).astype(jnp.bfloat16)
        served = lax.all_to_all(
            summed.reshape(n_ctx, chunk, half_d), "ctx", split_axis=0, concat_axis=0, tiled=True
        ).reshape(n_ctx * chunk, half_d)
        weights_k = combine_slots[:, :, k * chunk : (k + 1) * chunk].reshape(-1, n_ctx * chunk)
        term = jnp.dot(
            weights_k,
            served.astype(jnp.float32),
            precision=lax.Precision.HIGHEST,
            preferred_element_type=jnp.float32,
        )
        moe_half = term if moe_half is None else moe_half + term
    my_tok, other_tok = halves(moe_half, first, 0)
    got_tok = exp_swap(other_tok.astype(jnp.bfloat16)).astype(jnp.float32)
    return join(my_tok, got_tok, first, 1)


def ctx_gather_blocks(rows, n_ctx, my_ctx):
    n_chip = n_ctx // 2
    my_chip = my_ctx // 2
    my_core = my_ctx % 2
    stack = [rows]
    for shift in range(1, n_chip):
        perm = [(i, ((i // 2 + shift) % n_chip) * 2 + i % 2) for i in range(n_ctx)]
        stack.append(lax.ppermute(rows, "ctx", perm=perm))
    own = jnp.stack(stack)
    partner = lax.ppermute(own, "ctx", perm=[(i, i ^ 1) for i in range(n_ctx)])
    shifts = jnp.arange(n_chip, dtype=jnp.int32)
    chips = (my_chip - shifts) % n_chip
    src_ctx = jnp.concatenate([chips * 2 + my_core, chips * 2 + (1 - my_core)])
    return jnp.concatenate([own, partner]), src_ctx


def gather_out_weight(weight_rows, n_ctx, my_ctx):
    rows_dev, width = weight_rows.shape
    split = rows_dev // 2
    if n_ctx % 2 or split % 8:
        return lax.all_gather(weight_rows, "ctx", axis=0, tiled=True)
    front = lax.all_gather(weight_rows[:split], "ctx", axis=0, tiled=False)
    back_blocks, src_ctx = ctx_gather_blocks(weight_rows[split:], n_ctx, my_ctx)
    n_chip = n_ctx // 2
    ctx_ids = jnp.arange(n_ctx, dtype=jnp.int32)
    block_of = (ctx_ids % 2 != my_ctx % 2) * n_chip + (my_ctx // 2 - ctx_ids // 2) % n_chip
    back = jnp.take(back_blocks, block_of, axis=0)
    return jnp.concatenate([front, back], axis=1).reshape(n_ctx * rows_dev, width)


def local(
    query_states,
    key_states,
    value_states,
    residual,
    out_weight,
    norm_gain,
    gate_weight,
    up_weight,
    down_weight,
    routes,
    route_weights,
    prompt_lengths,
):
    n_ctx = lax.axis_size("ctx")
    my_ctx = lax.axis_index("ctx")
    tok_here = query_states.shape[1]
    feat_width = query_states.shape[2]
    heads_dev = feat_width // HD
    half_block = tok_here // 2
    score_scale = HD ** (-0.5)
    length = prompt_lengths[0]
    local_ids = jnp.arange(tok_here, dtype=jnp.int32)
    query_pos = row_positions(my_ctx * tok_here + local_ids, half_block, n_ctx)
    decode_pos = my_ctx * tok_here + local_ids
    query_three = query_states[0].reshape(tok_here, heads_dev, HD)
    run_max = jnp.full((heads_dev, tok_here), NEG, jnp.float32)
    kv_here = jnp.concatenate([key_states[0], value_states[0]], axis=1)
    kv_blocks, src_ctx = ctx_gather_blocks(kv_here, n_ctx, my_ctx)
    kv_all = kv_blocks.reshape(n_ctx * tok_here, 2 * feat_width)
    key_two = kv_all[:, :feat_width]
    value_two = kv_all[:, feat_width:]
    row_count = key_two.shape[0]
    row_ids = (src_ctx[:, None] * tok_here + local_ids[None, :]).reshape(row_count)
    key_pos = row_positions(row_ids, half_block, n_ctx)
    pick_rows = (decode_pos[:, None] == key_pos[None, :]).astype(jnp.bfloat16)
    kept_keys = jnp.dot(pick_rows, key_two, preferred_element_type=jnp.float32)
    kept_values = jnp.dot(pick_rows, value_two, preferred_element_type=jnp.float32)
    old_max = run_max
    key_heads = key_two.reshape(row_count, heads_dev, HD)
    value_heads = value_two.reshape(row_count, heads_dev, HD)
    logits = (
        jnp.einsum("qhd,khd->hqk", query_three, key_heads, preferred_element_type=jnp.float32)
        * score_scale
    )
    visible = (key_pos[None, :] <= query_pos[:, None]) & (key_pos[None, :] < length)
    logits = jnp.where(visible[None], logits, NEG)
    new_max = jnp.maximum(old_max, jnp.max(logits, axis=2))
    weights = jnp.where(visible[None], jnp.exp(logits - new_max[:, :, None]), 0.0)
    new_sum = jnp.sum(weights, axis=2)
    gained = jnp.einsum(
        "hqk,khd->hqd",
        weights.astype(jnp.bfloat16),
        value_heads,
        preferred_element_type=jnp.float32,
    )
    inner_state = (new_max, new_sum, gained)
    run_max, run_sum, run_out, kept_keys, kept_values = inner_state + (kept_keys, kept_values)
    mixed = (run_out / run_sum[:, :, None]).astype(jnp.bfloat16)
    mixed = jnp.transpose(mixed, (1, 0, 2)).reshape(tok_here, feat_width)
    out_parts = jnp.einsum(
        "tc,oc->to",
        mixed,
        gather_out_weight(out_weight, n_ctx, my_ctx),
        preferred_element_type=jnp.float32,
    )
    head_total = exp_reduce_rows(out_parts)
    stream = (residual[0].astype(jnp.float32) + head_total).astype(jnp.bfloat16)
    stream_f = stream.astype(jnp.float32)
    mean_sq = jnp.mean(stream_f * stream_f, axis=1, keepdims=True)
    normed = (stream_f * lax.rsqrt(mean_sq + EPS) * norm_gain).astype(jnp.bfloat16)
    capacity = min(tok_here, 2 * max(1, 3 * tok_here * TOP // (4 * n_ctx)))
    dispatch, combine = slot_tables(routes[0], route_weights[0], n_ctx, capacity)
    if lax.axis_size("exp") == 2:
        moe_rows = moe_column_halves(
            normed, dispatch, combine, gate_weight[0], up_weight[0], down_weight[0], n_ctx, capacity
        )
    else:
        moe_rows = moe_whole_rows(
            normed, dispatch, combine, gate_weight[0], up_weight[0], down_weight[0], n_ctx, capacity
        )
    layer_out = (stream.astype(jnp.float32) + moe_rows).astype(jnp.bfloat16)
    return (
        layer_out[None],
        kept_keys.astype(jnp.bfloat16)[None],
        kept_values.astype(jnp.bfloat16)[None],
    )


def solution(mesh):
    return jax.shard_map(
        local,
        mesh=mesh,
        in_specs=(
            P("req", "ctx", "exp"),
            P("req", "ctx", "exp"),
            P("req", "ctx", "exp"),
            P("req", ("ctx", "exp"), None),
            P("ctx", "exp"),
            P(),
            P("ctx", None, "exp"),
            P("ctx", None, "exp"),
            P("ctx", "exp", None),
            P("req", "ctx", None),
            P("req", "ctx", None),
            P("req"),
        ),
        out_specs=(P("req", ("ctx", "exp"), None), P("req", "ctx", "exp"), P("req", "ctx", "exp")),
        check_vma=False,
    )
```

```python
import jax
import jax.numpy as jnp
from jax import lax
from jax.sharding import PartitionSpec as P

D = 2048
HD = 128
TOP = 4


EPS = 1e-06
NEG = -1e30


def row_positions(row_ids, half_block, n_groups):
    block_ids = row_ids // half_block
    device = block_ids // 2
    target = jnp.where(block_ids % 2 == 0, device, 2 * n_groups - 1 - device)
    return target * half_block + row_ids % half_block


def slot_tables(route_block, weight_block, experts, capacity):
    tok_here, top_here = route_block.shape
    flat_ids = route_block.reshape(tok_here * top_here)
    hit_table = (flat_ids[:, None] == jnp.arange(experts, dtype=jnp.int32)[None, :]).astype(
        jnp.int32
    )
    before = jnp.cumsum(hit_table, axis=0) - hit_table
    slot_rank = jnp.sum(before * hit_table, axis=1)
    slot_index = flat_ids * capacity + slot_rank
    slot_match = (
        jnp.arange(experts * capacity, dtype=jnp.int32)[:, None] == slot_index[None, :]
    ).astype(jnp.float32)
    slot_match = slot_match.reshape(experts * capacity, tok_here, top_here)
    dispatch = jnp.sum(slot_match, axis=2)
    combine = jnp.transpose(jnp.sum(slot_match * weight_block[None, :, :], axis=2))
    return (dispatch, combine)


def expert_ffn(token_rows, gate_matrix, up_matrix, down_matrix):
    gate_act = jnp.dot(token_rows, gate_matrix, preferred_element_type=jnp.float32)
    up_act = jnp.dot(token_rows, up_matrix, preferred_element_type=jnp.float32)
    hidden = (jax.nn.silu(gate_act) * up_act).astype(jnp.bfloat16)
    return jnp.dot(hidden, down_matrix, preferred_element_type=jnp.float32)


def exp_swap(x):
    return lax.ppermute(x, "exp", perm=[(0, 1), (1, 0)])


def exp_reduce_rows(parts):
    if lax.axis_size("exp") != 2:
        return lax.psum_scatter(
            parts.astype(jnp.bfloat16), "exp", scatter_dimension=0, tiled=True
        ).astype(jnp.float32)
    half = parts.shape[0] // 2
    first = lax.axis_index("exp") == 0
    lower = parts[:half]
    upper = parts[half:]
    mine = jnp.where(first, lower, upper)
    theirs = jnp.where(first, upper, lower)
    got = exp_swap(theirs.astype(jnp.bfloat16))
    return mine + got.astype(jnp.float32)


def exp_gather_rows(rows):
    if lax.axis_size("exp") != 2:
        return lax.all_gather(rows, "exp", axis=0, tiled=True)
    got = exp_swap(rows)
    first = lax.axis_index("exp") == 0
    return jnp.where(
        first, jnp.concatenate([rows, got], axis=0), jnp.concatenate([got, rows], axis=0)
    )


def moe_whole_rows(normed, dispatch, combine, gate_matrix, up_matrix, down_matrix, n_ctx, capacity):
    all_normed = lax.all_gather(normed, "exp", axis=0, tiled=True)
    send_rows = jnp.dot(
        dispatch.astype(jnp.bfloat16), all_normed, preferred_element_type=jnp.float32
    ).astype(jnp.bfloat16)
    send_rows = send_rows.reshape(n_ctx, capacity, D)
    arrived = lax.all_to_all(send_rows, "ctx", split_axis=0, concat_axis=0, tiled=True)
    flat_rows = arrived.reshape(n_ctx * capacity, D)
    produced = expert_ffn(flat_rows, gate_matrix, up_matrix, down_matrix).reshape(
        n_ctx, capacity, D
    )
    served = lax.all_to_all(
        produced.astype(jnp.bfloat16), "ctx", split_axis=0, concat_axis=0, tiled=True
    )
    results = served.reshape(n_ctx * capacity, D).astype(jnp.float32)
    moe_part = jnp.dot(
        combine, results, precision=lax.Precision.HIGHEST, preferred_element_type=jnp.float32
    )
    return lax.psum_scatter(
        moe_part.astype(jnp.bfloat16), "exp", scatter_dimension=0, tiled=True
    ).astype(jnp.float32)


def halves(x, first, axis):
    size = x.shape[axis] // 2
    lower = lax.slice_in_dim(x, 0, size, axis=axis)
    upper = lax.slice_in_dim(x, size, 2 * size, axis=axis)
    return jnp.where(first, lower, upper), jnp.where(first, upper, lower)


def join(mine, theirs, first, axis):
    return jnp.where(
        first,
        jnp.concatenate([mine, theirs], axis=axis),
        jnp.concatenate([theirs, mine], axis=axis),
    )


def moe_column_halves(normed, dispatch, combine, gate_matrix, up_matrix, down_matrix, n_ctx, capacity):
    my_exp = lax.axis_index("exp")
    first = my_exp == 0
    half_d = normed.shape[1] // 2
    my_cols, other_cols = halves(normed, first, 1)
    tokens_cols = join(my_cols, exp_swap(other_cols), first, 0)
    tok_count = tokens_cols.shape[0]
    my_ctx = lax.axis_index("ctx")
    dispatch_rot = jnp.roll(dispatch.reshape(n_ctx, capacity, tok_count), -my_ctx, axis=0)
    send_rows = jnp.dot(
        dispatch_rot.reshape(n_ctx * capacity, tok_count).astype(jnp.bfloat16),
        tokens_cols,
        preferred_element_type=jnp.float32,
    ).astype(jnp.bfloat16)
    send_rows = send_rows.reshape(n_ctx, capacity, half_d)
    arrived = [send_rows[0]]
    for shift in range(1, n_ctx):
        perm = [(i, (i + shift) % n_ctx) for i in range(n_ctx)]
        arrived.append(lax.ppermute(send_rows[shift], "ctx", perm=perm))
    my_start = my_exp * half_d
    other_start = (1 - my_exp) * half_d
    gate_mine = lax.dynamic_slice_in_dim(gate_matrix, my_start, half_d, axis=0)
    gate_other = lax.dynamic_slice_in_dim(gate_matrix, other_start, half_d, axis=0)
    up_mine = lax.dynamic_slice_in_dim(up_matrix, my_start, half_d, axis=0)
    up_other = lax.dynamic_slice_in_dim(up_matrix, other_start, half_d, axis=0)
    down_other = lax.dynamic_slice_in_dim(down_matrix, other_start, half_d, axis=1)
    down_mine = lax.dynamic_slice_in_dim(down_matrix, my_start, half_d, axis=1)
    n_groups = 2 if n_ctx % 2 == 0 else 1
    per_group = n_ctx // n_groups
    returned = [None] * n_ctx
    for group in range(n_groups):
        shifts = range(group * per_group, (group + 1) * per_group)
        block = jnp.concatenate([arrived[k] for k in shifts], axis=0)
        partner_cols = exp_swap(block)
        gate_act = jnp.dot(block, gate_mine, preferred_element_type=jnp.float32) + jnp.dot(
            partner_cols, gate_other, preferred_element_type=jnp.float32
        )
        up_act = jnp.dot(block, up_mine, preferred_element_type=jnp.float32) + jnp.dot(
            partner_cols, up_other, preferred_element_type=jnp.float32
        )
        hidden = (jax.nn.silu(gate_act) * up_act).astype(jnp.bfloat16)
        out_other = jnp.dot(hidden, down_other, preferred_element_type=jnp.float32)
        got_other = exp_swap(out_other.astype(jnp.bfloat16))
        out_mine = jnp.dot(hidden, down_mine, preferred_element_type=jnp.float32)
        summed = (out_mine + got_other.astype(jnp.float32)).astype(jnp.bfloat16)
        summed = summed.reshape(per_group, capacity, half_d)
        for idx, shift in enumerate(shifts):
            if shift == 0:
                returned[shift] = summed[idx]
            else:
                perm = [(i, (i - shift) % n_ctx) for i in range(n_ctx)]
                returned[shift] = lax.ppermute(summed[idx], "ctx", perm=perm)
    served = jnp.stack(returned).reshape(n_ctx * capacity, half_d)
    combine_rot = jnp.roll(combine.reshape(tok_count, n_ctx, capacity), -my_ctx, axis=1)
    moe_half = jnp.dot(
        combine_rot.reshape(tok_count, n_ctx * capacity),
        served.astype(jnp.float32),
        precision=lax.Precision.HIGHEST,
        preferred_element_type=jnp.float32,
    )
    my_tok, other_tok = halves(moe_half, first, 0)
    got_tok = exp_swap(other_tok.astype(jnp.bfloat16)).astype(jnp.float32)
    return join(my_tok, got_tok, first, 1)


def ctx_gather_blocks(rows, n_ctx, my_ctx):
    n_chip = n_ctx // 2
    my_chip = my_ctx // 2
    my_core = my_ctx % 2
    stack = [rows]
    for shift in range(1, n_chip):
        perm = [(i, ((i // 2 + shift) % n_chip) * 2 + i % 2) for i in range(n_ctx)]
        stack.append(lax.ppermute(rows, "ctx", perm=perm))
    own = jnp.stack(stack)
    partner = lax.ppermute(own, "ctx", perm=[(i, i ^ 1) for i in range(n_ctx)])
    shifts = jnp.arange(n_chip, dtype=jnp.int32)
    chips = (my_chip - shifts) % n_chip
    src_ctx = jnp.concatenate([chips * 2 + my_core, chips * 2 + (1 - my_core)])
    return jnp.concatenate([own, partner]), src_ctx


def local(
    query_states,
    key_states,
    value_states,
    residual,
    out_weight,
    norm_gain,
    gate_weight,
    up_weight,
    down_weight,
    routes,
    route_weights,
    prompt_lengths,
):
    n_ctx = lax.axis_size("ctx")
    my_ctx = lax.axis_index("ctx")
    tok_here = query_states.shape[1]
    feat_width = query_states.shape[2]
    heads_dev = feat_width // HD
    half_block = tok_here // 2
    score_scale = HD ** (-0.5)
    length = prompt_lengths[0]
    local_ids = jnp.arange(tok_here, dtype=jnp.int32)
    query_pos = row_positions(my_ctx * tok_here + local_ids, half_block, n_ctx)
    decode_pos = my_ctx * tok_here + local_ids
    query_three = query_states[0].reshape(tok_here, heads_dev, HD)
    run_max = jnp.full((heads_dev, tok_here), NEG, jnp.float32)
    kv_here = jnp.concatenate([key_states[0], value_states[0]], axis=1)
    kv_blocks, src_ctx = ctx_gather_blocks(kv_here, n_ctx, my_ctx)
    kv_all = kv_blocks.reshape(n_ctx * tok_here, 2 * feat_width)
    key_two = kv_all[:, :feat_width]
    value_two = kv_all[:, feat_width:]
    row_count = key_two.shape[0]
    row_ids = (src_ctx[:, None] * tok_here + local_ids[None, :]).reshape(row_count)
    key_pos = row_positions(row_ids, half_block, n_ctx)
    pick_rows = (decode_pos[:, None] == key_pos[None, :]).astype(jnp.bfloat16)
    kept_keys = jnp.dot(pick_rows, key_two, preferred_element_type=jnp.float32)
    kept_values = jnp.dot(pick_rows, value_two, preferred_element_type=jnp.float32)
    old_max = run_max
    key_heads = key_two.reshape(row_count, heads_dev, HD)
    value_heads = value_two.reshape(row_count, heads_dev, HD)
    logits = (
        jnp.einsum("qhd,khd->hqk", query_three, key_heads, preferred_element_type=jnp.float32)
        * score_scale
    )
    visible = (key_pos[None, :] <= query_pos[:, None]) & (key_pos[None, :] < length)
    logits = jnp.where(visible[None], logits, NEG)
    new_max = jnp.maximum(old_max, jnp.max(logits, axis=2))
    weights = jnp.where(visible[None], jnp.exp(logits - new_max[:, :, None]), 0.0)
    new_sum = jnp.sum(weights, axis=2)
    gained = jnp.einsum(
        "hqk,khd->hqd",
        weights.astype(jnp.bfloat16),
        value_heads,
        preferred_element_type=jnp.float32,
    )
    inner_state = (new_max, new_sum, gained)
    run_max, run_sum, run_out, kept_keys, kept_values = inner_state + (kept_keys, kept_values)
    mixed = (run_out / run_sum[:, :, None]).astype(jnp.bfloat16)
    mixed = jnp.transpose(mixed, (1, 0, 2)).reshape(tok_here, feat_width)
    out_parts = jnp.einsum(
        "tc,oc->to",
        mixed,
        lax.all_gather(out_weight, "ctx", axis=0, tiled=True),
        preferred_element_type=jnp.float32,
    )
    head_total = exp_reduce_rows(out_parts)
    stream = (residual[0].astype(jnp.float32) + head_total).astype(jnp.bfloat16)
    stream_f = stream.astype(jnp.float32)
    mean_sq = jnp.mean(stream_f * stream_f, axis=1, keepdims=True)
    normed = (stream_f * lax.rsqrt(mean_sq + EPS) * norm_gain).astype(jnp.bfloat16)
    capacity = min(tok_here, 2 * max(1, 3 * tok_here * TOP // (4 * n_ctx)))
    dispatch, combine = slot_tables(routes[0], route_weights[0], n_ctx, capacity)
    if lax.axis_size("exp") == 2:
        moe_rows = moe_column_halves(
            normed, dispatch, combine, gate_weight[0], up_weight[0], down_weight[0], n_ctx, capacity
        )
    else:
        moe_rows = moe_whole_rows(
            normed, dispatch, combine, gate_weight[0], up_weight[0], down_weight[0], n_ctx, capacity
        )
    layer_out = (stream.astype(jnp.float32) + moe_rows).astype(jnp.bfloat16)
    return (
        layer_out[None],
        kept_keys.astype(jnp.bfloat16)[None],
        kept_values.astype(jnp.bfloat16)[None],
    )


def solution(mesh):
    return jax.shard_map(
        local,
        mesh=mesh,
        in_specs=(
            P("req", "ctx", "exp"),
            P("req", "ctx", "exp"),
            P("req", "ctx", "exp"),
            P("req", ("ctx", "exp"), None),
            P("ctx", "exp"),
            P(),
            P("ctx", None, "exp"),
            P("ctx", None, "exp"),
            P("ctx", "exp", None),
            P("req", "ctx", None),
            P("req", "ctx", None),
            P("req"),
        ),
        out_specs=(P("req", ("ctx", "exp"), None), P("req", "ctx", "exp"), P("req", "ctx", "exp")),
        check_vma=False,
    )
```

```python
import jax
import jax.numpy as jnp
from jax import lax
from jax.sharding import PartitionSpec as P

D = 2048
HD = 128
TOP = 4


EPS = 1e-06
NEG = -1e30


def row_positions(row_ids, half_block, n_groups):
    block_ids = row_ids // half_block
    device = block_ids // 2
    target = jnp.where(block_ids % 2 == 0, device, 2 * n_groups - 1 - device)
    return target * half_block + row_ids % half_block


def slot_tables(route_block, weight_block, experts, capacity):
    tok_here, top_here = route_block.shape
    flat_ids = route_block.reshape(tok_here * top_here)
    hit_table = (flat_ids[:, None] == jnp.arange(experts, dtype=jnp.int32)[None, :]).astype(
        jnp.int32
    )
    before = jnp.cumsum(hit_table, axis=0) - hit_table
    slot_rank = jnp.sum(before * hit_table, axis=1)
    slot_index = flat_ids * capacity + slot_rank
    slot_match = (
        jnp.arange(experts * capacity, dtype=jnp.int32)[:, None] == slot_index[None, :]
    ).astype(jnp.float32)
    slot_match = slot_match.reshape(experts * capacity, tok_here, top_here)
    dispatch = jnp.sum(slot_match, axis=2)
    combine = jnp.transpose(jnp.sum(slot_match * weight_block[None, :, :], axis=2))
    return (dispatch, combine)


def expert_ffn(token_rows, gate_matrix, up_matrix, down_matrix):
    gate_act = jnp.dot(token_rows, gate_matrix, preferred_element_type=jnp.float32)
    up_act = jnp.dot(token_rows, up_matrix, preferred_element_type=jnp.float32)
    hidden = (jax.nn.silu(gate_act) * up_act).astype(jnp.bfloat16)
    return jnp.dot(hidden, down_matrix, preferred_element_type=jnp.float32)


def exp_swap(x):
    return lax.ppermute(x, "exp", perm=[(0, 1), (1, 0)])


def exp_reduce_rows(parts):
    if lax.axis_size("exp") != 2:
        return lax.psum_scatter(
            parts.astype(jnp.bfloat16), "exp", scatter_dimension=0, tiled=True
        ).astype(jnp.float32)
    half = parts.shape[0] // 2
    first = lax.axis_index("exp") == 0
    lower = parts[:half]
    upper = parts[half:]
    mine = jnp.where(first, lower, upper)
    theirs = jnp.where(first, upper, lower)
    got = exp_swap(theirs.astype(jnp.bfloat16))
    return mine + got.astype(jnp.float32)


def exp_gather_rows(rows):
    if lax.axis_size("exp") != 2:
        return lax.all_gather(rows, "exp", axis=0, tiled=True)
    got = exp_swap(rows)
    first = lax.axis_index("exp") == 0
    return jnp.where(
        first, jnp.concatenate([rows, got], axis=0), jnp.concatenate([got, rows], axis=0)
    )


def moe_whole_rows(normed, dispatch, combine, gate_matrix, up_matrix, down_matrix, n_ctx, capacity):
    all_normed = lax.all_gather(normed, "exp", axis=0, tiled=True)
    send_rows = jnp.dot(
        dispatch.astype(jnp.bfloat16), all_normed, preferred_element_type=jnp.float32
    ).astype(jnp.bfloat16)
    send_rows = send_rows.reshape(n_ctx, capacity, D)
    arrived = lax.all_to_all(send_rows, "ctx", split_axis=0, concat_axis=0, tiled=True)
    flat_rows = arrived.reshape(n_ctx * capacity, D)
    produced = expert_ffn(flat_rows, gate_matrix, up_matrix, down_matrix).reshape(
        n_ctx, capacity, D
    )
    served = lax.all_to_all(
        produced.astype(jnp.bfloat16), "ctx", split_axis=0, concat_axis=0, tiled=True
    )
    results = served.reshape(n_ctx * capacity, D).astype(jnp.float32)
    moe_part = jnp.dot(
        combine, results, precision=lax.Precision.HIGHEST, preferred_element_type=jnp.float32
    )
    return lax.psum_scatter(
        moe_part.astype(jnp.bfloat16), "exp", scatter_dimension=0, tiled=True
    ).astype(jnp.float32)


def halves(x, first, axis):
    size = x.shape[axis] // 2
    lower = lax.slice_in_dim(x, 0, size, axis=axis)
    upper = lax.slice_in_dim(x, size, 2 * size, axis=axis)
    return jnp.where(first, lower, upper), jnp.where(first, upper, lower)


def join(mine, theirs, first, axis):
    return jnp.where(
        first,
        jnp.concatenate([mine, theirs], axis=axis),
        jnp.concatenate([theirs, mine], axis=axis),
    )


def moe_column_halves(normed, dispatch, combine, gate_matrix, up_matrix, down_matrix, n_ctx, capacity):
    my_exp = lax.axis_index("exp")
    first = my_exp == 0
    half_d = normed.shape[1] // 2
    my_cols, other_cols = halves(normed, first, 1)
    tokens_cols = join(my_cols, exp_swap(other_cols), first, 0)
    tok_count = tokens_cols.shape[0]
    my_ctx = lax.axis_index("ctx")
    n_chip = n_ctx // 2
    my_chip = my_ctx // 2
    my_core = my_ctx % 2
    chips = (my_chip + jnp.arange(n_chip, dtype=jnp.int32)) % n_chip
    expert_ids = jnp.concatenate([chips * 2 + my_core, chips * 2 + (1 - my_core)])
    dispatch_ord = jnp.take(dispatch.reshape(n_ctx, capacity, tok_count), expert_ids, axis=0)
    send_rows = jnp.dot(
        dispatch_ord.reshape(n_ctx * capacity, tok_count).astype(jnp.bfloat16),
        tokens_cols,
        preferred_element_type=jnp.float32,
    ).astype(jnp.bfloat16)
    send_rows = send_rows.reshape(2, n_chip, capacity, half_d)
    core_swap = [(i, i ^ 1) for i in range(n_ctx)]
    from_partner = lax.ppermute(send_rows[1], "ctx", perm=core_swap)
    pairs = jnp.stack([send_rows[0], from_partner], axis=1)
    arrived = [pairs[0]]
    for shift in range(1, n_chip):
        perm = [(i, ((i // 2 + shift) % n_chip) * 2 + i % 2) for i in range(n_ctx)]
        arrived.append(lax.ppermute(pairs[shift], "ctx", perm=perm))
    my_start = my_exp * half_d
    other_start = (1 - my_exp) * half_d
    gate_mine = lax.dynamic_slice_in_dim(gate_matrix, my_start, half_d, axis=0)
    gate_other = lax.dynamic_slice_in_dim(gate_matrix, other_start, half_d, axis=0)
    up_mine = lax.dynamic_slice_in_dim(up_matrix, my_start, half_d, axis=0)
    up_other = lax.dynamic_slice_in_dim(up_matrix, other_start, half_d, axis=0)
    down_other = lax.dynamic_slice_in_dim(down_matrix, other_start, half_d, axis=1)
    down_mine = lax.dynamic_slice_in_dim(down_matrix, my_start, half_d, axis=1)
    n_groups = 2 if n_chip % 2 == 0 else 1
    per_group = n_chip // n_groups
    returned = [None] * n_chip
    for group in range(n_groups):
        shifts = range(group * per_group, (group + 1) * per_group)
        block = jnp.concatenate([arrived[k] for k in shifts], axis=0).reshape(-1, half_d)
        partner_cols = exp_swap(block)
        gate_act = jnp.dot(block, gate_mine, preferred_element_type=jnp.float32) + jnp.dot(
            partner_cols, gate_other, preferred_element_type=jnp.float32
        )
        up_act = jnp.dot(block, up_mine, preferred_element_type=jnp.float32) + jnp.dot(
            partner_cols, up_other, preferred_element_type=jnp.float32
        )
        hidden = (jax.nn.silu(gate_act) * up_act).astype(jnp.bfloat16)
        out_other = jnp.dot(hidden, down_other, preferred_element_type=jnp.float32)
        got_other = exp_swap(out_other.astype(jnp.bfloat16))
        out_mine = jnp.dot(hidden, down_mine, preferred_element_type=jnp.float32)
        summed = (out_mine + got_other.astype(jnp.float32)).astype(jnp.bfloat16)
        summed = summed.reshape(per_group, 2, capacity, half_d)
        for idx, shift in enumerate(shifts):
            if shift == 0:
                returned[shift] = summed[idx]
            else:
                perm = [(i, ((i // 2 - shift) % n_chip) * 2 + i % 2) for i in range(n_ctx)]
                returned[shift] = lax.ppermute(summed[idx], "ctx", perm=perm)
    back = jnp.stack(returned)
    partner_res = lax.ppermute(back[:, 1], "ctx", perm=core_swap)
    served = jnp.stack([back[:, 0], partner_res]).reshape(n_ctx * capacity, half_d)
    combine_ord = jnp.take(combine.reshape(tok_count, n_ctx, capacity), expert_ids, axis=1)
    moe_half = jnp.dot(
        combine_ord.reshape(tok_count, n_ctx * capacity),
        served.astype(jnp.float32),
        precision=lax.Precision.HIGHEST,
        preferred_element_type=jnp.float32,
    )
    my_tok, other_tok = halves(moe_half, first, 0)
    got_tok = exp_swap(other_tok.astype(jnp.bfloat16)).astype(jnp.float32)
    return join(my_tok, got_tok, first, 1)


def ctx_gather_blocks(rows, n_ctx, my_ctx):
    n_chip = n_ctx // 2
    my_chip = my_ctx // 2
    my_core = my_ctx % 2
    stack = [rows]
    for shift in range(1, n_chip):
        perm = [(i, ((i // 2 + shift) % n_chip) * 2 + i % 2) for i in range(n_ctx)]
        stack.append(lax.ppermute(rows, "ctx", perm=perm))
    own = jnp.stack(stack)
    partner = lax.ppermute(own, "ctx", perm=[(i, i ^ 1) for i in range(n_ctx)])
    shifts = jnp.arange(n_chip, dtype=jnp.int32)
    chips = (my_chip - shifts) % n_chip
    src_ctx = jnp.concatenate([chips * 2 + my_core, chips * 2 + (1 - my_core)])
    return jnp.concatenate([own, partner]), src_ctx


def local(
    query_states,
    key_states,
    value_states,
    residual,
    out_weight,
    norm_gain,
    gate_weight,
    up_weight,
    down_weight,
    routes,
    route_weights,
    prompt_lengths,
):
    n_ctx = lax.axis_size("ctx")
    my_ctx = lax.axis_index("ctx")
    tok_here = query_states.shape[1]
    feat_width = query_states.shape[2]
    heads_dev = feat_width // HD
    half_block = tok_here // 2
    score_scale = HD ** (-0.5)
    length = prompt_lengths[0]
    local_ids = jnp.arange(tok_here, dtype=jnp.int32)
    query_pos = row_positions(my_ctx * tok_here + local_ids, half_block, n_ctx)
    decode_pos = my_ctx * tok_here + local_ids
    query_three = query_states[0].reshape(tok_here, heads_dev, HD)
    run_max = jnp.full((heads_dev, tok_here), NEG, jnp.float32)
    kv_here = jnp.concatenate([key_states[0], value_states[0]], axis=1)
    kv_blocks, src_ctx = ctx_gather_blocks(kv_here, n_ctx, my_ctx)
    kv_all = kv_blocks.reshape(n_ctx * tok_here, 2 * feat_width)
    key_two = kv_all[:, :feat_width]
    value_two = kv_all[:, feat_width:]
    row_count = key_two.shape[0]
    row_ids = (src_ctx[:, None] * tok_here + local_ids[None, :]).reshape(row_count)
    key_pos = row_positions(row_ids, half_block, n_ctx)
    pick_rows = (decode_pos[:, None] == key_pos[None, :]).astype(jnp.bfloat16)
    kept_keys = jnp.dot(pick_rows, key_two, preferred_element_type=jnp.float32)
    kept_values = jnp.dot(pick_rows, value_two, preferred_element_type=jnp.float32)
    old_max = run_max
    key_heads = key_two.reshape(row_count, heads_dev, HD)
    value_heads = value_two.reshape(row_count, heads_dev, HD)
    logits = (
        jnp.einsum("qhd,khd->hqk", query_three, key_heads, preferred_element_type=jnp.float32)
        * score_scale
    )
    visible = (key_pos[None, :] <= query_pos[:, None]) & (key_pos[None, :] < length)
    logits = jnp.where(visible[None], logits, NEG)
    new_max = jnp.maximum(old_max, jnp.max(logits, axis=2))
    weights = jnp.where(visible[None], jnp.exp(logits - new_max[:, :, None]), 0.0)
    new_sum = jnp.sum(weights, axis=2)
    gained = jnp.einsum(
        "hqk,khd->hqd",
        weights.astype(jnp.bfloat16),
        value_heads,
        preferred_element_type=jnp.float32,
    )
    inner_state = (new_max, new_sum, gained)
    run_max, run_sum, run_out, kept_keys, kept_values = inner_state + (kept_keys, kept_values)
    mixed = (run_out / run_sum[:, :, None]).astype(jnp.bfloat16)
    mixed = jnp.transpose(mixed, (1, 0, 2)).reshape(tok_here, feat_width)
    out_parts = jnp.einsum(
        "tc,oc->to",
        mixed,
        lax.all_gather(out_weight, "ctx", axis=0, tiled=True),
        preferred_element_type=jnp.float32,
    )
    head_total = exp_reduce_rows(out_parts)
    stream = (residual[0].astype(jnp.float32) + head_total).astype(jnp.bfloat16)
    stream_f = stream.astype(jnp.float32)
    mean_sq = jnp.mean(stream_f * stream_f, axis=1, keepdims=True)
    normed = (stream_f * lax.rsqrt(mean_sq + EPS) * norm_gain).astype(jnp.bfloat16)
    capacity = min(tok_here, 2 * max(1, 3 * tok_here * TOP // (4 * n_ctx)))
    dispatch, combine = slot_tables(routes[0], route_weights[0], n_ctx, capacity)
    if lax.axis_size("exp") == 2:
        moe_rows = moe_column_halves(
            normed, dispatch, combine, gate_weight[0], up_weight[0], down_weight[0], n_ctx, capacity
        )
    else:
        moe_rows = moe_whole_rows(
            normed, dispatch, combine, gate_weight[0], up_weight[0], down_weight[0], n_ctx, capacity
        )
    layer_out = (stream.astype(jnp.float32) + moe_rows).astype(jnp.bfloat16)
    return (
        layer_out[None],
        kept_keys.astype(jnp.bfloat16)[None],
        kept_values.astype(jnp.bfloat16)[None],
    )


def solution(mesh):
    return jax.shard_map(
        local,
        mesh=mesh,
        in_specs=(
            P("req", "ctx", "exp"),
            P("req", "ctx", "exp"),
            P("req", "ctx", "exp"),
            P("req", ("ctx", "exp"), None),
            P("ctx", "exp"),
            P(),
            P("ctx", None, "exp"),
            P("ctx", None, "exp"),
            P("ctx", "exp", None),
            P("req", "ctx", None),
            P("req", "ctx", None),
            P("req"),
        ),
        out_specs=(P("req", ("ctx", "exp"), None), P("req", "ctx", "exp"), P("req", "ctx", "exp")),
        check_vma=False,
    )
```

```python
import jax
import jax.numpy as jnp
from jax import lax
from jax.sharding import PartitionSpec as P

D = 2048
HD = 128
TOP = 4


EPS = 1e-06
NEG = -1e30


def row_positions(row_ids, half_block, n_groups):
    block_ids = row_ids // half_block
    device = block_ids // 2
    target = jnp.where(block_ids % 2 == 0, device, 2 * n_groups - 1 - device)
    return target * half_block + row_ids % half_block


def slot_tables(route_block, weight_block, experts, capacity):
    tok_here, top_here = route_block.shape
    flat_ids = route_block.reshape(tok_here * top_here)
    hit_table = (flat_ids[:, None] == jnp.arange(experts, dtype=jnp.int32)[None, :]).astype(
        jnp.int32
    )
    before = jnp.cumsum(hit_table, axis=0) - hit_table
    slot_rank = jnp.sum(before * hit_table, axis=1)
    slot_index = flat_ids * capacity + slot_rank
    slot_match = (
        jnp.arange(experts * capacity, dtype=jnp.int32)[:, None] == slot_index[None, :]
    ).astype(jnp.float32)
    slot_match = slot_match.reshape(experts * capacity, tok_here, top_here)
    dispatch = jnp.sum(slot_match, axis=2)
    combine = jnp.transpose(jnp.sum(slot_match * weight_block[None, :, :], axis=2))
    return (dispatch, combine)


def expert_ffn(token_rows, gate_matrix, up_matrix, down_matrix):
    gate_act = jnp.dot(token_rows, gate_matrix, preferred_element_type=jnp.float32)
    up_act = jnp.dot(token_rows, up_matrix, preferred_element_type=jnp.float32)
    hidden = (jax.nn.silu(gate_act) * up_act).astype(jnp.bfloat16)
    return jnp.dot(hidden, down_matrix, preferred_element_type=jnp.float32)


def exp_swap(x):
    return lax.ppermute(x, "exp", perm=[(0, 1), (1, 0)])


def exp_reduce_rows(parts):
    if lax.axis_size("exp") != 2:
        return lax.psum_scatter(
            parts.astype(jnp.bfloat16), "exp", scatter_dimension=0, tiled=True
        ).astype(jnp.float32)
    half = parts.shape[0] // 2
    first = lax.axis_index("exp") == 0
    lower = parts[:half]
    upper = parts[half:]
    mine = jnp.where(first, lower, upper)
    theirs = jnp.where(first, upper, lower)
    got = exp_swap(theirs.astype(jnp.bfloat16))
    return mine + got.astype(jnp.float32)


def exp_gather_rows(rows):
    if lax.axis_size("exp") != 2:
        return lax.all_gather(rows, "exp", axis=0, tiled=True)
    got = exp_swap(rows)
    first = lax.axis_index("exp") == 0
    return jnp.where(
        first, jnp.concatenate([rows, got], axis=0), jnp.concatenate([got, rows], axis=0)
    )


def moe_whole_rows(normed, dispatch, combine, gate_matrix, up_matrix, down_matrix, n_ctx, capacity):
    all_normed = lax.all_gather(normed, "exp", axis=0, tiled=True)
    send_rows = jnp.dot(
        dispatch.astype(jnp.bfloat16), all_normed, preferred_element_type=jnp.float32
    ).astype(jnp.bfloat16)
    send_rows = send_rows.reshape(n_ctx, capacity, D)
    arrived = lax.all_to_all(send_rows, "ctx", split_axis=0, concat_axis=0, tiled=True)
    flat_rows = arrived.reshape(n_ctx * capacity, D)
    produced = expert_ffn(flat_rows, gate_matrix, up_matrix, down_matrix).reshape(
        n_ctx, capacity, D
    )
    served = lax.all_to_all(
        produced.astype(jnp.bfloat16), "ctx", split_axis=0, concat_axis=0, tiled=True
    )
    results = served.reshape(n_ctx * capacity, D).astype(jnp.float32)
    moe_part = jnp.dot(
        combine, results, precision=lax.Precision.HIGHEST, preferred_element_type=jnp.float32
    )
    return lax.psum_scatter(
        moe_part.astype(jnp.bfloat16), "exp", scatter_dimension=0, tiled=True
    ).astype(jnp.float32)


def halves(x, first, axis):
    size = x.shape[axis] // 2
    lower = lax.slice_in_dim(x, 0, size, axis=axis)
    upper = lax.slice_in_dim(x, size, 2 * size, axis=axis)
    return jnp.where(first, lower, upper), jnp.where(first, upper, lower)


def join(mine, theirs, first, axis):
    return jnp.where(
        first,
        jnp.concatenate([mine, theirs], axis=axis),
        jnp.concatenate([theirs, mine], axis=axis),
    )


def moe_column_halves(normed, dispatch, combine, gate_matrix, up_matrix, down_matrix, n_ctx, capacity):
    my_exp = lax.axis_index("exp")
    first = my_exp == 0
    half_d = normed.shape[1] // 2
    my_cols, other_cols = halves(normed, first, 1)
    tokens_cols = join(my_cols, exp_swap(other_cols), first, 0)
    tok_count = tokens_cols.shape[0]
    my_ctx = lax.axis_index("ctx")
    n_chip = n_ctx // 2
    my_chip = my_ctx // 2
    my_core = my_ctx % 2
    chips = (my_chip + jnp.arange(n_chip, dtype=jnp.int32)) % n_chip
    expert_ids = jnp.concatenate([chips * 2 + my_core, chips * 2 + (1 - my_core)])
    dispatch_ord = jnp.take(dispatch.reshape(n_ctx, capacity, tok_count), expert_ids, axis=0)
    send_rows = jnp.dot(
        dispatch_ord.reshape(n_ctx * capacity, tok_count).astype(jnp.bfloat16),
        tokens_cols,
        preferred_element_type=jnp.float32,
    ).astype(jnp.bfloat16)
    send_rows = send_rows.reshape(2, n_chip, capacity, half_d)
    core_swap = [(i, i ^ 1) for i in range(n_ctx)]
    from_partner = lax.ppermute(send_rows[1], "ctx", perm=core_swap)
    pairs = jnp.stack([send_rows[0], from_partner], axis=1)
    arrived = [pairs[0]]
    for shift in range(1, n_chip):
        perm = [(i, ((i // 2 + shift) % n_chip) * 2 + i % 2) for i in range(n_ctx)]
        arrived.append(lax.ppermute(pairs[shift], "ctx", perm=perm))
    my_start = my_exp * half_d
    other_start = (1 - my_exp) * half_d
    gate_mine = lax.dynamic_slice_in_dim(gate_matrix, my_start, half_d, axis=0)
    gate_other = lax.dynamic_slice_in_dim(gate_matrix, other_start, half_d, axis=0)
    up_mine = lax.dynamic_slice_in_dim(up_matrix, my_start, half_d, axis=0)
    up_other = lax.dynamic_slice_in_dim(up_matrix, other_start, half_d, axis=0)
    down_other = lax.dynamic_slice_in_dim(down_matrix, other_start, half_d, axis=1)
    down_mine = lax.dynamic_slice_in_dim(down_matrix, my_start, half_d, axis=1)
    per_group = 1 if n_chip <= 4 else n_chip // 2
    n_groups = n_chip // per_group
    returned = [None] * n_chip
    for group in range(n_groups):
        shifts = range(group * per_group, (group + 1) * per_group)
        block = jnp.concatenate([arrived[k] for k in shifts], axis=0).reshape(-1, half_d)
        partner_cols = exp_swap(block)
        gate_act = jnp.dot(block, gate_mine, preferred_element_type=jnp.float32) + jnp.dot(
            partner_cols, gate_other, preferred_element_type=jnp.float32
        )
        up_act = jnp.dot(block, up_mine, preferred_element_type=jnp.float32) + jnp.dot(
            partner_cols, up_other, preferred_element_type=jnp.float32
        )
        hidden = (jax.nn.silu(gate_act) * up_act).astype(jnp.bfloat16)
        out_other = jnp.dot(hidden, down_other, preferred_element_type=jnp.float32)
        got_other = exp_swap(out_other.astype(jnp.bfloat16))
        out_mine = jnp.dot(hidden, down_mine, preferred_element_type=jnp.float32)
        summed = (out_mine + got_other.astype(jnp.float32)).astype(jnp.bfloat16)
        summed = summed.reshape(per_group, 2, capacity, half_d)
        for idx, shift in enumerate(shifts):
            if shift == 0:
                returned[shift] = summed[idx]
            else:
                perm = [(i, ((i // 2 - shift) % n_chip) * 2 + i % 2) for i in range(n_ctx)]
                returned[shift] = lax.ppermute(summed[idx], "ctx", perm=perm)
    back = jnp.stack(returned)
    partner_res = lax.ppermute(back[:, 1], "ctx", perm=core_swap)
    served = jnp.stack([back[:, 0], partner_res]).reshape(n_ctx * capacity, half_d)
    combine_ord = jnp.take(combine.reshape(tok_count, n_ctx, capacity), expert_ids, axis=1)
    moe_half = jnp.dot(
        combine_ord.reshape(tok_count, n_ctx * capacity),
        served.astype(jnp.float32),
        precision=lax.Precision.HIGHEST,
        preferred_element_type=jnp.float32,
    )
    my_tok, other_tok = halves(moe_half, first, 0)
    got_tok = exp_swap(other_tok.astype(jnp.bfloat16)).astype(jnp.float32)
    return join(my_tok, got_tok, first, 1)


def ctx_gather_blocks(rows, n_ctx, my_ctx):
    n_chip = n_ctx // 2
    my_chip = my_ctx // 2
    my_core = my_ctx % 2
    stack = [rows]
    for shift in range(1, n_chip):
        perm = [(i, ((i // 2 + shift) % n_chip) * 2 + i % 2) for i in range(n_ctx)]
        stack.append(lax.ppermute(rows, "ctx", perm=perm))
    own = jnp.stack(stack)
    partner = lax.ppermute(own, "ctx", perm=[(i, i ^ 1) for i in range(n_ctx)])
    shifts = jnp.arange(n_chip, dtype=jnp.int32)
    chips = (my_chip - shifts) % n_chip
    src_ctx = jnp.concatenate([chips * 2 + my_core, chips * 2 + (1 - my_core)])
    return jnp.concatenate([own, partner]), src_ctx


def local(
    query_states,
    key_states,
    value_states,
    residual,
    out_weight,
    norm_gain,
    gate_weight,
    up_weight,
    down_weight,
    routes,
    route_weights,
    prompt_lengths,
):
    n_ctx = lax.axis_size("ctx")
    my_ctx = lax.axis_index("ctx")
    tok_here = query_states.shape[1]
    feat_width = query_states.shape[2]
    heads_dev = feat_width // HD
    half_block = tok_here // 2
    score_scale = HD ** (-0.5)
    length = prompt_lengths[0]
    local_ids = jnp.arange(tok_here, dtype=jnp.int32)
    query_pos = row_positions(my_ctx * tok_here + local_ids, half_block, n_ctx)
    decode_pos = my_ctx * tok_here + local_ids
    query_three = query_states[0].reshape(tok_here, heads_dev, HD)
    run_max = jnp.full((heads_dev, tok_here), NEG, jnp.float32)
    kv_here = jnp.concatenate([key_states[0], value_states[0]], axis=1)
    kv_blocks, src_ctx = ctx_gather_blocks(kv_here, n_ctx, my_ctx)
    kv_all = kv_blocks.reshape(n_ctx * tok_here, 2 * feat_width)
    key_two = kv_all[:, :feat_width]
    value_two = kv_all[:, feat_width:]
    row_count = key_two.shape[0]
    row_ids = (src_ctx[:, None] * tok_here + local_ids[None, :]).reshape(row_count)
    key_pos = row_positions(row_ids, half_block, n_ctx)
    pick_rows = (decode_pos[:, None] == key_pos[None, :]).astype(jnp.bfloat16)
    kept_keys = jnp.dot(pick_rows, key_two, preferred_element_type=jnp.float32)
    kept_values = jnp.dot(pick_rows, value_two, preferred_element_type=jnp.float32)
    old_max = run_max
    key_heads = key_two.reshape(row_count, heads_dev, HD)
    value_heads = value_two.reshape(row_count, heads_dev, HD)
    logits = (
        jnp.einsum("qhd,khd->hqk", query_three, key_heads, preferred_element_type=jnp.float32)
        * score_scale
    )
    visible = (key_pos[None, :] <= query_pos[:, None]) & (key_pos[None, :] < length)
    logits = jnp.where(visible[None], logits, NEG)
    new_max = jnp.maximum(old_max, jnp.max(logits, axis=2))
    weights = jnp.where(visible[None], jnp.exp(logits - new_max[:, :, None]), 0.0)
    new_sum = jnp.sum(weights, axis=2)
    gained = jnp.einsum(
        "hqk,khd->hqd",
        weights.astype(jnp.bfloat16),
        value_heads,
        preferred_element_type=jnp.float32,
    )
    inner_state = (new_max, new_sum, gained)
    run_max, run_sum, run_out, kept_keys, kept_values = inner_state + (kept_keys, kept_values)
    mixed = (run_out / run_sum[:, :, None]).astype(jnp.bfloat16)
    mixed = jnp.transpose(mixed, (1, 0, 2)).reshape(tok_here, feat_width)
    out_parts = jnp.einsum(
        "tc,oc->to",
        mixed,
        lax.all_gather(out_weight, "ctx", axis=0, tiled=True),
        preferred_element_type=jnp.float32,
    )
    head_total = exp_reduce_rows(out_parts)
    stream = (residual[0].astype(jnp.float32) + head_total).astype(jnp.bfloat16)
    stream_f = stream.astype(jnp.float32)
    mean_sq = jnp.mean(stream_f * stream_f, axis=1, keepdims=True)
    normed = (stream_f * lax.rsqrt(mean_sq + EPS) * norm_gain).astype(jnp.bfloat16)
    capacity = min(tok_here, 2 * max(1, 3 * tok_here * TOP // (4 * n_ctx)))
    dispatch, combine = slot_tables(routes[0], route_weights[0], n_ctx, capacity)
    if lax.axis_size("exp") == 2:
        moe_rows = moe_column_halves(
            normed, dispatch, combine, gate_weight[0], up_weight[0], down_weight[0], n_ctx, capacity
        )
    else:
        moe_rows = moe_whole_rows(
            normed, dispatch, combine, gate_weight[0], up_weight[0], down_weight[0], n_ctx, capacity
        )
    layer_out = (stream.astype(jnp.float32) + moe_rows).astype(jnp.bfloat16)
    return (
        layer_out[None],
        kept_keys.astype(jnp.bfloat16)[None],
        kept_values.astype(jnp.bfloat16)[None],
    )


def solution(mesh):
    return jax.shard_map(
        local,
        mesh=mesh,
        in_specs=(
            P("req", "ctx", "exp"),
            P("req", "ctx", "exp"),
            P("req", "ctx", "exp"),
            P("req", ("ctx", "exp"), None),
            P("ctx", "exp"),
            P(),
            P("ctx", None, "exp"),
            P("ctx", None, "exp"),
            P("ctx", "exp", None),
            P("req", "ctx", None),
            P("req", "ctx", None),
            P("req"),
        ),
        out_specs=(P("req", ("ctx", "exp"), None), P("req", "ctx", "exp"), P("req", "ctx", "exp")),
        check_vma=False,
    )
```

```python
import jax
import jax.numpy as jnp
from jax import lax
from jax.sharding import PartitionSpec as P

D = 2048
HD = 128
TOP = 4


EPS = 1e-06
NEG = -1e30


def row_positions(row_ids, half_block, n_groups):
    block_ids = row_ids // half_block
    device = block_ids // 2
    target = jnp.where(block_ids % 2 == 0, device, 2 * n_groups - 1 - device)
    return target * half_block + row_ids % half_block


def slot_tables(route_block, weight_block, experts, capacity, block_of=None):
    tok_here, top_here = route_block.shape
    flat_ids = route_block.reshape(tok_here * top_here)
    hit_table = (flat_ids[:, None] == jnp.arange(experts, dtype=jnp.int32)[None, :]).astype(
        jnp.int32
    )
    before = jnp.cumsum(hit_table, axis=0) - hit_table
    slot_rank = jnp.sum(before * hit_table, axis=1)
    blocks = flat_ids if block_of is None else block_of(flat_ids)
    slot_index = blocks * capacity + slot_rank
    slot_match = (
        jnp.arange(experts * capacity, dtype=jnp.int32)[:, None] == slot_index[None, :]
    ).astype(jnp.float32)
    slot_match = slot_match.reshape(experts * capacity, tok_here, top_here)
    dispatch = jnp.sum(slot_match, axis=2)
    combine = jnp.transpose(jnp.sum(slot_match * weight_block[None, :, :], axis=2))
    return (dispatch, combine)


def expert_ffn(token_rows, gate_matrix, up_matrix, down_matrix):
    gate_act = jnp.dot(token_rows, gate_matrix, preferred_element_type=jnp.float32)
    up_act = jnp.dot(token_rows, up_matrix, preferred_element_type=jnp.float32)
    hidden = (jax.nn.silu(gate_act) * up_act).astype(jnp.bfloat16)
    return jnp.dot(hidden, down_matrix, preferred_element_type=jnp.float32)


def exp_swap(x):
    return lax.ppermute(x, "exp", perm=[(0, 1), (1, 0)])


def exp_reduce_rows(parts):
    if lax.axis_size("exp") != 2:
        return lax.psum_scatter(
            parts.astype(jnp.bfloat16), "exp", scatter_dimension=0, tiled=True
        ).astype(jnp.float32)
    half = parts.shape[0] // 2
    first = lax.axis_index("exp") == 0
    lower = parts[:half]
    upper = parts[half:]
    mine = jnp.where(first, lower, upper)
    theirs = jnp.where(first, upper, lower)
    got = exp_swap(theirs.astype(jnp.bfloat16))
    return mine + got.astype(jnp.float32)


def exp_gather_rows(rows):
    if lax.axis_size("exp") != 2:
        return lax.all_gather(rows, "exp", axis=0, tiled=True)
    got = exp_swap(rows)
    first = lax.axis_index("exp") == 0
    return jnp.where(
        first, jnp.concatenate([rows, got], axis=0), jnp.concatenate([got, rows], axis=0)
    )


def moe_whole_rows(normed, dispatch, combine, gate_matrix, up_matrix, down_matrix, n_ctx, capacity):
    all_normed = lax.all_gather(normed, "exp", axis=0, tiled=True)
    send_rows = jnp.dot(
        dispatch.astype(jnp.bfloat16), all_normed, preferred_element_type=jnp.float32
    ).astype(jnp.bfloat16)
    send_rows = send_rows.reshape(n_ctx, capacity, D)
    arrived = lax.all_to_all(send_rows, "ctx", split_axis=0, concat_axis=0, tiled=True)
    flat_rows = arrived.reshape(n_ctx * capacity, D)
    produced = expert_ffn(flat_rows, gate_matrix, up_matrix, down_matrix).reshape(
        n_ctx, capacity, D
    )
    served = lax.all_to_all(
        produced.astype(jnp.bfloat16), "ctx", split_axis=0, concat_axis=0, tiled=True
    )
    results = served.reshape(n_ctx * capacity, D).astype(jnp.float32)
    moe_part = jnp.dot(
        combine, results, precision=lax.Precision.HIGHEST, preferred_element_type=jnp.float32
    )
    return lax.psum_scatter(
        moe_part.astype(jnp.bfloat16), "exp", scatter_dimension=0, tiled=True
    ).astype(jnp.float32)


def halves(x, first, axis):
    size = x.shape[axis] // 2
    lower = lax.slice_in_dim(x, 0, size, axis=axis)
    upper = lax.slice_in_dim(x, size, 2 * size, axis=axis)
    return jnp.where(first, lower, upper), jnp.where(first, upper, lower)


def join(mine, theirs, first, axis):
    return jnp.where(
        first,
        jnp.concatenate([mine, theirs], axis=axis),
        jnp.concatenate([theirs, mine], axis=axis),
    )


def moe_column_halves(normed, dispatch, combine, gate_matrix, up_matrix, down_matrix, n_ctx, capacity):
    my_exp = lax.axis_index("exp")
    first = my_exp == 0
    half_d = normed.shape[1] // 2
    my_cols, other_cols = halves(normed, first, 1)
    tokens_cols = join(my_cols, exp_swap(other_cols), first, 0)
    tok_count = tokens_cols.shape[0]
    my_ctx = lax.axis_index("ctx")
    n_chip = n_ctx // 2
    my_chip = my_ctx // 2
    my_core = my_ctx % 2
    send_rows = jnp.dot(
        dispatch.astype(jnp.bfloat16),
        tokens_cols,
        preferred_element_type=jnp.float32,
    ).astype(jnp.bfloat16)
    send_rows = send_rows.reshape(2, n_chip, capacity, half_d)
    core_swap = [(i, i ^ 1) for i in range(n_ctx)]
    from_partner = lax.ppermute(send_rows[1], "ctx", perm=core_swap)
    pairs = jnp.stack([send_rows[0], from_partner], axis=1)
    arrived = [pairs[0]]
    for shift in range(1, n_chip):
        perm = [(i, ((i // 2 + shift) % n_chip) * 2 + i % 2) for i in range(n_ctx)]
        arrived.append(lax.ppermute(pairs[shift], "ctx", perm=perm))
    my_start = my_exp * half_d
    other_start = (1 - my_exp) * half_d
    gate_mine = lax.dynamic_slice_in_dim(gate_matrix, my_start, half_d, axis=0)
    gate_other = lax.dynamic_slice_in_dim(gate_matrix, other_start, half_d, axis=0)
    up_mine = lax.dynamic_slice_in_dim(up_matrix, my_start, half_d, axis=0)
    up_other = lax.dynamic_slice_in_dim(up_matrix, other_start, half_d, axis=0)
    down_other = lax.dynamic_slice_in_dim(down_matrix, other_start, half_d, axis=1)
    down_mine = lax.dynamic_slice_in_dim(down_matrix, my_start, half_d, axis=1)
    per_group = 1 if n_chip <= 4 else n_chip // 2
    n_groups = n_chip // per_group
    returned = [None] * n_chip
    for group in range(n_groups):
        shifts = range(group * per_group, (group + 1) * per_group)
        block = jnp.concatenate([arrived[k] for k in shifts], axis=0).reshape(-1, half_d)
        partner_cols = exp_swap(block)
        gate_act = jnp.dot(block, gate_mine, preferred_element_type=jnp.float32) + jnp.dot(
            partner_cols, gate_other, preferred_element_type=jnp.float32
        )
        up_act = jnp.dot(block, up_mine, preferred_element_type=jnp.float32) + jnp.dot(
            partner_cols, up_other, preferred_element_type=jnp.float32
        )
        hidden = (jax.nn.silu(gate_act) * up_act).astype(jnp.bfloat16)
        out_other = jnp.dot(hidden, down_other, preferred_element_type=jnp.float32)
        got_other = exp_swap(out_other.astype(jnp.bfloat16))
        out_mine = jnp.dot(hidden, down_mine, preferred_element_type=jnp.float32)
        summed = (out_mine + got_other.astype(jnp.float32)).astype(jnp.bfloat16)
        summed = summed.reshape(per_group, 2, capacity, half_d)
        for idx, shift in enumerate(shifts):
            if shift == 0:
                returned[shift] = summed[idx]
            else:
                perm = [(i, ((i // 2 - shift) % n_chip) * 2 + i % 2) for i in range(n_ctx)]
                returned[shift] = lax.ppermute(summed[idx], "ctx", perm=perm)
    back = jnp.stack(returned)
    partner_res = lax.ppermute(back[:, 1], "ctx", perm=core_swap)
    served = jnp.stack([back[:, 0], partner_res]).reshape(n_ctx * capacity, half_d)
    moe_half = jnp.dot(
        combine,
        served.astype(jnp.float32),
        precision=lax.Precision.HIGHEST,
        preferred_element_type=jnp.float32,
    )
    my_tok, other_tok = halves(moe_half, first, 0)
    got_tok = exp_swap(other_tok.astype(jnp.bfloat16)).astype(jnp.float32)
    return join(my_tok, got_tok, first, 1)


def ctx_gather_blocks(rows, n_ctx, my_ctx):
    n_chip = n_ctx // 2
    my_chip = my_ctx // 2
    my_core = my_ctx % 2
    stack = [rows]
    for shift in range(1, n_chip):
        perm = [(i, ((i // 2 + shift) % n_chip) * 2 + i % 2) for i in range(n_ctx)]
        stack.append(lax.ppermute(rows, "ctx", perm=perm))
    own = jnp.stack(stack)
    partner = lax.ppermute(own, "ctx", perm=[(i, i ^ 1) for i in range(n_ctx)])
    shifts = jnp.arange(n_chip, dtype=jnp.int32)
    chips = (my_chip - shifts) % n_chip
    src_ctx = jnp.concatenate([chips * 2 + my_core, chips * 2 + (1 - my_core)])
    return jnp.concatenate([own, partner]), src_ctx


def local(
    query_states,
    key_states,
    value_states,
    residual,
    out_weight,
    norm_gain,
    gate_weight,
    up_weight,
    down_weight,
    routes,
    route_weights,
    prompt_lengths,
):
    n_ctx = lax.axis_size("ctx")
    my_ctx = lax.axis_index("ctx")
    tok_here = query_states.shape[1]
    feat_width = query_states.shape[2]
    heads_dev = feat_width // HD
    half_block = tok_here // 2
    score_scale = HD ** (-0.5)
    length = prompt_lengths[0]
    local_ids = jnp.arange(tok_here, dtype=jnp.int32)
    query_pos = row_positions(my_ctx * tok_here + local_ids, half_block, n_ctx)
    decode_pos = my_ctx * tok_here + local_ids
    query_three = query_states[0].reshape(tok_here, heads_dev, HD)
    run_max = jnp.full((heads_dev, tok_here), NEG, jnp.float32)
    kv_here = jnp.concatenate([key_states[0], value_states[0]], axis=1)
    kv_blocks, src_ctx = ctx_gather_blocks(kv_here, n_ctx, my_ctx)
    kv_all = kv_blocks.reshape(n_ctx * tok_here, 2 * feat_width)
    key_two = kv_all[:, :feat_width]
    value_two = kv_all[:, feat_width:]
    row_count = key_two.shape[0]
    row_ids = (src_ctx[:, None] * tok_here + local_ids[None, :]).reshape(row_count)
    key_pos = row_positions(row_ids, half_block, n_ctx)
    pick_rows = (decode_pos[:, None] == key_pos[None, :]).astype(jnp.bfloat16)
    kept_keys = jnp.dot(pick_rows, key_two, preferred_element_type=jnp.float32)
    kept_values = jnp.dot(pick_rows, value_two, preferred_element_type=jnp.float32)
    old_max = run_max
    key_heads = key_two.reshape(row_count, heads_dev, HD)
    value_heads = value_two.reshape(row_count, heads_dev, HD)
    logits = (
        jnp.einsum("qhd,khd->hqk", query_three, key_heads, preferred_element_type=jnp.float32)
        * score_scale
    )
    visible = (key_pos[None, :] <= query_pos[:, None]) & (key_pos[None, :] < length)
    logits = jnp.where(visible[None], logits, NEG)
    new_max = jnp.maximum(old_max, jnp.max(logits, axis=2))
    weights = jnp.where(visible[None], jnp.exp(logits - new_max[:, :, None]), 0.0)
    new_sum = jnp.sum(weights, axis=2)
    gained = jnp.einsum(
        "hqk,khd->hqd",
        weights.astype(jnp.bfloat16),
        value_heads,
        preferred_element_type=jnp.float32,
    )
    inner_state = (new_max, new_sum, gained)
    run_max, run_sum, run_out, kept_keys, kept_values = inner_state + (kept_keys, kept_values)
    mixed = (run_out / run_sum[:, :, None]).astype(jnp.bfloat16)
    mixed = jnp.transpose(mixed, (1, 0, 2)).reshape(tok_here, feat_width)
    out_parts = jnp.einsum(
        "tc,oc->to",
        mixed,
        lax.all_gather(out_weight, "ctx", axis=0, tiled=True),
        preferred_element_type=jnp.float32,
    )
    head_total = exp_reduce_rows(out_parts)
    stream = (residual[0].astype(jnp.float32) + head_total).astype(jnp.bfloat16)
    stream_f = stream.astype(jnp.float32)
    mean_sq = jnp.mean(stream_f * stream_f, axis=1, keepdims=True)
    normed = (stream_f * lax.rsqrt(mean_sq + EPS) * norm_gain).astype(jnp.bfloat16)
    capacity = min(tok_here, 2 * max(1, 3 * tok_here * TOP // (4 * n_ctx)))
    if lax.axis_size("exp") == 2:
        n_chip = n_ctx // 2

        def block_of(expert):
            other_core = (expert % 2 != my_ctx % 2).astype(jnp.int32)
            return other_core * n_chip + (expert // 2 - my_ctx // 2) % n_chip

        dispatch, combine = slot_tables(routes[0], route_weights[0], n_ctx, capacity, block_of)
        moe_rows = moe_column_halves(
            normed, dispatch, combine, gate_weight[0], up_weight[0], down_weight[0], n_ctx, capacity
        )
    else:
        dispatch, combine = slot_tables(routes[0], route_weights[0], n_ctx, capacity)
        moe_rows = moe_whole_rows(
            normed, dispatch, combine, gate_weight[0], up_weight[0], down_weight[0], n_ctx, capacity
        )
    layer_out = (stream.astype(jnp.float32) + moe_rows).astype(jnp.bfloat16)
    return (
        layer_out[None],
        kept_keys.astype(jnp.bfloat16)[None],
        kept_values.astype(jnp.bfloat16)[None],
    )


def solution(mesh):
    return jax.shard_map(
        local,
        mesh=mesh,
        in_specs=(
            P("req", "ctx", "exp"),
            P("req", "ctx", "exp"),
            P("req", "ctx", "exp"),
            P("req", ("ctx", "exp"), None),
            P("ctx", "exp"),
            P(),
            P("ctx", None, "exp"),
            P("ctx", None, "exp"),
            P("ctx", "exp", None),
            P("req", "ctx", None),
            P("req", "ctx", None),
            P("req"),
        ),
        out_specs=(P("req", ("ctx", "exp"), None), P("req", "ctx", "exp"), P("req", "ctx", "exp")),
        check_vma=False,
    )
```

```python
import jax
import jax.numpy as jnp
from jax import lax
from jax.sharding import PartitionSpec as P

D = 2048
HD = 128
TOP = 4


EPS = 1e-06
NEG = -1e30


def row_positions(row_ids, half_block, n_groups):
    block_ids = row_ids // half_block
    device = block_ids // 2
    target = jnp.where(block_ids % 2 == 0, device, 2 * n_groups - 1 - device)
    return target * half_block + row_ids % half_block


def slot_tables(route_block, weight_block, experts, capacity, block_of=None):
    tok_here, top_here = route_block.shape
    flat_ids = route_block.reshape(tok_here * top_here)
    hit_table = (flat_ids[:, None] == jnp.arange(experts, dtype=jnp.int32)[None, :]).astype(
        jnp.int32
    )
    before = jnp.cumsum(hit_table, axis=0) - hit_table
    slot_rank = jnp.sum(before * hit_table, axis=1)
    blocks = flat_ids if block_of is None else block_of(flat_ids)
    slot_index = blocks * capacity + slot_rank
    slot_match = (
        jnp.arange(experts * capacity, dtype=jnp.int32)[:, None] == slot_index[None, :]
    ).astype(jnp.float32)
    slot_match = slot_match.reshape(experts * capacity, tok_here, top_here)
    dispatch = jnp.sum(slot_match, axis=2)
    combine = jnp.transpose(jnp.sum(slot_match * weight_block[None, :, :], axis=2))
    return (dispatch, combine)


def expert_ffn(token_rows, gate_matrix, up_matrix, down_matrix):
    gate_act = jnp.dot(token_rows, gate_matrix, preferred_element_type=jnp.float32)
    up_act = jnp.dot(token_rows, up_matrix, preferred_element_type=jnp.float32)
    hidden = (jax.nn.silu(gate_act) * up_act).astype(jnp.bfloat16)
    return jnp.dot(hidden, down_matrix, preferred_element_type=jnp.float32)


def exp_swap(x):
    return lax.ppermute(x, "exp", perm=[(0, 1), (1, 0)])


def exp_reduce_rows(parts):
    if lax.axis_size("exp") != 2:
        return lax.psum_scatter(
            parts.astype(jnp.bfloat16), "exp", scatter_dimension=0, tiled=True
        ).astype(jnp.float32)
    half = parts.shape[0] // 2
    first = lax.axis_index("exp") == 0
    lower = parts[:half]
    upper = parts[half:]
    mine = jnp.where(first, lower, upper)
    theirs = jnp.where(first, upper, lower)
    got = exp_swap(theirs.astype(jnp.bfloat16))
    return mine + got.astype(jnp.float32)


def exp_gather_rows(rows):
    if lax.axis_size("exp") != 2:
        return lax.all_gather(rows, "exp", axis=0, tiled=True)
    got = exp_swap(rows)
    first = lax.axis_index("exp") == 0
    return jnp.where(
        first, jnp.concatenate([rows, got], axis=0), jnp.concatenate([got, rows], axis=0)
    )


def moe_whole_rows(normed, dispatch, combine, gate_matrix, up_matrix, down_matrix, n_ctx, capacity):
    all_normed = lax.all_gather(normed, "exp", axis=0, tiled=True)
    send_rows = jnp.dot(
        dispatch.astype(jnp.bfloat16), all_normed, preferred_element_type=jnp.float32
    ).astype(jnp.bfloat16)
    send_rows = send_rows.reshape(n_ctx, capacity, D)
    arrived = lax.all_to_all(send_rows, "ctx", split_axis=0, concat_axis=0, tiled=True)
    flat_rows = arrived.reshape(n_ctx * capacity, D)
    produced = expert_ffn(flat_rows, gate_matrix, up_matrix, down_matrix).reshape(
        n_ctx, capacity, D
    )
    served = lax.all_to_all(
        produced.astype(jnp.bfloat16), "ctx", split_axis=0, concat_axis=0, tiled=True
    )
    results = served.reshape(n_ctx * capacity, D).astype(jnp.float32)
    moe_part = jnp.dot(
        combine, results, precision=lax.Precision.HIGHEST, preferred_element_type=jnp.float32
    )
    return lax.psum_scatter(
        moe_part.astype(jnp.bfloat16), "exp", scatter_dimension=0, tiled=True
    ).astype(jnp.float32)


def halves(x, first, axis):
    size = x.shape[axis] // 2
    lower = lax.slice_in_dim(x, 0, size, axis=axis)
    upper = lax.slice_in_dim(x, size, 2 * size, axis=axis)
    return jnp.where(first, lower, upper), jnp.where(first, upper, lower)


def join(mine, theirs, first, axis):
    return jnp.where(
        first,
        jnp.concatenate([mine, theirs], axis=axis),
        jnp.concatenate([theirs, mine], axis=axis),
    )


def moe_column_halves(normed, dispatch, combine, gate_matrix, up_matrix, down_matrix, n_ctx, capacity):
    my_exp = lax.axis_index("exp")
    first = my_exp == 0
    half_d = normed.shape[1] // 2
    my_cols, other_cols = halves(normed, first, 1)
    tokens_cols = join(my_cols, exp_swap(other_cols), first, 0)
    tok_count = tokens_cols.shape[0]
    my_ctx = lax.axis_index("ctx")
    n_chip = n_ctx // 2
    my_chip = my_ctx // 2
    my_core = my_ctx % 2
    send_rows = jnp.dot(
        dispatch.astype(jnp.bfloat16),
        tokens_cols,
        preferred_element_type=jnp.float32,
    ).astype(jnp.bfloat16)
    send_rows = send_rows.reshape(2, n_chip, capacity, half_d)
    core_swap = [(i, i ^ 1) for i in range(n_ctx)]
    from_partner = lax.ppermute(send_rows[1], "ctx", perm=core_swap)
    pairs = jnp.stack([send_rows[0], from_partner], axis=1)
    arrived = [pairs[0]]
    for shift in range(1, n_chip):
        perm = [(i, ((i // 2 + shift) % n_chip) * 2 + i % 2) for i in range(n_ctx)]
        arrived.append(lax.ppermute(pairs[shift], "ctx", perm=perm))
    my_start = my_exp * half_d
    other_start = (1 - my_exp) * half_d
    gate_mine = lax.dynamic_slice_in_dim(gate_matrix, my_start, half_d, axis=0)
    gate_other = lax.dynamic_slice_in_dim(gate_matrix, other_start, half_d, axis=0)
    up_mine = lax.dynamic_slice_in_dim(up_matrix, my_start, half_d, axis=0)
    up_other = lax.dynamic_slice_in_dim(up_matrix, other_start, half_d, axis=0)
    down_other = lax.dynamic_slice_in_dim(down_matrix, other_start, half_d, axis=1)
    down_mine = lax.dynamic_slice_in_dim(down_matrix, my_start, half_d, axis=1)
    per_group = 1 if n_chip <= 4 else n_chip // 2
    n_groups = n_chip // per_group
    returned = [None] * n_chip
    for group in range(n_groups):
        shifts = range(group * per_group, (group + 1) * per_group)
        block = jnp.concatenate([arrived[k] for k in shifts], axis=0).reshape(-1, half_d)
        partner_cols = exp_swap(block)
        gate_act = jnp.dot(block, gate_mine, preferred_element_type=jnp.float32) + jnp.dot(
            partner_cols, gate_other, preferred_element_type=jnp.float32
        )
        up_act = jnp.dot(block, up_mine, preferred_element_type=jnp.float32) + jnp.dot(
            partner_cols, up_other, preferred_element_type=jnp.float32
        )
        hidden = (jax.nn.silu(gate_act) * up_act).astype(jnp.bfloat16)
        out_other = jnp.dot(hidden, down_other, preferred_element_type=jnp.float32)
        got_other = exp_swap(out_other.astype(jnp.bfloat16))
        out_mine = jnp.dot(hidden, down_mine, preferred_element_type=jnp.float32)
        summed = (out_mine + got_other.astype(jnp.float32)).astype(jnp.bfloat16)
        summed = summed.reshape(per_group, 2, capacity, half_d)
        for idx, shift in enumerate(shifts):
            if shift == 0:
                returned[shift] = summed[idx]
            else:
                perm = [(i, ((i // 2 - shift) % n_chip) * 2 + i % 2) for i in range(n_ctx)]
                returned[shift] = lax.ppermute(summed[idx], "ctx", perm=perm)
    back = jnp.stack(returned)
    partner_res = lax.ppermute(back[:, 1], "ctx", perm=core_swap)
    served = jnp.stack([back[:, 0], partner_res]).reshape(n_ctx * capacity, half_d)
    moe_half = jnp.dot(
        combine,
        served.astype(jnp.float32),
        precision=lax.Precision.HIGHEST,
        preferred_element_type=jnp.float32,
    )
    my_tok, other_tok = halves(moe_half, first, 0)
    got_tok = exp_swap(other_tok.astype(jnp.bfloat16)).astype(jnp.float32)
    return join(my_tok, got_tok, first, 1)


def ctx_gather_blocks(rows, n_ctx, my_ctx):
    n_chip = n_ctx // 2
    my_chip = my_ctx // 2
    my_core = my_ctx % 2
    stack = [rows]
    for shift in range(1, n_chip):
        perm = [(i, ((i // 2 + shift) % n_chip) * 2 + i % 2) for i in range(n_ctx)]
        stack.append(lax.ppermute(rows, "ctx", perm=perm))
    own = jnp.stack(stack)
    partner = lax.ppermute(own, "ctx", perm=[(i, i ^ 1) for i in range(n_ctx)])
    shifts = jnp.arange(n_chip, dtype=jnp.int32)
    chips = (my_chip - shifts) % n_chip
    src_ctx = jnp.concatenate([chips * 2 + my_core, chips * 2 + (1 - my_core)])
    return jnp.concatenate([own, partner]), src_ctx


def gather_out_weight(weight_rows, n_ctx, my_ctx):
    if n_ctx % 2:
        return lax.all_gather(weight_rows, "ctx", axis=0, tiled=True)
    blocks, _ = ctx_gather_blocks(weight_rows, n_ctx, my_ctx)
    n_chip = n_ctx // 2
    ctx_ids = jnp.arange(n_ctx, dtype=jnp.int32)
    other_core = (ctx_ids % 2 != my_ctx % 2).astype(jnp.int32)
    block_of = other_core * n_chip + (my_ctx // 2 - ctx_ids // 2) % n_chip
    return jnp.take(blocks, block_of, axis=0).reshape(n_ctx * weight_rows.shape[0], -1)


def local(
    query_states,
    key_states,
    value_states,
    residual,
    out_weight,
    norm_gain,
    gate_weight,
    up_weight,
    down_weight,
    routes,
    route_weights,
    prompt_lengths,
):
    n_ctx = lax.axis_size("ctx")
    my_ctx = lax.axis_index("ctx")
    tok_here = query_states.shape[1]
    feat_width = query_states.shape[2]
    heads_dev = feat_width // HD
    half_block = tok_here // 2
    score_scale = HD ** (-0.5)
    length = prompt_lengths[0]
    local_ids = jnp.arange(tok_here, dtype=jnp.int32)
    query_pos = row_positions(my_ctx * tok_here + local_ids, half_block, n_ctx)
    decode_pos = my_ctx * tok_here + local_ids
    query_three = query_states[0].reshape(tok_here, heads_dev, HD)
    run_max = jnp.full((heads_dev, tok_here), NEG, jnp.float32)
    kv_here = jnp.concatenate([key_states[0], value_states[0]], axis=1)
    kv_blocks, src_ctx = ctx_gather_blocks(kv_here, n_ctx, my_ctx)
    kv_all = kv_blocks.reshape(n_ctx * tok_here, 2 * feat_width)
    key_two = kv_all[:, :feat_width]
    value_two = kv_all[:, feat_width:]
    row_count = key_two.shape[0]
    row_ids = (src_ctx[:, None] * tok_here + local_ids[None, :]).reshape(row_count)
    key_pos = row_positions(row_ids, half_block, n_ctx)
    pick_rows = (decode_pos[:, None] == key_pos[None, :]).astype(jnp.bfloat16)
    kept_keys = jnp.dot(pick_rows, key_two, preferred_element_type=jnp.float32)
    kept_values = jnp.dot(pick_rows, value_two, preferred_element_type=jnp.float32)
    old_max = run_max
    key_heads = key_two.reshape(row_count, heads_dev, HD)
    value_heads = value_two.reshape(row_count, heads_dev, HD)
    logits = (
        jnp.einsum("qhd,khd->hqk", query_three, key_heads, preferred_element_type=jnp.float32)
        * score_scale
    )
    visible = (key_pos[None, :] <= query_pos[:, None]) & (key_pos[None, :] < length)
    logits = jnp.where(visible[None], logits, NEG)
    new_max = jnp.maximum(old_max, jnp.max(logits, axis=2))
    weights = jnp.where(visible[None], jnp.exp(logits - new_max[:, :, None]), 0.0)
    new_sum = jnp.sum(weights, axis=2)
    gained = jnp.einsum(
        "hqk,khd->hqd",
        weights.astype(jnp.bfloat16),
        value_heads,
        preferred_element_type=jnp.float32,
    )
    inner_state = (new_max, new_sum, gained)
    run_max, run_sum, run_out, kept_keys, kept_values = inner_state + (kept_keys, kept_values)
    mixed = (run_out / run_sum[:, :, None]).astype(jnp.bfloat16)
    mixed = jnp.transpose(mixed, (1, 0, 2)).reshape(tok_here, feat_width)
    out_parts = jnp.einsum(
        "tc,oc->to",
        mixed,
        gather_out_weight(out_weight, n_ctx, my_ctx),
        preferred_element_type=jnp.float32,
    )
    head_total = exp_reduce_rows(out_parts)
    stream = (residual[0].astype(jnp.float32) + head_total).astype(jnp.bfloat16)
    stream_f = stream.astype(jnp.float32)
    mean_sq = jnp.mean(stream_f * stream_f, axis=1, keepdims=True)
    normed = (stream_f * lax.rsqrt(mean_sq + EPS) * norm_gain).astype(jnp.bfloat16)
    capacity = min(tok_here, 2 * max(1, 3 * tok_here * TOP // (4 * n_ctx)))
    if lax.axis_size("exp") == 2:
        n_chip = n_ctx // 2

        def block_of(expert):
            other_core = (expert % 2 != my_ctx % 2).astype(jnp.int32)
            return other_core * n_chip + (expert // 2 - my_ctx // 2) % n_chip

        dispatch, combine = slot_tables(routes[0], route_weights[0], n_ctx, capacity, block_of)
        moe_rows = moe_column_halves(
            normed, dispatch, combine, gate_weight[0], up_weight[0], down_weight[0], n_ctx, capacity
        )
    else:
        dispatch, combine = slot_tables(routes[0], route_weights[0], n_ctx, capacity)
        moe_rows = moe_whole_rows(
            normed, dispatch, combine, gate_weight[0], up_weight[0], down_weight[0], n_ctx, capacity
        )
    layer_out = (stream.astype(jnp.float32) + moe_rows).astype(jnp.bfloat16)
    return (
        layer_out[None],
        kept_keys.astype(jnp.bfloat16)[None],
        kept_values.astype(jnp.bfloat16)[None],
    )


def solution(mesh):
    return jax.shard_map(
        local,
        mesh=mesh,
        in_specs=(
            P("req", "ctx", "exp"),
            P("req", "ctx", "exp"),
            P("req", "ctx", "exp"),
            P("req", ("ctx", "exp"), None),
            P("ctx", "exp"),
            P(),
            P("ctx", None, "exp"),
            P("ctx", None, "exp"),
            P("ctx", "exp", None),
            P("req", "ctx", None),
            P("req", "ctx", None),
            P("req"),
        ),
        out_specs=(P("req", ("ctx", "exp"), None), P("req", "ctx", "exp"), P("req", "ctx", "exp")),
        check_vma=False,
    )
```

```python
import jax
import jax.numpy as jnp
from jax import lax
from jax.sharding import PartitionSpec as P

D = 2048
HD = 128
TOP = 4


EPS = 1e-06
NEG = -1e30


def row_positions(row_ids, half_block, n_groups):
    block_ids = row_ids // half_block
    device = block_ids // 2
    target = jnp.where(block_ids % 2 == 0, device, 2 * n_groups - 1 - device)
    return target * half_block + row_ids % half_block


def slot_tables(route_block, weight_block, experts, capacity, block_of=None):
    tok_here, top_here = route_block.shape
    flat_ids = route_block.reshape(tok_here * top_here)
    hit_table = (flat_ids[:, None] == jnp.arange(experts, dtype=jnp.int32)[None, :]).astype(
        jnp.int32
    )
    before = jnp.cumsum(hit_table, axis=0) - hit_table
    slot_rank = jnp.sum(before * hit_table, axis=1)
    blocks = flat_ids if block_of is None else block_of(flat_ids)
    slot_index = blocks * capacity + slot_rank
    slot_match = (
        jnp.arange(experts * capacity, dtype=jnp.int32)[:, None] == slot_index[None, :]
    ).astype(jnp.float32)
    slot_match = slot_match.reshape(experts * capacity, tok_here, top_here)
    dispatch = jnp.sum(slot_match, axis=2)
    combine = jnp.transpose(jnp.sum(slot_match * weight_block[None, :, :], axis=2))
    return (dispatch, combine)


def expert_ffn(token_rows, gate_matrix, up_matrix, down_matrix):
    gate_act = jnp.dot(token_rows, gate_matrix, preferred_element_type=jnp.float32)
    up_act = jnp.dot(token_rows, up_matrix, preferred_element_type=jnp.float32)
    hidden = (jax.nn.silu(gate_act) * up_act).astype(jnp.bfloat16)
    return jnp.dot(hidden, down_matrix, preferred_element_type=jnp.float32)


def exp_swap(x):
    return lax.ppermute(x, "exp", perm=[(0, 1), (1, 0)])


def exp_reduce_rows(parts):
    if lax.axis_size("exp") != 2:
        return lax.psum_scatter(
            parts.astype(jnp.bfloat16), "exp", scatter_dimension=0, tiled=True
        ).astype(jnp.float32)
    half = parts.shape[0] // 2
    first = lax.axis_index("exp") == 0
    lower = parts[:half]
    upper = parts[half:]
    mine = jnp.where(first, lower, upper)
    theirs = jnp.where(first, upper, lower)
    got = exp_swap(theirs.astype(jnp.bfloat16))
    return mine + got.astype(jnp.float32)


def exp_gather_rows(rows):
    if lax.axis_size("exp") != 2:
        return lax.all_gather(rows, "exp", axis=0, tiled=True)
    got = exp_swap(rows)
    first = lax.axis_index("exp") == 0
    return jnp.where(
        first, jnp.concatenate([rows, got], axis=0), jnp.concatenate([got, rows], axis=0)
    )


def moe_whole_rows(normed, dispatch, combine, gate_matrix, up_matrix, down_matrix, n_ctx, capacity):
    all_normed = lax.all_gather(normed, "exp", axis=0, tiled=True)
    send_rows = jnp.dot(
        dispatch.astype(jnp.bfloat16), all_normed, preferred_element_type=jnp.float32
    ).astype(jnp.bfloat16)
    send_rows = send_rows.reshape(n_ctx, capacity, D)
    arrived = lax.all_to_all(send_rows, "ctx", split_axis=0, concat_axis=0, tiled=True)
    flat_rows = arrived.reshape(n_ctx * capacity, D)
    produced = expert_ffn(flat_rows, gate_matrix, up_matrix, down_matrix).reshape(
        n_ctx, capacity, D
    )
    served = lax.all_to_all(
        produced.astype(jnp.bfloat16), "ctx", split_axis=0, concat_axis=0, tiled=True
    )
    results = served.reshape(n_ctx * capacity, D).astype(jnp.float32)
    moe_part = jnp.dot(
        combine, results, precision=lax.Precision.HIGHEST, preferred_element_type=jnp.float32
    )
    return lax.psum_scatter(
        moe_part.astype(jnp.bfloat16), "exp", scatter_dimension=0, tiled=True
    ).astype(jnp.float32)


def halves(x, first, axis):
    size = x.shape[axis] // 2
    lower = lax.slice_in_dim(x, 0, size, axis=axis)
    upper = lax.slice_in_dim(x, size, 2 * size, axis=axis)
    return jnp.where(first, lower, upper), jnp.where(first, upper, lower)


def join(mine, theirs, first, axis):
    return jnp.where(
        first,
        jnp.concatenate([mine, theirs], axis=axis),
        jnp.concatenate([theirs, mine], axis=axis),
    )


def moe_column_halves(normed, dispatch, combine, gate_matrix, up_matrix, down_matrix, n_ctx, capacity):
    my_exp = lax.axis_index("exp")
    first = my_exp == 0
    half_d = normed.shape[1] // 2
    my_cols, other_cols = halves(normed, first, 1)
    tokens_cols = join(my_cols, exp_swap(other_cols), first, 0)
    tok_count = tokens_cols.shape[0]
    my_ctx = lax.axis_index("ctx")
    n_chip = n_ctx // 2
    my_chip = my_ctx // 2
    my_core = my_ctx % 2
    send_rows = jnp.dot(
        dispatch.astype(jnp.bfloat16),
        tokens_cols,
        preferred_element_type=jnp.float32,
    ).astype(jnp.bfloat16)
    send_rows = send_rows.reshape(2, n_chip, capacity, half_d)
    core_swap = [(i, i ^ 1) for i in range(n_ctx)]
    from_partner = lax.ppermute(send_rows[1], "ctx", perm=core_swap)
    pairs = jnp.stack([send_rows[0], from_partner], axis=1)
    arrived = [pairs[0]]
    for shift in range(1, n_chip):
        perm = [(i, ((i // 2 + shift) % n_chip) * 2 + i % 2) for i in range(n_ctx)]
        arrived.append(lax.ppermute(pairs[shift], "ctx", perm=perm))
    my_start = my_exp * half_d
    other_start = (1 - my_exp) * half_d
    gate_mine = lax.dynamic_slice_in_dim(gate_matrix, my_start, half_d, axis=0)
    gate_other = lax.dynamic_slice_in_dim(gate_matrix, other_start, half_d, axis=0)
    up_mine = lax.dynamic_slice_in_dim(up_matrix, my_start, half_d, axis=0)
    up_other = lax.dynamic_slice_in_dim(up_matrix, other_start, half_d, axis=0)
    down_other = lax.dynamic_slice_in_dim(down_matrix, other_start, half_d, axis=1)
    down_mine = lax.dynamic_slice_in_dim(down_matrix, my_start, half_d, axis=1)
    per_group = 1 if n_chip <= 4 else n_chip // 2
    n_groups = n_chip // per_group
    returned = [None] * n_chip
    for group in range(n_groups):
        shifts = range(group * per_group, (group + 1) * per_group)
        block = jnp.concatenate([arrived[k] for k in shifts], axis=0).reshape(-1, half_d)
        partner_cols = exp_swap(block)
        gate_act = jnp.dot(block, gate_mine, preferred_element_type=jnp.float32) + jnp.dot(
            partner_cols, gate_other, preferred_element_type=jnp.float32
        )
        up_act = jnp.dot(block, up_mine, preferred_element_type=jnp.float32) + jnp.dot(
            partner_cols, up_other, preferred_element_type=jnp.float32
        )
        hidden = (jax.nn.silu(gate_act) * up_act).astype(jnp.bfloat16)
        out_other = jnp.dot(hidden, down_other, preferred_element_type=jnp.float32)
        got_other = exp_swap(out_other.astype(jnp.bfloat16))
        out_mine = jnp.dot(hidden, down_mine, preferred_element_type=jnp.float32)
        summed = (out_mine + got_other.astype(jnp.float32)).astype(jnp.bfloat16)
        summed = summed.reshape(per_group, 2, capacity, half_d)
        for idx, shift in enumerate(shifts):
            if shift == 0:
                returned[shift] = summed[idx]
            else:
                perm = [(i, ((i // 2 - shift) % n_chip) * 2 + i % 2) for i in range(n_ctx)]
                returned[shift] = lax.ppermute(summed[idx], "ctx", perm=perm)
    back = jnp.stack(returned)
    partner_res = lax.ppermute(back[:, 1], "ctx", perm=core_swap)
    served = jnp.stack([back[:, 0], partner_res]).reshape(n_ctx * capacity, half_d)
    moe_half = jnp.dot(
        combine,
        served.astype(jnp.float32),
        precision=lax.Precision.HIGHEST,
        preferred_element_type=jnp.float32,
    )
    my_tok, other_tok = halves(moe_half, first, 0)
    got_tok = exp_swap(other_tok.astype(jnp.bfloat16)).astype(jnp.float32)
    return join(my_tok, got_tok, first, 1)


def ctx_gather_blocks(rows, n_ctx, my_ctx):
    n_chip = n_ctx // 2
    my_chip = my_ctx // 2
    my_core = my_ctx % 2
    stack = [rows]
    for shift in range(1, n_chip):
        perm = [(i, ((i // 2 + shift) % n_chip) * 2 + i % 2) for i in range(n_ctx)]
        stack.append(lax.ppermute(rows, "ctx", perm=perm))
    own = jnp.stack(stack)
    partner = lax.ppermute(own, "ctx", perm=[(i, i ^ 1) for i in range(n_ctx)])
    shifts = jnp.arange(n_chip, dtype=jnp.int32)
    chips = (my_chip - shifts) % n_chip
    src_ctx = jnp.concatenate([chips * 2 + my_core, chips * 2 + (1 - my_core)])
    return jnp.concatenate([own, partner]), src_ctx


def unrotate_blocks(blocks, n_ctx, my_ctx):
    n_chip = n_ctx // 2
    ctx_ids = jnp.arange(n_ctx, dtype=jnp.int32)
    other_core = (ctx_ids % 2 != my_ctx % 2).astype(jnp.int32)
    block_of = other_core * n_chip + (my_ctx // 2 - ctx_ids // 2) % n_chip
    return jnp.take(blocks, block_of, axis=0)


def local(
    query_states,
    key_states,
    value_states,
    residual,
    out_weight,
    norm_gain,
    gate_weight,
    up_weight,
    down_weight,
    routes,
    route_weights,
    prompt_lengths,
):
    n_ctx = lax.axis_size("ctx")
    my_ctx = lax.axis_index("ctx")
    tok_here = query_states.shape[1]
    feat_width = query_states.shape[2]
    heads_dev = feat_width // HD
    half_block = tok_here // 2
    score_scale = HD ** (-0.5)
    length = prompt_lengths[0]
    local_ids = jnp.arange(tok_here, dtype=jnp.int32)
    query_pos = row_positions(my_ctx * tok_here + local_ids, half_block, n_ctx)
    decode_pos = my_ctx * tok_here + local_ids
    query_three = query_states[0].reshape(tok_here, heads_dev, HD)
    run_max = jnp.full((heads_dev, tok_here), NEG, jnp.float32)
    kv_here = jnp.concatenate([key_states[0], value_states[0]], axis=1)
    weight_rows = out_weight.reshape(-1, 2 * feat_width)
    both_blocks, src_ctx = ctx_gather_blocks(
        jnp.concatenate([kv_here, weight_rows], axis=0), n_ctx, my_ctx
    )
    kv_blocks = both_blocks[:, :tok_here]
    weight_blocks = both_blocks[:, tok_here:].reshape(n_ctx, out_weight.shape[0], feat_width)
    weight_all = unrotate_blocks(weight_blocks, n_ctx, my_ctx).reshape(-1, feat_width)
    kv_all = kv_blocks.reshape(n_ctx * tok_here, 2 * feat_width)
    key_two = kv_all[:, :feat_width]
    value_two = kv_all[:, feat_width:]
    row_count = key_two.shape[0]
    row_ids = (src_ctx[:, None] * tok_here + local_ids[None, :]).reshape(row_count)
    key_pos = row_positions(row_ids, half_block, n_ctx)
    pick_rows = (decode_pos[:, None] == key_pos[None, :]).astype(jnp.bfloat16)
    kept_keys = jnp.dot(pick_rows, key_two, preferred_element_type=jnp.float32)
    kept_values = jnp.dot(pick_rows, value_two, preferred_element_type=jnp.float32)
    old_max = run_max
    key_heads = key_two.reshape(row_count, heads_dev, HD)
    value_heads = value_two.reshape(row_count, heads_dev, HD)
    logits = (
        jnp.einsum("qhd,khd->hqk", query_three, key_heads, preferred_element_type=jnp.float32)
        * score_scale
    )
    visible = (key_pos[None, :] <= query_pos[:, None]) & (key_pos[None, :] < length)
    logits = jnp.where(visible[None], logits, NEG)
    new_max = jnp.maximum(old_max, jnp.max(logits, axis=2))
    weights = jnp.where(visible[None], jnp.exp(logits - new_max[:, :, None]), 0.0)
    new_sum = jnp.sum(weights, axis=2)
    gained = jnp.einsum(
        "hqk,khd->hqd",
        weights.astype(jnp.bfloat16),
        value_heads,
        preferred_element_type=jnp.float32,
    )
    inner_state = (new_max, new_sum, gained)
    run_max, run_sum, run_out, kept_keys, kept_values = inner_state + (kept_keys, kept_values)
    mixed = (run_out / run_sum[:, :, None]).astype(jnp.bfloat16)
    mixed = jnp.transpose(mixed, (1, 0, 2)).reshape(tok_here, feat_width)
    out_parts = jnp.einsum(
        "tc,oc->to",
        mixed,
        weight_all,
        preferred_element_type=jnp.float32,
    )
    head_total = exp_reduce_rows(out_parts)
    stream = (residual[0].astype(jnp.float32) + head_total).astype(jnp.bfloat16)
    stream_f = stream.astype(jnp.float32)
    mean_sq = jnp.mean(stream_f * stream_f, axis=1, keepdims=True)
    normed = (stream_f * lax.rsqrt(mean_sq + EPS) * norm_gain).astype(jnp.bfloat16)
    capacity = min(tok_here, 2 * max(1, 3 * tok_here * TOP // (4 * n_ctx)))
    if lax.axis_size("exp") == 2:
        n_chip = n_ctx // 2

        def block_of(expert):
            other_core = (expert % 2 != my_ctx % 2).astype(jnp.int32)
            return other_core * n_chip + (expert // 2 - my_ctx // 2) % n_chip

        dispatch, combine = slot_tables(routes[0], route_weights[0], n_ctx, capacity, block_of)
        moe_rows = moe_column_halves(
            normed, dispatch, combine, gate_weight[0], up_weight[0], down_weight[0], n_ctx, capacity
        )
    else:
        dispatch, combine = slot_tables(routes[0], route_weights[0], n_ctx, capacity)
        moe_rows = moe_whole_rows(
            normed, dispatch, combine, gate_weight[0], up_weight[0], down_weight[0], n_ctx, capacity
        )
    layer_out = (stream.astype(jnp.float32) + moe_rows).astype(jnp.bfloat16)
    return (
        layer_out[None],
        kept_keys.astype(jnp.bfloat16)[None],
        kept_values.astype(jnp.bfloat16)[None],
    )


def solution(mesh):
    return jax.shard_map(
        local,
        mesh=mesh,
        in_specs=(
            P("req", "ctx", "exp"),
            P("req", "ctx", "exp"),
            P("req", "ctx", "exp"),
            P("req", ("ctx", "exp"), None),
            P("ctx", "exp"),
            P(),
            P("ctx", None, "exp"),
            P("ctx", None, "exp"),
            P("ctx", "exp", None),
            P("req", "ctx", None),
            P("req", "ctx", None),
            P("req"),
        ),
        out_specs=(P("req", ("ctx", "exp"), None), P("req", "ctx", "exp"), P("req", "ctx", "exp")),
        check_vma=False,
    )
```

```python
import jax
import jax.numpy as jnp
from jax import lax
from jax.sharding import PartitionSpec as P

D = 2048
HD = 128
TOP = 4


EPS = 1e-06
NEG = -1e30


def row_positions(row_ids, half_block, n_groups):
    block_ids = row_ids // half_block
    device = block_ids // 2
    target = jnp.where(block_ids % 2 == 0, device, 2 * n_groups - 1 - device)
    return target * half_block + row_ids % half_block


def slot_tables(route_block, weight_block, experts, capacity, block_of=None):
    tok_here, top_here = route_block.shape
    flat_ids = route_block.reshape(tok_here * top_here)
    hit_table = (flat_ids[:, None] == jnp.arange(experts, dtype=jnp.int32)[None, :]).astype(
        jnp.int32
    )
    before = jnp.cumsum(hit_table, axis=0) - hit_table
    slot_rank = jnp.sum(before * hit_table, axis=1)
    blocks = flat_ids if block_of is None else block_of(flat_ids)
    slot_index = blocks * capacity + slot_rank
    slot_match = (
        jnp.arange(experts * capacity, dtype=jnp.int32)[:, None] == slot_index[None, :]
    ).astype(jnp.float32)
    slot_match = slot_match.reshape(experts * capacity, tok_here, top_here)
    dispatch = jnp.sum(slot_match, axis=2)
    combine = jnp.transpose(jnp.sum(slot_match * weight_block[None, :, :], axis=2))
    return (dispatch, combine)


def expert_ffn(token_rows, gate_matrix, up_matrix, down_matrix):
    gate_act = jnp.dot(token_rows, gate_matrix, preferred_element_type=jnp.float32)
    up_act = jnp.dot(token_rows, up_matrix, preferred_element_type=jnp.float32)
    hidden = (jax.nn.silu(gate_act) * up_act).astype(jnp.bfloat16)
    return jnp.dot(hidden, down_matrix, preferred_element_type=jnp.float32)


def exp_swap(x):
    return lax.ppermute(x, "exp", perm=[(0, 1), (1, 0)])


def exp_reduce_rows(parts):
    if lax.axis_size("exp") != 2:
        return lax.psum_scatter(
            parts.astype(jnp.bfloat16), "exp", scatter_dimension=0, tiled=True
        ).astype(jnp.float32)
    half = parts.shape[0] // 2
    first = lax.axis_index("exp") == 0
    lower = parts[:half]
    upper = parts[half:]
    mine = jnp.where(first, lower, upper)
    theirs = jnp.where(first, upper, lower)
    got = exp_swap(theirs.astype(jnp.bfloat16))
    return mine + got.astype(jnp.float32)


def exp_gather_rows(rows):
    if lax.axis_size("exp") != 2:
        return lax.all_gather(rows, "exp", axis=0, tiled=True)
    got = exp_swap(rows)
    first = lax.axis_index("exp") == 0
    return jnp.where(
        first, jnp.concatenate([rows, got], axis=0), jnp.concatenate([got, rows], axis=0)
    )


def moe_whole_rows(normed, dispatch, combine, gate_matrix, up_matrix, down_matrix, n_ctx, capacity):
    all_normed = lax.all_gather(normed, "exp", axis=0, tiled=True)
    send_rows = jnp.dot(
        dispatch.astype(jnp.bfloat16), all_normed, preferred_element_type=jnp.float32
    ).astype(jnp.bfloat16)
    send_rows = send_rows.reshape(n_ctx, capacity, D)
    arrived = lax.all_to_all(send_rows, "ctx", split_axis=0, concat_axis=0, tiled=True)
    flat_rows = arrived.reshape(n_ctx * capacity, D)
    produced = expert_ffn(flat_rows, gate_matrix, up_matrix, down_matrix).reshape(
        n_ctx, capacity, D
    )
    served = lax.all_to_all(
        produced.astype(jnp.bfloat16), "ctx", split_axis=0, concat_axis=0, tiled=True
    )
    results = served.reshape(n_ctx * capacity, D).astype(jnp.float32)
    moe_part = jnp.dot(
        combine, results, precision=lax.Precision.HIGHEST, preferred_element_type=jnp.float32
    )
    return lax.psum_scatter(
        moe_part.astype(jnp.bfloat16), "exp", scatter_dimension=0, tiled=True
    ).astype(jnp.float32)


def halves(x, first, axis):
    size = x.shape[axis] // 2
    lower = lax.slice_in_dim(x, 0, size, axis=axis)
    upper = lax.slice_in_dim(x, size, 2 * size, axis=axis)
    return jnp.where(first, lower, upper), jnp.where(first, upper, lower)


def join(mine, theirs, first, axis):
    return jnp.where(
        first,
        jnp.concatenate([mine, theirs], axis=axis),
        jnp.concatenate([theirs, mine], axis=axis),
    )


def moe_column_halves(normed, dispatch, combine, gate_matrix, up_matrix, down_matrix, n_ctx, capacity):
    my_exp = lax.axis_index("exp")
    first = my_exp == 0
    half_d = normed.shape[1] // 2
    my_cols, other_cols = halves(normed, first, 1)
    tokens_cols = join(my_cols, exp_swap(other_cols), first, 0)
    tok_count = tokens_cols.shape[0]
    my_ctx = lax.axis_index("ctx")
    n_chip = n_ctx // 2
    my_chip = my_ctx // 2
    my_core = my_ctx % 2
    send_rows = jnp.dot(
        dispatch.astype(jnp.bfloat16),
        tokens_cols,
        preferred_element_type=jnp.float32,
    ).astype(jnp.bfloat16)
    send_rows = send_rows.reshape(2, n_chip, capacity, half_d)
    core_swap = [(i, i ^ 1) for i in range(n_ctx)]
    from_partner = lax.ppermute(send_rows[1], "ctx", perm=core_swap)
    pairs = jnp.stack([send_rows[0], from_partner], axis=1)
    arrived = [pairs[0]]
    for shift in range(1, n_chip):
        perm = [(i, ((i // 2 + shift) % n_chip) * 2 + i % 2) for i in range(n_ctx)]
        arrived.append(lax.ppermute(pairs[shift], "ctx", perm=perm))
    my_start = my_exp * half_d
    other_start = (1 - my_exp) * half_d
    gate_mine = lax.dynamic_slice_in_dim(gate_matrix, my_start, half_d, axis=0)
    gate_other = lax.dynamic_slice_in_dim(gate_matrix, other_start, half_d, axis=0)
    up_mine = lax.dynamic_slice_in_dim(up_matrix, my_start, half_d, axis=0)
    up_other = lax.dynamic_slice_in_dim(up_matrix, other_start, half_d, axis=0)
    down_other = lax.dynamic_slice_in_dim(down_matrix, other_start, half_d, axis=1)
    down_mine = lax.dynamic_slice_in_dim(down_matrix, my_start, half_d, axis=1)
    per_group = 1 if n_chip <= 4 else n_chip // 2
    n_groups = n_chip // per_group
    returned = [None] * n_chip
    for group in range(n_groups):
        shifts = range(group * per_group, (group + 1) * per_group)
        block = jnp.concatenate([arrived[k] for k in shifts], axis=0).reshape(-1, half_d)
        partner_cols = exp_swap(block)
        gate_act = jnp.dot(block, gate_mine, preferred_element_type=jnp.float32) + jnp.dot(
            partner_cols, gate_other, preferred_element_type=jnp.float32
        )
        up_act = jnp.dot(block, up_mine, preferred_element_type=jnp.float32) + jnp.dot(
            partner_cols, up_other, preferred_element_type=jnp.float32
        )
        hidden = (jax.nn.silu(gate_act) * up_act).astype(jnp.bfloat16)
        out_other = jnp.dot(hidden, down_other, preferred_element_type=jnp.float32)
        got_other = exp_swap(out_other.astype(jnp.bfloat16))
        out_mine = jnp.dot(hidden, down_mine, preferred_element_type=jnp.float32)
        summed = (out_mine + got_other.astype(jnp.float32)).astype(jnp.bfloat16)
        summed = summed.reshape(per_group, 2, capacity, half_d)
        for idx, shift in enumerate(shifts):
            if shift == 0:
                returned[shift] = summed[idx]
            else:
                perm = [(i, ((i // 2 - shift) % n_chip) * 2 + i % 2) for i in range(n_ctx)]
                returned[shift] = lax.ppermute(summed[idx], "ctx", perm=perm)
    back = jnp.stack(returned)
    partner_res = lax.ppermute(back[:, 1], "ctx", perm=core_swap)
    served = jnp.stack([back[:, 0], partner_res]).reshape(n_ctx * capacity, half_d)
    moe_half = jnp.dot(
        combine,
        served.astype(jnp.float32),
        precision=lax.Precision.HIGHEST,
        preferred_element_type=jnp.float32,
    )
    my_tok, other_tok = halves(moe_half, first, 0)
    got_tok = exp_swap(other_tok.astype(jnp.bfloat16)).astype(jnp.float32)
    return join(my_tok, got_tok, first, 1)


def ctx_gather_blocks(rows, n_ctx, my_ctx):
    n_chip = n_ctx // 2
    my_chip = my_ctx // 2
    my_core = my_ctx % 2
    stack = [rows]
    for shift in range(1, n_chip):
        perm = [(i, ((i // 2 + shift) % n_chip) * 2 + i % 2) for i in range(n_ctx)]
        stack.append(lax.ppermute(rows, "ctx", perm=perm))
    own = jnp.stack(stack)
    partner = lax.ppermute(own, "ctx", perm=[(i, i ^ 1) for i in range(n_ctx)])
    shifts = jnp.arange(n_chip, dtype=jnp.int32)
    chips = (my_chip - shifts) % n_chip
    src_ctx = jnp.concatenate([chips * 2 + my_core, chips * 2 + (1 - my_core)])
    return jnp.concatenate([own, partner]), src_ctx


def gather_out_weight(weight_rows, n_ctx, my_ctx):
    if n_ctx % 2:
        return lax.all_gather(weight_rows, "ctx", axis=0, tiled=True)
    blocks, _ = ctx_gather_blocks(weight_rows, n_ctx, my_ctx)
    n_chip = n_ctx // 2
    ctx_ids = jnp.arange(n_ctx, dtype=jnp.int32)
    other_core = (ctx_ids % 2 != my_ctx % 2).astype(jnp.int32)
    block_of = other_core * n_chip + (my_ctx // 2 - ctx_ids // 2) % n_chip
    return jnp.take(blocks, block_of, axis=0).reshape(n_ctx * weight_rows.shape[0], -1)


def local(
    query_states,
    key_states,
    value_states,
    residual,
    out_weight,
    norm_gain,
    gate_weight,
    up_weight,
    down_weight,
    routes,
    route_weights,
    prompt_lengths,
):
    n_ctx = lax.axis_size("ctx")
    my_ctx = lax.axis_index("ctx")
    tok_here = query_states.shape[1]
    feat_width = query_states.shape[2]
    heads_dev = feat_width // HD
    half_block = tok_here // 2
    score_scale = HD ** (-0.5)
    length = prompt_lengths[0]
    local_ids = jnp.arange(tok_here, dtype=jnp.int32)
    query_pos = row_positions(my_ctx * tok_here + local_ids, half_block, n_ctx)
    decode_pos = my_ctx * tok_here + local_ids
    query_three = query_states[0].reshape(tok_here, heads_dev, HD)
    run_max = jnp.full((heads_dev, tok_here), NEG, jnp.float32)
    kv_here = jnp.concatenate([key_states[0], value_states[0]], axis=1)
    kv_blocks, src_ctx = ctx_gather_blocks(kv_here, n_ctx, my_ctx)
    kv_blocks, weight_after = lax.optimization_barrier((kv_blocks, out_weight))
    kv_all = kv_blocks.reshape(n_ctx * tok_here, 2 * feat_width)
    key_two = kv_all[:, :feat_width]
    value_two = kv_all[:, feat_width:]
    row_count = key_two.shape[0]
    row_ids = (src_ctx[:, None] * tok_here + local_ids[None, :]).reshape(row_count)
    key_pos = row_positions(row_ids, half_block, n_ctx)
    pick_rows = (decode_pos[:, None] == key_pos[None, :]).astype(jnp.bfloat16)
    kept_keys = jnp.dot(pick_rows, key_two, preferred_element_type=jnp.float32)
    kept_values = jnp.dot(pick_rows, value_two, preferred_element_type=jnp.float32)
    old_max = run_max
    key_heads = key_two.reshape(row_count, heads_dev, HD)
    value_heads = value_two.reshape(row_count, heads_dev, HD)
    logits = (
        jnp.einsum("qhd,khd->hqk", query_three, key_heads, preferred_element_type=jnp.float32)
        * score_scale
    )
    visible = (key_pos[None, :] <= query_pos[:, None]) & (key_pos[None, :] < length)
    logits = jnp.where(visible[None], logits, NEG)
    new_max = jnp.maximum(old_max, jnp.max(logits, axis=2))
    weights = jnp.where(visible[None], jnp.exp(logits - new_max[:, :, None]), 0.0)
    new_sum = jnp.sum(weights, axis=2)
    gained = jnp.einsum(
        "hqk,khd->hqd",
        weights.astype(jnp.bfloat16),
        value_heads,
        preferred_element_type=jnp.float32,
    )
    inner_state = (new_max, new_sum, gained)
    run_max, run_sum, run_out, kept_keys, kept_values = inner_state + (kept_keys, kept_values)
    mixed = (run_out / run_sum[:, :, None]).astype(jnp.bfloat16)
    mixed = jnp.transpose(mixed, (1, 0, 2)).reshape(tok_here, feat_width)
    out_parts = jnp.einsum(
        "tc,oc->to",
        mixed,
        gather_out_weight(weight_after, n_ctx, my_ctx),
        preferred_element_type=jnp.float32,
    )
    head_total = exp_reduce_rows(out_parts)
    stream = (residual[0].astype(jnp.float32) + head_total).astype(jnp.bfloat16)
    stream_f = stream.astype(jnp.float32)
    mean_sq = jnp.mean(stream_f * stream_f, axis=1, keepdims=True)
    normed = (stream_f * lax.rsqrt(mean_sq + EPS) * norm_gain).astype(jnp.bfloat16)
    capacity = min(tok_here, 2 * max(1, 3 * tok_here * TOP // (4 * n_ctx)))
    if lax.axis_size("exp") == 2:
        n_chip = n_ctx // 2

        def block_of(expert):
            other_core = (expert % 2 != my_ctx % 2).astype(jnp.int32)
            return other_core * n_chip + (expert // 2 - my_ctx // 2) % n_chip

        dispatch, combine = slot_tables(routes[0], route_weights[0], n_ctx, capacity, block_of)
        moe_rows = moe_column_halves(
            normed, dispatch, combine, gate_weight[0], up_weight[0], down_weight[0], n_ctx, capacity
        )
    else:
        dispatch, combine = slot_tables(routes[0], route_weights[0], n_ctx, capacity)
        moe_rows = moe_whole_rows(
            normed, dispatch, combine, gate_weight[0], up_weight[0], down_weight[0], n_ctx, capacity
        )
    layer_out = (stream.astype(jnp.float32) + moe_rows).astype(jnp.bfloat16)
    return (
        layer_out[None],
        kept_keys.astype(jnp.bfloat16)[None],
        kept_values.astype(jnp.bfloat16)[None],
    )


def solution(mesh):
    return jax.shard_map(
        local,
        mesh=mesh,
        in_specs=(
            P("req", "ctx", "exp"),
            P("req", "ctx", "exp"),
            P("req", "ctx", "exp"),
            P("req", ("ctx", "exp"), None),
            P("ctx", "exp"),
            P(),
            P("ctx", None, "exp"),
            P("ctx", None, "exp"),
            P("ctx", "exp", None),
            P("req", "ctx", None),
            P("req", "ctx", None),
            P("req"),
        ),
        out_specs=(P("req", ("ctx", "exp"), None), P("req", "ctx", "exp"), P("req", "ctx", "exp")),
        check_vma=False,
    )
```

```python
import jax
import jax.numpy as jnp
from jax import lax
from jax.sharding import PartitionSpec as P

D = 2048
HD = 128
TOP = 4


EPS = 1e-06
NEG = -1e30


def row_positions(row_ids, half_block, n_groups):
    block_ids = row_ids // half_block
    device = block_ids // 2
    target = jnp.where(block_ids % 2 == 0, device, 2 * n_groups - 1 - device)
    return target * half_block + row_ids % half_block


def slot_tables(route_block, weight_block, experts, capacity, block_of=None):
    tok_here, top_here = route_block.shape
    flat_ids = route_block.reshape(tok_here * top_here)
    hit_table = (flat_ids[:, None] == jnp.arange(experts, dtype=jnp.int32)[None, :]).astype(
        jnp.int32
    )
    before = jnp.cumsum(hit_table, axis=0) - hit_table
    slot_rank = jnp.sum(before * hit_table, axis=1)
    blocks = flat_ids if block_of is None else block_of(flat_ids)
    slot_index = blocks * capacity + slot_rank
    slot_match = (
        jnp.arange(experts * capacity, dtype=jnp.int32)[:, None] == slot_index[None, :]
    ).astype(jnp.float32)
    slot_match = slot_match.reshape(experts * capacity, tok_here, top_here)
    dispatch = jnp.sum(slot_match, axis=2)
    combine = jnp.transpose(jnp.sum(slot_match * weight_block[None, :, :], axis=2))
    return (dispatch, combine)


def expert_ffn(token_rows, gate_matrix, up_matrix, down_matrix):
    gate_act = jnp.dot(token_rows, gate_matrix, preferred_element_type=jnp.float32)
    up_act = jnp.dot(token_rows, up_matrix, preferred_element_type=jnp.float32)
    hidden = (jax.nn.silu(gate_act) * up_act).astype(jnp.bfloat16)
    return jnp.dot(hidden, down_matrix, preferred_element_type=jnp.float32)


def exp_swap(x):
    return lax.ppermute(x, "exp", perm=[(0, 1), (1, 0)])


def exp_reduce_rows(parts):
    if lax.axis_size("exp") != 2:
        return lax.psum_scatter(
            parts.astype(jnp.bfloat16), "exp", scatter_dimension=0, tiled=True
        ).astype(jnp.float32)
    half = parts.shape[0] // 2
    first = lax.axis_index("exp") == 0
    lower = parts[:half]
    upper = parts[half:]
    mine = jnp.where(first, lower, upper)
    theirs = jnp.where(first, upper, lower)
    got = exp_swap(theirs.astype(jnp.bfloat16))
    return mine + got.astype(jnp.float32)


def exp_gather_rows(rows):
    if lax.axis_size("exp") != 2:
        return lax.all_gather(rows, "exp", axis=0, tiled=True)
    got = exp_swap(rows)
    first = lax.axis_index("exp") == 0
    return jnp.where(
        first, jnp.concatenate([rows, got], axis=0), jnp.concatenate([got, rows], axis=0)
    )


def moe_whole_rows(normed, dispatch, combine, gate_matrix, up_matrix, down_matrix, n_ctx, capacity):
    all_normed = lax.all_gather(normed, "exp", axis=0, tiled=True)
    send_rows = jnp.dot(
        dispatch.astype(jnp.bfloat16), all_normed, preferred_element_type=jnp.float32
    ).astype(jnp.bfloat16)
    send_rows = send_rows.reshape(n_ctx, capacity, D)
    arrived = lax.all_to_all(send_rows, "ctx", split_axis=0, concat_axis=0, tiled=True)
    flat_rows = arrived.reshape(n_ctx * capacity, D)
    produced = expert_ffn(flat_rows, gate_matrix, up_matrix, down_matrix).reshape(
        n_ctx, capacity, D
    )
    served = lax.all_to_all(
        produced.astype(jnp.bfloat16), "ctx", split_axis=0, concat_axis=0, tiled=True
    )
    results = served.reshape(n_ctx * capacity, D).astype(jnp.float32)
    moe_part = jnp.dot(
        combine, results, precision=lax.Precision.HIGHEST, preferred_element_type=jnp.float32
    )
    return lax.psum_scatter(
        moe_part.astype(jnp.bfloat16), "exp", scatter_dimension=0, tiled=True
    ).astype(jnp.float32)


def halves(x, first, axis):
    size = x.shape[axis] // 2
    lower = lax.slice_in_dim(x, 0, size, axis=axis)
    upper = lax.slice_in_dim(x, size, 2 * size, axis=axis)
    return jnp.where(first, lower, upper), jnp.where(first, upper, lower)


def join(mine, theirs, first, axis):
    return jnp.where(
        first,
        jnp.concatenate([mine, theirs], axis=axis),
        jnp.concatenate([theirs, mine], axis=axis),
    )


def moe_column_halves(normed, dispatch, combine, gate_matrix, up_matrix, down_matrix, n_ctx, capacity):
    my_exp = lax.axis_index("exp")
    first = my_exp == 0
    half_d = normed.shape[1] // 2
    tokens_cols = halves(normed, first, 1)[0]
    tok_count = tokens_cols.shape[0]
    my_ctx = lax.axis_index("ctx")
    n_chip = n_ctx // 2
    my_chip = my_ctx // 2
    my_core = my_ctx % 2
    send_rows = jnp.dot(
        dispatch.astype(jnp.bfloat16),
        tokens_cols,
        preferred_element_type=jnp.float32,
    ).astype(jnp.bfloat16)
    send_rows = send_rows.reshape(2, n_chip, capacity, half_d)
    core_swap = [(i, i ^ 1) for i in range(n_ctx)]
    from_partner = lax.ppermute(send_rows[1], "ctx", perm=core_swap)
    pairs = jnp.stack([send_rows[0], from_partner], axis=1)
    arrived = [pairs[0]]
    for shift in range(1, n_chip):
        perm = [(i, ((i // 2 + shift) % n_chip) * 2 + i % 2) for i in range(n_ctx)]
        arrived.append(lax.ppermute(pairs[shift], "ctx", perm=perm))
    my_start = my_exp * half_d
    other_start = (1 - my_exp) * half_d
    gate_mine = lax.dynamic_slice_in_dim(gate_matrix, my_start, half_d, axis=0)
    gate_other = lax.dynamic_slice_in_dim(gate_matrix, other_start, half_d, axis=0)
    up_mine = lax.dynamic_slice_in_dim(up_matrix, my_start, half_d, axis=0)
    up_other = lax.dynamic_slice_in_dim(up_matrix, other_start, half_d, axis=0)
    down_other = lax.dynamic_slice_in_dim(down_matrix, other_start, half_d, axis=1)
    down_mine = lax.dynamic_slice_in_dim(down_matrix, my_start, half_d, axis=1)
    per_group = 1 if n_chip <= 4 else n_chip // 2
    n_groups = n_chip // per_group
    returned = [None] * n_chip
    for group in range(n_groups):
        shifts = range(group * per_group, (group + 1) * per_group)
        block = jnp.concatenate([arrived[k] for k in shifts], axis=0).reshape(-1, half_d)
        partner_cols = exp_swap(block)
        gate_act = jnp.dot(block, gate_mine, preferred_element_type=jnp.float32) + jnp.dot(
            partner_cols, gate_other, preferred_element_type=jnp.float32
        )
        up_act = jnp.dot(block, up_mine, preferred_element_type=jnp.float32) + jnp.dot(
            partner_cols, up_other, preferred_element_type=jnp.float32
        )
        hidden = (jax.nn.silu(gate_act) * up_act).astype(jnp.bfloat16)
        out_other = jnp.dot(hidden, down_other, preferred_element_type=jnp.float32)
        got_other = exp_swap(out_other.astype(jnp.bfloat16))
        out_mine = jnp.dot(hidden, down_mine, preferred_element_type=jnp.float32)
        summed = (out_mine + got_other.astype(jnp.float32)).astype(jnp.bfloat16)
        summed = summed.reshape(per_group, 2, capacity, half_d)
        for idx, shift in enumerate(shifts):
            if shift == 0:
                returned[shift] = summed[idx]
            else:
                perm = [(i, ((i // 2 - shift) % n_chip) * 2 + i % 2) for i in range(n_ctx)]
                returned[shift] = lax.ppermute(summed[idx], "ctx", perm=perm)
    back = jnp.stack(returned)
    partner_res = lax.ppermute(back[:, 1], "ctx", perm=core_swap)
    served = jnp.stack([back[:, 0], partner_res]).reshape(n_ctx * capacity, half_d)
    moe_half = jnp.dot(
        combine,
        served.astype(jnp.float32),
        precision=lax.Precision.HIGHEST,
        preferred_element_type=jnp.float32,
    )
    my_tok, other_tok = halves(moe_half, first, 0)
    got_tok = exp_swap(other_tok.astype(jnp.bfloat16)).astype(jnp.float32)
    return join(my_tok, got_tok, first, 1)


def ctx_gather_blocks(rows, n_ctx, my_ctx):
    n_chip = n_ctx // 2
    my_chip = my_ctx // 2
    my_core = my_ctx % 2
    stack = [rows]
    for shift in range(1, n_chip):
        perm = [(i, ((i // 2 + shift) % n_chip) * 2 + i % 2) for i in range(n_ctx)]
        stack.append(lax.ppermute(rows, "ctx", perm=perm))
    own = jnp.stack(stack)
    partner = lax.ppermute(own, "ctx", perm=[(i, i ^ 1) for i in range(n_ctx)])
    shifts = jnp.arange(n_chip, dtype=jnp.int32)
    chips = (my_chip - shifts) % n_chip
    src_ctx = jnp.concatenate([chips * 2 + my_core, chips * 2 + (1 - my_core)])
    return jnp.concatenate([own, partner]), src_ctx


def local(
    query_states,
    key_states,
    value_states,
    residual,
    out_weight,
    norm_gain,
    gate_weight,
    up_weight,
    down_weight,
    routes,
    route_weights,
    prompt_lengths,
):
    n_ctx = lax.axis_size("ctx")
    my_ctx = lax.axis_index("ctx")
    tok_here = query_states.shape[1]
    feat_width = query_states.shape[2]
    heads_dev = feat_width // HD
    half_block = tok_here // 2
    score_scale = HD ** (-0.5)
    length = prompt_lengths[0]
    local_ids = jnp.arange(tok_here, dtype=jnp.int32)
    query_pos = row_positions(my_ctx * tok_here + local_ids, half_block, n_ctx)
    decode_pos = my_ctx * tok_here + local_ids
    query_three = query_states[0].reshape(tok_here, heads_dev, HD)
    run_max = jnp.full((heads_dev, tok_here), NEG, jnp.float32)
    kv_here = jnp.concatenate([key_states[0], value_states[0]], axis=1)
    kv_blocks, src_ctx = ctx_gather_blocks(kv_here, n_ctx, my_ctx)
    kv_all = kv_blocks.reshape(n_ctx * tok_here, 2 * feat_width)
    key_two = kv_all[:, :feat_width]
    value_two = kv_all[:, feat_width:]
    row_count = key_two.shape[0]
    row_ids = (src_ctx[:, None] * tok_here + local_ids[None, :]).reshape(row_count)
    key_pos = row_positions(row_ids, half_block, n_ctx)
    pick_rows = (decode_pos[:, None] == key_pos[None, :]).astype(jnp.bfloat16)
    kept_keys = jnp.dot(pick_rows, key_two, preferred_element_type=jnp.float32)
    kept_values = jnp.dot(pick_rows, value_two, preferred_element_type=jnp.float32)
    old_max = run_max
    key_heads = key_two.reshape(row_count, heads_dev, HD)
    value_heads = value_two.reshape(row_count, heads_dev, HD)
    logits = (
        jnp.einsum("qhd,khd->hqk", query_three, key_heads, preferred_element_type=jnp.float32)
        * score_scale
    )
    visible = (key_pos[None, :] <= query_pos[:, None]) & (key_pos[None, :] < length)
    logits = jnp.where(visible[None], logits, NEG)
    new_max = jnp.maximum(old_max, jnp.max(logits, axis=2))
    weights = jnp.where(visible[None], jnp.exp(logits - new_max[:, :, None]), 0.0)
    new_sum = jnp.sum(weights, axis=2)
    gained = jnp.einsum(
        "hqk,khd->hqd",
        weights.astype(jnp.bfloat16),
        value_heads,
        preferred_element_type=jnp.float32,
    )
    inner_state = (new_max, new_sum, gained)
    run_max, run_sum, run_out, kept_keys, kept_values = inner_state + (kept_keys, kept_values)
    mixed = (run_out / run_sum[:, :, None]).astype(jnp.bfloat16)
    mixed = jnp.transpose(mixed, (1, 0, 2)).reshape(tok_here, feat_width)
    out_parts = jnp.einsum(
        "tc,oc->to",
        mixed,
        lax.all_gather(out_weight, "ctx", axis=0, tiled=True),
        preferred_element_type=jnp.float32,
    )
    if lax.axis_size("exp") == 2:
        first_exp = lax.axis_index("exp") == 0
        residual_all = join(residual[0], exp_swap(residual[0]), first_exp, 0)
        head_all = out_parts + exp_swap(out_parts.astype(jnp.bfloat16)).astype(jnp.float32)
        stream_all = (residual_all.astype(jnp.float32) + head_all).astype(jnp.bfloat16)
        stream = halves(stream_all, first_exp, 0)[0]
        stream_f = stream_all.astype(jnp.float32)
    else:
        head_total = exp_reduce_rows(out_parts)
        stream = (residual[0].astype(jnp.float32) + head_total).astype(jnp.bfloat16)
        stream_f = stream.astype(jnp.float32)
    mean_sq = jnp.mean(stream_f * stream_f, axis=1, keepdims=True)
    normed = (stream_f * lax.rsqrt(mean_sq + EPS) * norm_gain).astype(jnp.bfloat16)
    capacity = min(tok_here, 2 * max(1, 3 * tok_here * TOP // (4 * n_ctx)))
    if lax.axis_size("exp") == 2:
        n_chip = n_ctx // 2

        def block_of(expert):
            other_core = (expert % 2 != my_ctx % 2).astype(jnp.int32)
            return other_core * n_chip + (expert // 2 - my_ctx // 2) % n_chip

        dispatch, combine = slot_tables(routes[0], route_weights[0], n_ctx, capacity, block_of)
        moe_rows = moe_column_halves(
            normed, dispatch, combine, gate_weight[0], up_weight[0], down_weight[0], n_ctx, capacity
        )
    else:
        dispatch, combine = slot_tables(routes[0], route_weights[0], n_ctx, capacity)
        moe_rows = moe_whole_rows(
            normed, dispatch, combine, gate_weight[0], up_weight[0], down_weight[0], n_ctx, capacity
        )
    layer_out = (stream.astype(jnp.float32) + moe_rows).astype(jnp.bfloat16)
    return (
        layer_out[None],
        kept_keys.astype(jnp.bfloat16)[None],
        kept_values.astype(jnp.bfloat16)[None],
    )


def solution(mesh):
    return jax.shard_map(
        local,
        mesh=mesh,
        in_specs=(
            P("req", "ctx", "exp"),
            P("req", "ctx", "exp"),
            P("req", "ctx", "exp"),
            P("req", ("ctx", "exp"), None),
            P("ctx", "exp"),
            P(),
            P("ctx", None, "exp"),
            P("ctx", None, "exp"),
            P("ctx", "exp", None),
            P("req", "ctx", None),
            P("req", "ctx", None),
            P("req"),
        ),
        out_specs=(P("req", ("ctx", "exp"), None), P("req", "ctx", "exp"), P("req", "ctx", "exp")),
        check_vma=False,
    )
```

```python
import jax
import jax.numpy as jnp
from jax import lax
from jax.sharding import PartitionSpec as P

D = 2048
HD = 128
TOP = 4


EPS = 1e-06
NEG = -1e30


def row_positions(row_ids, half_block, n_groups):
    block_ids = row_ids // half_block
    device = block_ids // 2
    target = jnp.where(block_ids % 2 == 0, device, 2 * n_groups - 1 - device)
    return target * half_block + row_ids % half_block


def slot_tables(route_block, weight_block, experts, capacity, block_of=None):
    tok_here, top_here = route_block.shape
    flat_ids = route_block.reshape(tok_here * top_here)
    hit_table = (flat_ids[:, None] == jnp.arange(experts, dtype=jnp.int32)[None, :]).astype(
        jnp.int32
    )
    before = jnp.cumsum(hit_table, axis=0) - hit_table
    slot_rank = jnp.sum(before * hit_table, axis=1)
    blocks = flat_ids if block_of is None else block_of(flat_ids)
    slot_index = blocks * capacity + slot_rank
    slot_match = (
        jnp.arange(experts * capacity, dtype=jnp.int32)[:, None] == slot_index[None, :]
    ).astype(jnp.float32)
    slot_match = slot_match.reshape(experts * capacity, tok_here, top_here)
    dispatch = jnp.sum(slot_match, axis=2)
    combine = jnp.transpose(jnp.sum(slot_match * weight_block[None, :, :], axis=2))
    return (dispatch, combine)


def expert_ffn(token_rows, gate_matrix, up_matrix, down_matrix):
    gate_act = jnp.dot(token_rows, gate_matrix, preferred_element_type=jnp.float32)
    up_act = jnp.dot(token_rows, up_matrix, preferred_element_type=jnp.float32)
    hidden = (jax.nn.silu(gate_act) * up_act).astype(jnp.bfloat16)
    return jnp.dot(hidden, down_matrix, preferred_element_type=jnp.float32)


def exp_swap(x):
    return lax.ppermute(x, "exp", perm=[(0, 1), (1, 0)])


def exp_reduce_rows(parts):
    if lax.axis_size("exp") != 2:
        return lax.psum_scatter(
            parts.astype(jnp.bfloat16), "exp", scatter_dimension=0, tiled=True
        ).astype(jnp.float32)
    half = parts.shape[0] // 2
    first = lax.axis_index("exp") == 0
    lower = parts[:half]
    upper = parts[half:]
    mine = jnp.where(first, lower, upper)
    theirs = jnp.where(first, upper, lower)
    got = exp_swap(theirs.astype(jnp.bfloat16))
    return mine + got.astype(jnp.float32)


def exp_gather_rows(rows):
    if lax.axis_size("exp") != 2:
        return lax.all_gather(rows, "exp", axis=0, tiled=True)
    got = exp_swap(rows)
    first = lax.axis_index("exp") == 0
    return jnp.where(
        first, jnp.concatenate([rows, got], axis=0), jnp.concatenate([got, rows], axis=0)
    )


def moe_whole_rows(normed, dispatch, combine, gate_matrix, up_matrix, down_matrix, n_ctx, capacity):
    all_normed = lax.all_gather(normed, "exp", axis=0, tiled=True)
    send_rows = jnp.dot(
        dispatch.astype(jnp.bfloat16), all_normed, preferred_element_type=jnp.float32
    ).astype(jnp.bfloat16)
    send_rows = send_rows.reshape(n_ctx, capacity, D)
    arrived = lax.all_to_all(send_rows, "ctx", split_axis=0, concat_axis=0, tiled=True)
    flat_rows = arrived.reshape(n_ctx * capacity, D)
    produced = expert_ffn(flat_rows, gate_matrix, up_matrix, down_matrix).reshape(
        n_ctx, capacity, D
    )
    served = lax.all_to_all(
        produced.astype(jnp.bfloat16), "ctx", split_axis=0, concat_axis=0, tiled=True
    )
    results = served.reshape(n_ctx * capacity, D).astype(jnp.float32)
    moe_part = jnp.dot(
        combine, results, precision=lax.Precision.HIGHEST, preferred_element_type=jnp.float32
    )
    return lax.psum_scatter(
        moe_part.astype(jnp.bfloat16), "exp", scatter_dimension=0, tiled=True
    ).astype(jnp.float32)


def halves(x, first, axis):
    size = x.shape[axis] // 2
    lower = lax.slice_in_dim(x, 0, size, axis=axis)
    upper = lax.slice_in_dim(x, size, 2 * size, axis=axis)
    return jnp.where(first, lower, upper), jnp.where(first, upper, lower)


def join(mine, theirs, first, axis):
    return jnp.where(
        first,
        jnp.concatenate([mine, theirs], axis=axis),
        jnp.concatenate([theirs, mine], axis=axis),
    )


def moe_column_halves(normed, dispatch, combine, gate_matrix, up_matrix, down_matrix, n_ctx, capacity):
    my_exp = lax.axis_index("exp")
    first = my_exp == 0
    half_d = normed.shape[1] // 2
    tokens_cols = halves(normed, first, 1)[0]
    tok_count = tokens_cols.shape[0]
    my_ctx = lax.axis_index("ctx")
    n_chip = n_ctx // 2
    my_chip = my_ctx // 2
    my_core = my_ctx % 2
    send_rows = jnp.dot(
        dispatch.astype(jnp.bfloat16),
        tokens_cols,
        preferred_element_type=jnp.float32,
    ).astype(jnp.bfloat16)
    send_rows = send_rows.reshape(2, n_chip, capacity, half_d)
    core_swap = [(i, i ^ 1) for i in range(n_ctx)]
    from_partner = lax.ppermute(send_rows[1], "ctx", perm=core_swap)
    pairs = jnp.stack([send_rows[0], from_partner], axis=1)
    arrived = [pairs[0]]
    for shift in range(1, n_chip):
        perm = [(i, ((i // 2 + shift) % n_chip) * 2 + i % 2) for i in range(n_ctx)]
        arrived.append(lax.ppermute(pairs[shift], "ctx", perm=perm))
    my_start = my_exp * half_d
    other_start = (1 - my_exp) * half_d
    gate_mine = lax.dynamic_slice_in_dim(gate_matrix, my_start, half_d, axis=0)
    gate_other = lax.dynamic_slice_in_dim(gate_matrix, other_start, half_d, axis=0)
    up_mine = lax.dynamic_slice_in_dim(up_matrix, my_start, half_d, axis=0)
    up_other = lax.dynamic_slice_in_dim(up_matrix, other_start, half_d, axis=0)
    down_other = lax.dynamic_slice_in_dim(down_matrix, other_start, half_d, axis=1)
    down_mine = lax.dynamic_slice_in_dim(down_matrix, my_start, half_d, axis=1)
    per_group = 1 if n_chip <= 4 else n_chip // 2
    n_groups = n_chip // per_group
    returned = [None] * n_chip
    split_cores = n_chip <= 4
    for group in range(n_groups):
        shifts = range(group * per_group, (group + 1) * per_group)
        if split_cores:
            pieces = [arrived[k][side] for k in shifts for side in range(2)]
        else:
            pieces = [jnp.concatenate([arrived[k] for k in shifts], axis=0).reshape(-1, half_d)]
        outs = []
        for block in pieces:
            partner_cols = exp_swap(block)
            gate_act = jnp.dot(block, gate_mine, preferred_element_type=jnp.float32) + jnp.dot(
                partner_cols, gate_other, preferred_element_type=jnp.float32
            )
            up_act = jnp.dot(block, up_mine, preferred_element_type=jnp.float32) + jnp.dot(
                partner_cols, up_other, preferred_element_type=jnp.float32
            )
            hidden = (jax.nn.silu(gate_act) * up_act).astype(jnp.bfloat16)
            out_other = jnp.dot(hidden, down_other, preferred_element_type=jnp.float32)
            got_other = exp_swap(out_other.astype(jnp.bfloat16))
            out_mine = jnp.dot(hidden, down_mine, preferred_element_type=jnp.float32)
            outs.append((out_mine + got_other.astype(jnp.float32)).astype(jnp.bfloat16))
        summed = jnp.concatenate(outs, axis=0).reshape(per_group, 2, capacity, half_d)
        for idx, shift in enumerate(shifts):
            if shift == 0:
                returned[shift] = summed[idx]
            else:
                perm = [(i, ((i // 2 - shift) % n_chip) * 2 + i % 2) for i in range(n_ctx)]
                returned[shift] = lax.ppermute(summed[idx], "ctx", perm=perm)
    back = jnp.stack(returned)
    partner_res = lax.ppermute(back[:, 1], "ctx", perm=core_swap)
    served = jnp.stack([back[:, 0], partner_res]).reshape(n_ctx * capacity, half_d)
    moe_half = jnp.dot(
        combine,
        served.astype(jnp.float32),
        precision=lax.Precision.HIGHEST,
        preferred_element_type=jnp.float32,
    )
    my_tok, other_tok = halves(moe_half, first, 0)
    got_tok = exp_swap(other_tok.astype(jnp.bfloat16)).astype(jnp.float32)
    return join(my_tok, got_tok, first, 1)


def ctx_gather_blocks(rows, n_ctx, my_ctx):
    n_chip = n_ctx // 2
    my_chip = my_ctx // 2
    my_core = my_ctx % 2
    stack = [rows]
    for shift in range(1, n_chip):
        perm = [(i, ((i // 2 + shift) % n_chip) * 2 + i % 2) for i in range(n_ctx)]
        stack.append(lax.ppermute(rows, "ctx", perm=perm))
    own = jnp.stack(stack)
    partner = lax.ppermute(own, "ctx", perm=[(i, i ^ 1) for i in range(n_ctx)])
    shifts = jnp.arange(n_chip, dtype=jnp.int32)
    chips = (my_chip - shifts) % n_chip
    src_ctx = jnp.concatenate([chips * 2 + my_core, chips * 2 + (1 - my_core)])
    return jnp.concatenate([own, partner]), src_ctx


def local(
    query_states,
    key_states,
    value_states,
    residual,
    out_weight,
    norm_gain,
    gate_weight,
    up_weight,
    down_weight,
    routes,
    route_weights,
    prompt_lengths,
):
    n_ctx = lax.axis_size("ctx")
    my_ctx = lax.axis_index("ctx")
    tok_here = query_states.shape[1]
    feat_width = query_states.shape[2]
    heads_dev = feat_width // HD
    half_block = tok_here // 2
    score_scale = HD ** (-0.5)
    length = prompt_lengths[0]
    local_ids = jnp.arange(tok_here, dtype=jnp.int32)
    query_pos = row_positions(my_ctx * tok_here + local_ids, half_block, n_ctx)
    decode_pos = my_ctx * tok_here + local_ids
    query_three = query_states[0].reshape(tok_here, heads_dev, HD)
    run_max = jnp.full((heads_dev, tok_here), NEG, jnp.float32)
    kv_here = jnp.concatenate([key_states[0], value_states[0]], axis=1)
    kv_blocks, src_ctx = ctx_gather_blocks(kv_here, n_ctx, my_ctx)
    kv_all = kv_blocks.reshape(n_ctx * tok_here, 2 * feat_width)
    key_two = kv_all[:, :feat_width]
    value_two = kv_all[:, feat_width:]
    row_count = key_two.shape[0]
    row_ids = (src_ctx[:, None] * tok_here + local_ids[None, :]).reshape(row_count)
    key_pos = row_positions(row_ids, half_block, n_ctx)
    pick_rows = (decode_pos[:, None] == key_pos[None, :]).astype(jnp.bfloat16)
    kept_keys = jnp.dot(pick_rows, key_two, preferred_element_type=jnp.float32)
    kept_values = jnp.dot(pick_rows, value_two, preferred_element_type=jnp.float32)
    old_max = run_max
    key_heads = key_two.reshape(row_count, heads_dev, HD)
    value_heads = value_two.reshape(row_count, heads_dev, HD)
    logits = (
        jnp.einsum("qhd,khd->hqk", query_three, key_heads, preferred_element_type=jnp.float32)
        * score_scale
    )
    visible = (key_pos[None, :] <= query_pos[:, None]) & (key_pos[None, :] < length)
    logits = jnp.where(visible[None], logits, NEG)
    new_max = jnp.maximum(old_max, jnp.max(logits, axis=2))
    weights = jnp.where(visible[None], jnp.exp(logits - new_max[:, :, None]), 0.0)
    new_sum = jnp.sum(weights, axis=2)
    gained = jnp.einsum(
        "hqk,khd->hqd",
        weights.astype(jnp.bfloat16),
        value_heads,
        preferred_element_type=jnp.float32,
    )
    inner_state = (new_max, new_sum, gained)
    run_max, run_sum, run_out, kept_keys, kept_values = inner_state + (kept_keys, kept_values)
    mixed = (run_out / run_sum[:, :, None]).astype(jnp.bfloat16)
    mixed = jnp.transpose(mixed, (1, 0, 2)).reshape(tok_here, feat_width)
    out_parts = jnp.einsum(
        "tc,oc->to",
        mixed,
        lax.all_gather(out_weight, "ctx", axis=0, tiled=True),
        preferred_element_type=jnp.float32,
    )
    if lax.axis_size("exp") == 2:
        first_exp = lax.axis_index("exp") == 0
        residual_all = join(residual[0], exp_swap(residual[0]), first_exp, 0)
        head_all = out_parts + exp_swap(out_parts.astype(jnp.bfloat16)).astype(jnp.float32)
        stream_all = (residual_all.astype(jnp.float32) + head_all).astype(jnp.bfloat16)
        stream = halves(stream_all, first_exp, 0)[0]
        stream_f = stream_all.astype(jnp.float32)
    else:
        head_total = exp_reduce_rows(out_parts)
        stream = (residual[0].astype(jnp.float32) + head_total).astype(jnp.bfloat16)
        stream_f = stream.astype(jnp.float32)
    mean_sq = jnp.mean(stream_f * stream_f, axis=1, keepdims=True)
    normed = (stream_f * lax.rsqrt(mean_sq + EPS) * norm_gain).astype(jnp.bfloat16)
    capacity = min(tok_here, 2 * max(1, 3 * tok_here * TOP // (4 * n_ctx)))
    if lax.axis_size("exp") == 2:
        n_chip = n_ctx // 2

        def block_of(expert):
            other_core = (expert % 2 != my_ctx % 2).astype(jnp.int32)
            return other_core * n_chip + (expert // 2 - my_ctx // 2) % n_chip

        dispatch, combine = slot_tables(routes[0], route_weights[0], n_ctx, capacity, block_of)
        moe_rows = moe_column_halves(
            normed, dispatch, combine, gate_weight[0], up_weight[0], down_weight[0], n_ctx, capacity
        )
    else:
        dispatch, combine = slot_tables(routes[0], route_weights[0], n_ctx, capacity)
        moe_rows = moe_whole_rows(
            normed, dispatch, combine, gate_weight[0], up_weight[0], down_weight[0], n_ctx, capacity
        )
    layer_out = (stream.astype(jnp.float32) + moe_rows).astype(jnp.bfloat16)
    return (
        layer_out[None],
        kept_keys.astype(jnp.bfloat16)[None],
        kept_values.astype(jnp.bfloat16)[None],
    )


def solution(mesh):
    return jax.shard_map(
        local,
        mesh=mesh,
        in_specs=(
            P("req", "ctx", "exp"),
            P("req", "ctx", "exp"),
            P("req", "ctx", "exp"),
            P("req", ("ctx", "exp"), None),
            P("ctx", "exp"),
            P(),
            P("ctx", None, "exp"),
            P("ctx", None, "exp"),
            P("ctx", "exp", None),
            P("req", "ctx", None),
            P("req", "ctx", None),
            P("req"),
        ),
        out_specs=(P("req", ("ctx", "exp"), None), P("req", "ctx", "exp"), P("req", "ctx", "exp")),
        check_vma=False,
    )
```

```python
import jax
import jax.numpy as jnp
from jax import lax
from jax.sharding import PartitionSpec as P

D = 2048
HD = 128
TOP = 4


EPS = 1e-06
NEG = -1e30


def row_positions(row_ids, half_block, n_groups):
    block_ids = row_ids // half_block
    device = block_ids // 2
    target = jnp.where(block_ids % 2 == 0, device, 2 * n_groups - 1 - device)
    return target * half_block + row_ids % half_block


def slot_tables(route_block, weight_block, experts, capacity, block_of=None):
    tok_here, top_here = route_block.shape
    flat_ids = route_block.reshape(tok_here * top_here)
    hit_table = (flat_ids[:, None] == jnp.arange(experts, dtype=jnp.int32)[None, :]).astype(
        jnp.int32
    )
    before = jnp.cumsum(hit_table, axis=0) - hit_table
    slot_rank = jnp.sum(before * hit_table, axis=1)
    blocks = flat_ids if block_of is None else block_of(flat_ids)
    slot_index = blocks * capacity + slot_rank
    slot_match = (
        jnp.arange(experts * capacity, dtype=jnp.int32)[:, None] == slot_index[None, :]
    ).astype(jnp.float32)
    slot_match = slot_match.reshape(experts * capacity, tok_here, top_here)
    dispatch = jnp.sum(slot_match, axis=2)
    combine = jnp.transpose(jnp.sum(slot_match * weight_block[None, :, :], axis=2))
    return (dispatch, combine)


def expert_ffn(token_rows, gate_matrix, up_matrix, down_matrix):
    gate_act = jnp.dot(token_rows, gate_matrix, preferred_element_type=jnp.float32)
    up_act = jnp.dot(token_rows, up_matrix, preferred_element_type=jnp.float32)
    hidden = (jax.nn.silu(gate_act) * up_act).astype(jnp.bfloat16)
    return jnp.dot(hidden, down_matrix, preferred_element_type=jnp.float32)


def exp_swap(x):
    return lax.ppermute(x, "exp", perm=[(0, 1), (1, 0)])


def exp_reduce_rows(parts):
    if lax.axis_size("exp") != 2:
        return lax.psum_scatter(
            parts.astype(jnp.bfloat16), "exp", scatter_dimension=0, tiled=True
        ).astype(jnp.float32)
    half = parts.shape[0] // 2
    first = lax.axis_index("exp") == 0
    lower = parts[:half]
    upper = parts[half:]
    mine = jnp.where(first, lower, upper)
    theirs = jnp.where(first, upper, lower)
    got = exp_swap(theirs.astype(jnp.bfloat16))
    return mine + got.astype(jnp.float32)


def exp_gather_rows(rows):
    if lax.axis_size("exp") != 2:
        return lax.all_gather(rows, "exp", axis=0, tiled=True)
    got = exp_swap(rows)
    first = lax.axis_index("exp") == 0
    return jnp.where(
        first, jnp.concatenate([rows, got], axis=0), jnp.concatenate([got, rows], axis=0)
    )


def moe_whole_rows(normed, dispatch, combine, gate_matrix, up_matrix, down_matrix, n_ctx, capacity):
    all_normed = lax.all_gather(normed, "exp", axis=0, tiled=True)
    send_rows = jnp.dot(
        dispatch.astype(jnp.bfloat16), all_normed, preferred_element_type=jnp.float32
    ).astype(jnp.bfloat16)
    send_rows = send_rows.reshape(n_ctx, capacity, D)
    arrived = lax.all_to_all(send_rows, "ctx", split_axis=0, concat_axis=0, tiled=True)
    flat_rows = arrived.reshape(n_ctx * capacity, D)
    produced = expert_ffn(flat_rows, gate_matrix, up_matrix, down_matrix).reshape(
        n_ctx, capacity, D
    )
    served = lax.all_to_all(
        produced.astype(jnp.bfloat16), "ctx", split_axis=0, concat_axis=0, tiled=True
    )
    results = served.reshape(n_ctx * capacity, D).astype(jnp.float32)
    moe_part = jnp.dot(
        combine, results, precision=lax.Precision.HIGHEST, preferred_element_type=jnp.float32
    )
    return lax.psum_scatter(
        moe_part.astype(jnp.bfloat16), "exp", scatter_dimension=0, tiled=True
    ).astype(jnp.float32)


def halves(x, first, axis):
    size = x.shape[axis] // 2
    lower = lax.slice_in_dim(x, 0, size, axis=axis)
    upper = lax.slice_in_dim(x, size, 2 * size, axis=axis)
    return jnp.where(first, lower, upper), jnp.where(first, upper, lower)


def join(mine, theirs, first, axis):
    return jnp.where(
        first,
        jnp.concatenate([mine, theirs], axis=axis),
        jnp.concatenate([theirs, mine], axis=axis),
    )


def moe_column_halves(normed, dispatch, combine, gate_matrix, up_matrix, down_matrix, n_ctx, capacity):
    my_exp = lax.axis_index("exp")
    first = my_exp == 0
    half_d = normed.shape[1] // 2
    tokens_cols = halves(normed, first, 1)[0]
    tok_count = tokens_cols.shape[0]
    my_ctx = lax.axis_index("ctx")
    n_chip = n_ctx // 2
    my_chip = my_ctx // 2
    my_core = my_ctx % 2
    dispatch_parts = dispatch.reshape(2, n_chip, capacity, tok_count)
    full_d = normed.shape[1]
    near = jnp.dot(
        dispatch_parts[:, 0].reshape(2 * capacity, tok_count).astype(jnp.bfloat16),
        normed,
        preferred_element_type=jnp.float32,
    ).astype(jnp.bfloat16)
    near = near.reshape(2, capacity, full_d)
    far = jnp.dot(
        dispatch_parts[:, 1:].reshape(2 * (n_chip - 1) * capacity, tok_count).astype(jnp.bfloat16),
        tokens_cols,
        preferred_element_type=jnp.float32,
    ).astype(jnp.bfloat16)
    far = far.reshape(2, n_chip - 1, capacity, half_d)
    core_swap = [(i, i ^ 1) for i in range(n_ctx)]
    near_in = jnp.concatenate(
        [near[0], lax.ppermute(near[1], "ctx", perm=core_swap)], axis=0
    )
    far_pairs = jnp.stack([far[0], lax.ppermute(far[1], "ctx", perm=core_swap)], axis=1)
    arrived = [None]
    for shift in range(1, n_chip):
        perm = [(i, ((i // 2 + shift) % n_chip) * 2 + i % 2) for i in range(n_ctx)]
        arrived.append(lax.ppermute(far_pairs[shift - 1], "ctx", perm=perm))
    my_start = my_exp * half_d
    other_start = (1 - my_exp) * half_d
    gate_mine = lax.dynamic_slice_in_dim(gate_matrix, my_start, half_d, axis=0)
    gate_other = lax.dynamic_slice_in_dim(gate_matrix, other_start, half_d, axis=0)
    up_mine = lax.dynamic_slice_in_dim(up_matrix, my_start, half_d, axis=0)
    up_other = lax.dynamic_slice_in_dim(up_matrix, other_start, half_d, axis=0)
    down_other = lax.dynamic_slice_in_dim(down_matrix, other_start, half_d, axis=1)
    down_mine = lax.dynamic_slice_in_dim(down_matrix, my_start, half_d, axis=1)
    if n_chip <= 4:
        groups = [[0]] + [[k] for k in range(1, n_chip)]
    else:
        groups = [[0], list(range(1, n_chip // 2)), list(range(n_chip // 2, n_chip))]
    returned = [None] * n_chip
    for shifts in groups:
        if shifts == [0]:
            gate_act = jnp.dot(near_in, gate_matrix, preferred_element_type=jnp.float32)
            up_act = jnp.dot(near_in, up_matrix, preferred_element_type=jnp.float32)
        else:
            block = jnp.concatenate([arrived[k] for k in shifts], axis=0).reshape(-1, half_d)
            partner_cols = exp_swap(block)
            gate_act = jnp.dot(block, gate_mine, preferred_element_type=jnp.float32) + jnp.dot(
                partner_cols, gate_other, preferred_element_type=jnp.float32
            )
            up_act = jnp.dot(block, up_mine, preferred_element_type=jnp.float32) + jnp.dot(
                partner_cols, up_other, preferred_element_type=jnp.float32
            )
        hidden = (jax.nn.silu(gate_act) * up_act).astype(jnp.bfloat16)
        out_other = jnp.dot(hidden, down_other, preferred_element_type=jnp.float32)
        got_other = exp_swap(out_other.astype(jnp.bfloat16))
        out_mine = jnp.dot(hidden, down_mine, preferred_element_type=jnp.float32)
        summed = (out_mine + got_other.astype(jnp.float32)).astype(jnp.bfloat16)
        summed = summed.reshape(len(shifts), 2, capacity, half_d)
        for idx, shift in enumerate(shifts):
            if shift == 0:
                returned[shift] = summed[idx]
            else:
                perm = [(i, ((i // 2 - shift) % n_chip) * 2 + i % 2) for i in range(n_ctx)]
                returned[shift] = lax.ppermute(summed[idx], "ctx", perm=perm)
    back = jnp.stack(returned)
    partner_res = lax.ppermute(back[:, 1], "ctx", perm=core_swap)
    served = jnp.stack([back[:, 0], partner_res]).reshape(n_ctx * capacity, half_d)
    moe_half = jnp.dot(
        combine,
        served.astype(jnp.float32),
        precision=lax.Precision.HIGHEST,
        preferred_element_type=jnp.float32,
    )
    my_tok, other_tok = halves(moe_half, first, 0)
    got_tok = exp_swap(other_tok.astype(jnp.bfloat16)).astype(jnp.float32)
    return join(my_tok, got_tok, first, 1)


def ctx_gather_blocks(rows, n_ctx, my_ctx):
    n_chip = n_ctx // 2
    my_chip = my_ctx // 2
    my_core = my_ctx % 2
    stack = [rows]
    for shift in range(1, n_chip):
        perm = [(i, ((i // 2 + shift) % n_chip) * 2 + i % 2) for i in range(n_ctx)]
        stack.append(lax.ppermute(rows, "ctx", perm=perm))
    own = jnp.stack(stack)
    partner = lax.ppermute(own, "ctx", perm=[(i, i ^ 1) for i in range(n_ctx)])
    shifts = jnp.arange(n_chip, dtype=jnp.int32)
    chips = (my_chip - shifts) % n_chip
    src_ctx = jnp.concatenate([chips * 2 + my_core, chips * 2 + (1 - my_core)])
    return jnp.concatenate([own, partner]), src_ctx


def local(
    query_states,
    key_states,
    value_states,
    residual,
    out_weight,
    norm_gain,
    gate_weight,
    up_weight,
    down_weight,
    routes,
    route_weights,
    prompt_lengths,
):
    n_ctx = lax.axis_size("ctx")
    my_ctx = lax.axis_index("ctx")
    tok_here = query_states.shape[1]
    feat_width = query_states.shape[2]
    heads_dev = feat_width // HD
    half_block = tok_here // 2
    score_scale = HD ** (-0.5)
    length = prompt_lengths[0]
    local_ids = jnp.arange(tok_here, dtype=jnp.int32)
    query_pos = row_positions(my_ctx * tok_here + local_ids, half_block, n_ctx)
    decode_pos = my_ctx * tok_here + local_ids
    query_three = query_states[0].reshape(tok_here, heads_dev, HD)
    run_max = jnp.full((heads_dev, tok_here), NEG, jnp.float32)
    kv_here = jnp.concatenate([key_states[0], value_states[0]], axis=1)
    kv_blocks, src_ctx = ctx_gather_blocks(kv_here, n_ctx, my_ctx)
    kv_all = kv_blocks.reshape(n_ctx * tok_here, 2 * feat_width)
    key_two = kv_all[:, :feat_width]
    value_two = kv_all[:, feat_width:]
    row_count = key_two.shape[0]
    row_ids = (src_ctx[:, None] * tok_here + local_ids[None, :]).reshape(row_count)
    key_pos = row_positions(row_ids, half_block, n_ctx)
    pick_rows = (decode_pos[:, None] == key_pos[None, :]).astype(jnp.bfloat16)
    kept_keys = jnp.dot(pick_rows, key_two, preferred_element_type=jnp.float32)
    kept_values = jnp.dot(pick_rows, value_two, preferred_element_type=jnp.float32)
    old_max = run_max
    key_heads = key_two.reshape(row_count, heads_dev, HD)
    value_heads = value_two.reshape(row_count, heads_dev, HD)
    logits = (
        jnp.einsum("qhd,khd->hqk", query_three, key_heads, preferred_element_type=jnp.float32)
        * score_scale
    )
    visible = (key_pos[None, :] <= query_pos[:, None]) & (key_pos[None, :] < length)
    logits = jnp.where(visible[None], logits, NEG)
    new_max = jnp.maximum(old_max, jnp.max(logits, axis=2))
    weights = jnp.where(visible[None], jnp.exp(logits - new_max[:, :, None]), 0.0)
    new_sum = jnp.sum(weights, axis=2)
    gained = jnp.einsum(
        "hqk,khd->hqd",
        weights.astype(jnp.bfloat16),
        value_heads,
        preferred_element_type=jnp.float32,
    )
    inner_state = (new_max, new_sum, gained)
    run_max, run_sum, run_out, kept_keys, kept_values = inner_state + (kept_keys, kept_values)
    mixed = (run_out / run_sum[:, :, None]).astype(jnp.bfloat16)
    mixed = jnp.transpose(mixed, (1, 0, 2)).reshape(tok_here, feat_width)
    out_parts = jnp.einsum(
        "tc,oc->to",
        mixed,
        lax.all_gather(out_weight, "ctx", axis=0, tiled=True),
        preferred_element_type=jnp.float32,
    )
    if lax.axis_size("exp") == 2:
        first_exp = lax.axis_index("exp") == 0
        residual_all = join(residual[0], exp_swap(residual[0]), first_exp, 0)
        head_all = out_parts + exp_swap(out_parts.astype(jnp.bfloat16)).astype(jnp.float32)
        stream_all = (residual_all.astype(jnp.float32) + head_all).astype(jnp.bfloat16)
        stream = halves(stream_all, first_exp, 0)[0]
        stream_f = stream_all.astype(jnp.float32)
    else:
        head_total = exp_reduce_rows(out_parts)
        stream = (residual[0].astype(jnp.float32) + head_total).astype(jnp.bfloat16)
        stream_f = stream.astype(jnp.float32)
    mean_sq = jnp.mean(stream_f * stream_f, axis=1, keepdims=True)
    normed = (stream_f * lax.rsqrt(mean_sq + EPS) * norm_gain).astype(jnp.bfloat16)
    capacity = min(tok_here, 2 * max(1, 3 * tok_here * TOP // (4 * n_ctx)))
    if lax.axis_size("exp") == 2:
        n_chip = n_ctx // 2

        def block_of(expert):
            other_core = (expert % 2 != my_ctx % 2).astype(jnp.int32)
            return other_core * n_chip + (expert // 2 - my_ctx // 2) % n_chip

        dispatch, combine = slot_tables(routes[0], route_weights[0], n_ctx, capacity, block_of)
        moe_rows = moe_column_halves(
            normed, dispatch, combine, gate_weight[0], up_weight[0], down_weight[0], n_ctx, capacity
        )
    else:
        dispatch, combine = slot_tables(routes[0], route_weights[0], n_ctx, capacity)
        moe_rows = moe_whole_rows(
            normed, dispatch, combine, gate_weight[0], up_weight[0], down_weight[0], n_ctx, capacity
        )
    layer_out = (stream.astype(jnp.float32) + moe_rows).astype(jnp.bfloat16)
    return (
        layer_out[None],
        kept_keys.astype(jnp.bfloat16)[None],
        kept_values.astype(jnp.bfloat16)[None],
    )


def solution(mesh):
    return jax.shard_map(
        local,
        mesh=mesh,
        in_specs=(
            P("req", "ctx", "exp"),
            P("req", "ctx", "exp"),
            P("req", "ctx", "exp"),
            P("req", ("ctx", "exp"), None),
            P("ctx", "exp"),
            P(),
            P("ctx", None, "exp"),
            P("ctx", None, "exp"),
            P("ctx", "exp", None),
            P("req", "ctx", None),
            P("req", "ctx", None),
            P("req"),
        ),
        out_specs=(P("req", ("ctx", "exp"), None), P("req", "ctx", "exp"), P("req", "ctx", "exp")),
        check_vma=False,
    )
```

```python
import jax
import jax.numpy as jnp
from jax import lax
from jax.sharding import PartitionSpec as P

D = 2048
HD = 128
TOP = 4


EPS = 1e-06
NEG = -1e30


def row_positions(row_ids, half_block, n_groups):
    block_ids = row_ids // half_block
    device = block_ids // 2
    target = jnp.where(block_ids % 2 == 0, device, 2 * n_groups - 1 - device)
    return target * half_block + row_ids % half_block


def slot_tables(route_block, weight_block, experts, capacity, block_of=None):
    tok_here, top_here = route_block.shape
    flat_ids = route_block.reshape(tok_here * top_here)
    hit_table = (flat_ids[:, None] == jnp.arange(experts, dtype=jnp.int32)[None, :]).astype(
        jnp.int32
    )
    before = jnp.cumsum(hit_table, axis=0) - hit_table
    slot_rank = jnp.sum(before * hit_table, axis=1)
    blocks = flat_ids if block_of is None else block_of(flat_ids)
    slot_index = blocks * capacity + slot_rank
    slot_match = (
        jnp.arange(experts * capacity, dtype=jnp.int32)[:, None] == slot_index[None, :]
    ).astype(jnp.float32)
    slot_match = slot_match.reshape(experts * capacity, tok_here, top_here)
    dispatch = jnp.sum(slot_match, axis=2)
    combine = jnp.transpose(jnp.sum(slot_match * weight_block[None, :, :], axis=2))
    return (dispatch, combine)


def expert_ffn(token_rows, gate_matrix, up_matrix, down_matrix):
    gate_act = jnp.dot(token_rows, gate_matrix, preferred_element_type=jnp.float32)
    up_act = jnp.dot(token_rows, up_matrix, preferred_element_type=jnp.float32)
    hidden = (jax.nn.silu(gate_act) * up_act).astype(jnp.bfloat16)
    return jnp.dot(hidden, down_matrix, preferred_element_type=jnp.float32)


def exp_swap(x):
    return lax.ppermute(x, "exp", perm=[(0, 1), (1, 0)])


def exp_reduce_rows(parts):
    if lax.axis_size("exp") != 2:
        return lax.psum_scatter(
            parts.astype(jnp.bfloat16), "exp", scatter_dimension=0, tiled=True
        ).astype(jnp.float32)
    half = parts.shape[0] // 2
    first = lax.axis_index("exp") == 0
    lower = parts[:half]
    upper = parts[half:]
    mine = jnp.where(first, lower, upper)
    theirs = jnp.where(first, upper, lower)
    got = exp_swap(theirs.astype(jnp.bfloat16))
    return mine + got.astype(jnp.float32)


def exp_gather_rows(rows):
    if lax.axis_size("exp") != 2:
        return lax.all_gather(rows, "exp", axis=0, tiled=True)
    got = exp_swap(rows)
    first = lax.axis_index("exp") == 0
    return jnp.where(
        first, jnp.concatenate([rows, got], axis=0), jnp.concatenate([got, rows], axis=0)
    )


def moe_whole_rows(normed, dispatch, combine, gate_matrix, up_matrix, down_matrix, n_ctx, capacity):
    all_normed = lax.all_gather(normed, "exp", axis=0, tiled=True)
    send_rows = jnp.dot(
        dispatch.astype(jnp.bfloat16), all_normed, preferred_element_type=jnp.float32
    ).astype(jnp.bfloat16)
    send_rows = send_rows.reshape(n_ctx, capacity, D)
    arrived = lax.all_to_all(send_rows, "ctx", split_axis=0, concat_axis=0, tiled=True)
    flat_rows = arrived.reshape(n_ctx * capacity, D)
    produced = expert_ffn(flat_rows, gate_matrix, up_matrix, down_matrix).reshape(
        n_ctx, capacity, D
    )
    served = lax.all_to_all(
        produced.astype(jnp.bfloat16), "ctx", split_axis=0, concat_axis=0, tiled=True
    )
    results = served.reshape(n_ctx * capacity, D).astype(jnp.float32)
    moe_part = jnp.dot(
        combine, results, precision=lax.Precision.HIGHEST, preferred_element_type=jnp.float32
    )
    return lax.psum_scatter(
        moe_part.astype(jnp.bfloat16), "exp", scatter_dimension=0, tiled=True
    ).astype(jnp.float32)


def halves(x, first, axis):
    size = x.shape[axis] // 2
    lower = lax.slice_in_dim(x, 0, size, axis=axis)
    upper = lax.slice_in_dim(x, size, 2 * size, axis=axis)
    return jnp.where(first, lower, upper), jnp.where(first, upper, lower)


def join(mine, theirs, first, axis):
    return jnp.where(
        first,
        jnp.concatenate([mine, theirs], axis=axis),
        jnp.concatenate([theirs, mine], axis=axis),
    )


def moe_column_halves(normed, dispatch, combine, gate_matrix, up_matrix, down_matrix, n_ctx, capacity):
    my_exp = lax.axis_index("exp")
    first = my_exp == 0
    half_d = normed.shape[1] // 2
    tokens_cols = halves(normed, first, 1)[0]
    tok_count = tokens_cols.shape[0]
    my_ctx = lax.axis_index("ctx")
    n_chip = n_ctx // 2
    my_chip = my_ctx // 2
    my_core = my_ctx % 2
    dispatch_parts = dispatch.reshape(2, n_chip, capacity, tok_count)
    full_d = normed.shape[1]
    near = jnp.dot(
        dispatch_parts[:, 0].reshape(2 * capacity, tok_count).astype(jnp.bfloat16),
        normed,
        preferred_element_type=jnp.float32,
    ).astype(jnp.bfloat16)
    near = near.reshape(2, capacity, full_d)
    far = jnp.dot(
        dispatch_parts[:, 1:].reshape(2 * (n_chip - 1) * capacity, tok_count).astype(jnp.bfloat16),
        tokens_cols,
        preferred_element_type=jnp.float32,
    ).astype(jnp.bfloat16)
    far = far.reshape(2, n_chip - 1, capacity, half_d)
    core_swap = [(i, i ^ 1) for i in range(n_ctx)]
    near_rows = capacity * full_d // half_d
    to_partner = jnp.concatenate(
        [near[1].reshape(near_rows, half_d), far[1].reshape(-1, half_d)], axis=0
    )
    from_partner = lax.ppermute(to_partner, "ctx", perm=core_swap)
    near_in = jnp.concatenate(
        [near[0], from_partner[:near_rows].reshape(capacity, full_d)], axis=0
    )
    far_from_partner = from_partner[near_rows:].reshape(n_chip - 1, capacity, half_d)
    far_pairs = jnp.stack([far[0], far_from_partner], axis=1)
    arrived = [None]
    for shift in range(1, n_chip):
        perm = [(i, ((i // 2 + shift) % n_chip) * 2 + i % 2) for i in range(n_ctx)]
        arrived.append(lax.ppermute(far_pairs[shift - 1], "ctx", perm=perm))
    my_start = my_exp * half_d
    other_start = (1 - my_exp) * half_d
    gate_mine = lax.dynamic_slice_in_dim(gate_matrix, my_start, half_d, axis=0)
    gate_other = lax.dynamic_slice_in_dim(gate_matrix, other_start, half_d, axis=0)
    up_mine = lax.dynamic_slice_in_dim(up_matrix, my_start, half_d, axis=0)
    up_other = lax.dynamic_slice_in_dim(up_matrix, other_start, half_d, axis=0)
    down_other = lax.dynamic_slice_in_dim(down_matrix, other_start, half_d, axis=1)
    down_mine = lax.dynamic_slice_in_dim(down_matrix, my_start, half_d, axis=1)
    if n_chip <= 4:
        groups = [[0]] + [[k] for k in range(1, n_chip)]
    else:
        groups = [[0], list(range(1, n_chip // 2)), list(range(n_chip // 2, n_chip))]
    returned = [None] * n_chip
    for shifts in groups:
        if shifts == [0]:
            gate_act = jnp.dot(near_in, gate_matrix, preferred_element_type=jnp.float32)
            up_act = jnp.dot(near_in, up_matrix, preferred_element_type=jnp.float32)
        else:
            block = jnp.concatenate([arrived[k] for k in shifts], axis=0).reshape(-1, half_d)
            partner_cols = exp_swap(block)
            gate_act = jnp.dot(block, gate_mine, preferred_element_type=jnp.float32) + jnp.dot(
                partner_cols, gate_other, preferred_element_type=jnp.float32
            )
            up_act = jnp.dot(block, up_mine, preferred_element_type=jnp.float32) + jnp.dot(
                partner_cols, up_other, preferred_element_type=jnp.float32
            )
        hidden = (jax.nn.silu(gate_act) * up_act).astype(jnp.bfloat16)
        out_other = jnp.dot(hidden, down_other, preferred_element_type=jnp.float32)
        got_other = exp_swap(out_other.astype(jnp.bfloat16))
        out_mine = jnp.dot(hidden, down_mine, preferred_element_type=jnp.float32)
        summed = (out_mine + got_other.astype(jnp.float32)).astype(jnp.bfloat16)
        summed = summed.reshape(len(shifts), 2, capacity, half_d)
        for idx, shift in enumerate(shifts):
            if shift == 0:
                returned[shift] = summed[idx]
            else:
                perm = [(i, ((i // 2 - shift) % n_chip) * 2 + i % 2) for i in range(n_ctx)]
                returned[shift] = lax.ppermute(summed[idx], "ctx", perm=perm)
    back = jnp.stack(returned)
    partner_res = lax.ppermute(back[:, 1], "ctx", perm=core_swap)
    served = jnp.stack([back[:, 0], partner_res]).reshape(n_ctx * capacity, half_d)
    moe_half = jnp.dot(
        combine,
        served.astype(jnp.float32),
        precision=lax.Precision.HIGHEST,
        preferred_element_type=jnp.float32,
    )
    my_tok, other_tok = halves(moe_half, first, 0)
    got_tok = exp_swap(other_tok.astype(jnp.bfloat16)).astype(jnp.float32)
    return join(my_tok, got_tok, first, 1)


def ctx_gather_blocks(rows, n_ctx, my_ctx):
    n_chip = n_ctx // 2
    my_chip = my_ctx // 2
    my_core = my_ctx % 2
    stack = [rows]
    for shift in range(1, n_chip):
        perm = [(i, ((i // 2 + shift) % n_chip) * 2 + i % 2) for i in range(n_ctx)]
        stack.append(lax.ppermute(rows, "ctx", perm=perm))
    own = jnp.stack(stack)
    partner = lax.ppermute(own, "ctx", perm=[(i, i ^ 1) for i in range(n_ctx)])
    shifts = jnp.arange(n_chip, dtype=jnp.int32)
    chips = (my_chip - shifts) % n_chip
    src_ctx = jnp.concatenate([chips * 2 + my_core, chips * 2 + (1 - my_core)])
    return jnp.concatenate([own, partner]), src_ctx


def local(
    query_states,
    key_states,
    value_states,
    residual,
    out_weight,
    norm_gain,
    gate_weight,
    up_weight,
    down_weight,
    routes,
    route_weights,
    prompt_lengths,
):
    n_ctx = lax.axis_size("ctx")
    my_ctx = lax.axis_index("ctx")
    tok_here = query_states.shape[1]
    feat_width = query_states.shape[2]
    heads_dev = feat_width // HD
    half_block = tok_here // 2
    score_scale = HD ** (-0.5)
    length = prompt_lengths[0]
    local_ids = jnp.arange(tok_here, dtype=jnp.int32)
    query_pos = row_positions(my_ctx * tok_here + local_ids, half_block, n_ctx)
    decode_pos = my_ctx * tok_here + local_ids
    query_three = query_states[0].reshape(tok_here, heads_dev, HD)
    run_max = jnp.full((heads_dev, tok_here), NEG, jnp.float32)
    kv_here = jnp.concatenate([key_states[0], value_states[0]], axis=1)
    kv_blocks, src_ctx = ctx_gather_blocks(kv_here, n_ctx, my_ctx)
    kv_all = kv_blocks.reshape(n_ctx * tok_here, 2 * feat_width)
    key_two = kv_all[:, :feat_width]
    value_two = kv_all[:, feat_width:]
    row_count = key_two.shape[0]
    row_ids = (src_ctx[:, None] * tok_here + local_ids[None, :]).reshape(row_count)
    key_pos = row_positions(row_ids, half_block, n_ctx)
    pick_rows = (decode_pos[:, None] == key_pos[None, :]).astype(jnp.bfloat16)
    kept_keys = jnp.dot(pick_rows, key_two, preferred_element_type=jnp.float32)
    kept_values = jnp.dot(pick_rows, value_two, preferred_element_type=jnp.float32)
    old_max = run_max
    key_heads = key_two.reshape(row_count, heads_dev, HD)
    value_heads = value_two.reshape(row_count, heads_dev, HD)
    logits = (
        jnp.einsum("qhd,khd->hqk", query_three, key_heads, preferred_element_type=jnp.float32)
        * score_scale
    )
    visible = (key_pos[None, :] <= query_pos[:, None]) & (key_pos[None, :] < length)
    logits = jnp.where(visible[None], logits, NEG)
    new_max = jnp.maximum(old_max, jnp.max(logits, axis=2))
    weights = jnp.where(visible[None], jnp.exp(logits - new_max[:, :, None]), 0.0)
    new_sum = jnp.sum(weights, axis=2)
    gained = jnp.einsum(
        "hqk,khd->hqd",
        weights.astype(jnp.bfloat16),
        value_heads,
        preferred_element_type=jnp.float32,
    )
    inner_state = (new_max, new_sum, gained)
    run_max, run_sum, run_out, kept_keys, kept_values = inner_state + (kept_keys, kept_values)
    mixed = (run_out / run_sum[:, :, None]).astype(jnp.bfloat16)
    mixed = jnp.transpose(mixed, (1, 0, 2)).reshape(tok_here, feat_width)
    out_parts = jnp.einsum(
        "tc,oc->to",
        mixed,
        lax.all_gather(out_weight, "ctx", axis=0, tiled=True),
        preferred_element_type=jnp.float32,
    )
    if lax.axis_size("exp") == 2:
        first_exp = lax.axis_index("exp") == 0
        residual_all = join(residual[0], exp_swap(residual[0]), first_exp, 0)
        head_all = out_parts + exp_swap(out_parts.astype(jnp.bfloat16)).astype(jnp.float32)
        stream_all = (residual_all.astype(jnp.float32) + head_all).astype(jnp.bfloat16)
        stream = halves(stream_all, first_exp, 0)[0]
        stream_f = stream_all.astype(jnp.float32)
    else:
        head_total = exp_reduce_rows(out_parts)
        stream = (residual[0].astype(jnp.float32) + head_total).astype(jnp.bfloat16)
        stream_f = stream.astype(jnp.float32)
    mean_sq = jnp.mean(stream_f * stream_f, axis=1, keepdims=True)
    normed = (stream_f * lax.rsqrt(mean_sq + EPS) * norm_gain).astype(jnp.bfloat16)
    capacity = min(tok_here, 2 * max(1, 3 * tok_here * TOP // (4 * n_ctx)))
    if lax.axis_size("exp") == 2:
        n_chip = n_ctx // 2

        def block_of(expert):
            other_core = (expert % 2 != my_ctx % 2).astype(jnp.int32)
            return other_core * n_chip + (expert // 2 - my_ctx // 2) % n_chip

        dispatch, combine = slot_tables(routes[0], route_weights[0], n_ctx, capacity, block_of)
        moe_rows = moe_column_halves(
            normed, dispatch, combine, gate_weight[0], up_weight[0], down_weight[0], n_ctx, capacity
        )
    else:
        dispatch, combine = slot_tables(routes[0], route_weights[0], n_ctx, capacity)
        moe_rows = moe_whole_rows(
            normed, dispatch, combine, gate_weight[0], up_weight[0], down_weight[0], n_ctx, capacity
        )
    layer_out = (stream.astype(jnp.float32) + moe_rows).astype(jnp.bfloat16)
    return (
        layer_out[None],
        kept_keys.astype(jnp.bfloat16)[None],
        kept_values.astype(jnp.bfloat16)[None],
    )


def solution(mesh):
    return jax.shard_map(
        local,
        mesh=mesh,
        in_specs=(
            P("req", "ctx", "exp"),
            P("req", "ctx", "exp"),
            P("req", "ctx", "exp"),
            P("req", ("ctx", "exp"), None),
            P("ctx", "exp"),
            P(),
            P("ctx", None, "exp"),
            P("ctx", None, "exp"),
            P("ctx", "exp", None),
            P("req", "ctx", None),
            P("req", "ctx", None),
            P("req"),
        ),
        out_specs=(P("req", ("ctx", "exp"), None), P("req", "ctx", "exp"), P("req", "ctx", "exp")),
        check_vma=False,
    )
```

```python
import jax
import jax.numpy as jnp
from jax import lax
from jax.sharding import PartitionSpec as P

D = 2048
HD = 128
TOP = 4


EPS = 1e-06
NEG = -1e30


def row_positions(row_ids, half_block, n_groups):
    block_ids = row_ids // half_block
    device = block_ids // 2
    target = jnp.where(block_ids % 2 == 0, device, 2 * n_groups - 1 - device)
    return target * half_block + row_ids % half_block


def slot_tables(route_block, weight_block, experts, capacity, block_of=None):
    tok_here, top_here = route_block.shape
    flat_ids = route_block.reshape(tok_here * top_here)
    hit_table = (flat_ids[:, None] == jnp.arange(experts, dtype=jnp.int32)[None, :]).astype(
        jnp.int32
    )
    before = jnp.cumsum(hit_table, axis=0) - hit_table
    slot_rank = jnp.sum(before * hit_table, axis=1)
    blocks = flat_ids if block_of is None else block_of(flat_ids)
    slot_index = blocks * capacity + slot_rank
    slot_match = (
        jnp.arange(experts * capacity, dtype=jnp.int32)[:, None] == slot_index[None, :]
    ).astype(jnp.float32)
    slot_match = slot_match.reshape(experts * capacity, tok_here, top_here)
    dispatch = jnp.sum(slot_match, axis=2)
    combine = jnp.transpose(jnp.sum(slot_match * weight_block[None, :, :], axis=2))
    return (dispatch, combine)


def expert_ffn(token_rows, gate_matrix, up_matrix, down_matrix):
    gate_act = jnp.dot(token_rows, gate_matrix, preferred_element_type=jnp.float32)
    up_act = jnp.dot(token_rows, up_matrix, preferred_element_type=jnp.float32)
    hidden = (jax.nn.silu(gate_act) * up_act).astype(jnp.bfloat16)
    return jnp.dot(hidden, down_matrix, preferred_element_type=jnp.float32)


def exp_swap(x):
    return lax.ppermute(x, "exp", perm=[(0, 1), (1, 0)])


def exp_reduce_rows(parts):
    if lax.axis_size("exp") != 2:
        return lax.psum_scatter(
            parts.astype(jnp.bfloat16), "exp", scatter_dimension=0, tiled=True
        ).astype(jnp.float32)
    half = parts.shape[0] // 2
    first = lax.axis_index("exp") == 0
    lower = parts[:half]
    upper = parts[half:]
    mine = jnp.where(first, lower, upper)
    theirs = jnp.where(first, upper, lower)
    got = exp_swap(theirs.astype(jnp.bfloat16))
    return mine + got.astype(jnp.float32)


def exp_gather_rows(rows):
    if lax.axis_size("exp") != 2:
        return lax.all_gather(rows, "exp", axis=0, tiled=True)
    got = exp_swap(rows)
    first = lax.axis_index("exp") == 0
    return jnp.where(
        first, jnp.concatenate([rows, got], axis=0), jnp.concatenate([got, rows], axis=0)
    )


def moe_whole_rows(normed, dispatch, combine, gate_matrix, up_matrix, down_matrix, n_ctx, capacity):
    all_normed = lax.all_gather(normed, "exp", axis=0, tiled=True)
    send_rows = jnp.dot(
        dispatch.astype(jnp.bfloat16), all_normed, preferred_element_type=jnp.float32
    ).astype(jnp.bfloat16)
    send_rows = send_rows.reshape(n_ctx, capacity, D)
    arrived = lax.all_to_all(send_rows, "ctx", split_axis=0, concat_axis=0, tiled=True)
    flat_rows = arrived.reshape(n_ctx * capacity, D)
    produced = expert_ffn(flat_rows, gate_matrix, up_matrix, down_matrix).reshape(
        n_ctx, capacity, D
    )
    served = lax.all_to_all(
        produced.astype(jnp.bfloat16), "ctx", split_axis=0, concat_axis=0, tiled=True
    )
    results = served.reshape(n_ctx * capacity, D).astype(jnp.float32)
    moe_part = jnp.dot(
        combine, results, precision=lax.Precision.HIGHEST, preferred_element_type=jnp.float32
    )
    return lax.psum_scatter(
        moe_part.astype(jnp.bfloat16), "exp", scatter_dimension=0, tiled=True
    ).astype(jnp.float32)


def halves(x, first, axis):
    size = x.shape[axis] // 2
    lower = lax.slice_in_dim(x, 0, size, axis=axis)
    upper = lax.slice_in_dim(x, size, 2 * size, axis=axis)
    return jnp.where(first, lower, upper), jnp.where(first, upper, lower)


def join(mine, theirs, first, axis):
    return jnp.where(
        first,
        jnp.concatenate([mine, theirs], axis=axis),
        jnp.concatenate([theirs, mine], axis=axis),
    )


def moe_column_halves(normed, dispatch, combine, gate_matrix, up_matrix, down_matrix, n_ctx, capacity):
    my_exp = lax.axis_index("exp")
    first = my_exp == 0
    half_d = normed.shape[1] // 2
    tokens_cols = halves(normed, first, 1)[0]
    tok_count = tokens_cols.shape[0]
    my_ctx = lax.axis_index("ctx")
    n_chip = n_ctx // 2
    my_chip = my_ctx // 2
    my_core = my_ctx % 2
    dispatch_parts = dispatch.reshape(2, n_chip, capacity, tok_count)
    full_d = normed.shape[1]
    near = jnp.dot(
        dispatch_parts[:, 0].reshape(2 * capacity, tok_count).astype(jnp.bfloat16),
        normed,
        preferred_element_type=jnp.float32,
    ).astype(jnp.bfloat16)
    near = near.reshape(2, capacity, full_d)
    far = jnp.dot(
        dispatch_parts[:, 1:].reshape(2 * (n_chip - 1) * capacity, tok_count).astype(jnp.bfloat16),
        tokens_cols,
        preferred_element_type=jnp.float32,
    ).astype(jnp.bfloat16)
    far = far.reshape(2, n_chip - 1, capacity, half_d)
    core_swap = [(i, i ^ 1) for i in range(n_ctx)]
    near_in = jnp.concatenate(
        [near[0], lax.ppermute(near[1], "ctx", perm=core_swap)], axis=0
    )
    far_pairs = jnp.stack([far[0], lax.ppermute(far[1], "ctx", perm=core_swap)], axis=1)
    arrived = [None]
    for shift in range(1, n_chip):
        perm = [(i, ((i // 2 + shift) % n_chip) * 2 + i % 2) for i in range(n_ctx)]
        arrived.append(lax.ppermute(far_pairs[shift - 1], "ctx", perm=perm))
    my_start = my_exp * half_d
    other_start = (1 - my_exp) * half_d
    gate_mine = lax.dynamic_slice_in_dim(gate_matrix, my_start, half_d, axis=0)
    gate_other = lax.dynamic_slice_in_dim(gate_matrix, other_start, half_d, axis=0)
    up_mine = lax.dynamic_slice_in_dim(up_matrix, my_start, half_d, axis=0)
    up_other = lax.dynamic_slice_in_dim(up_matrix, other_start, half_d, axis=0)
    down_other = lax.dynamic_slice_in_dim(down_matrix, other_start, half_d, axis=1)
    down_mine = lax.dynamic_slice_in_dim(down_matrix, my_start, half_d, axis=1)
    if n_chip <= 4:
        groups = [[0], [1], list(range(2, n_chip))] if n_chip > 2 else [[0], [1]]
    else:
        groups = [[0], list(range(1, n_chip // 2)), list(range(n_chip // 2, n_chip))]
    returned = [None] * n_chip
    for shifts in groups:
        if shifts == [0]:
            gate_act = jnp.dot(near_in, gate_matrix, preferred_element_type=jnp.float32)
            up_act = jnp.dot(near_in, up_matrix, preferred_element_type=jnp.float32)
        else:
            block = jnp.concatenate([arrived[k] for k in shifts], axis=0).reshape(-1, half_d)
            partner_cols = exp_swap(block)
            gate_act = jnp.dot(block, gate_mine, preferred_element_type=jnp.float32) + jnp.dot(
                partner_cols, gate_other, preferred_element_type=jnp.float32
            )
            up_act = jnp.dot(block, up_mine, preferred_element_type=jnp.float32) + jnp.dot(
                partner_cols, up_other, preferred_element_type=jnp.float32
            )
        hidden = (jax.nn.silu(gate_act) * up_act).astype(jnp.bfloat16)
        out_other = jnp.dot(hidden, down_other, preferred_element_type=jnp.float32)
        got_other = exp_swap(out_other.astype(jnp.bfloat16))
        out_mine = jnp.dot(hidden, down_mine, preferred_element_type=jnp.float32)
        summed = (out_mine + got_other.astype(jnp.float32)).astype(jnp.bfloat16)
        summed = summed.reshape(len(shifts), 2, capacity, half_d)
        for idx, shift in enumerate(shifts):
            if shift == 0:
                returned[shift] = summed[idx]
            else:
                perm = [(i, ((i // 2 - shift) % n_chip) * 2 + i % 2) for i in range(n_ctx)]
                returned[shift] = lax.ppermute(summed[idx], "ctx", perm=perm)
    back = jnp.stack(returned)
    partner_res = lax.ppermute(back[:, 1], "ctx", perm=core_swap)
    served = jnp.stack([back[:, 0], partner_res]).reshape(n_ctx * capacity, half_d)
    moe_half = jnp.dot(
        combine,
        served.astype(jnp.float32),
        precision=lax.Precision.HIGHEST,
        preferred_element_type=jnp.float32,
    )
    my_tok, other_tok = halves(moe_half, first, 0)
    got_tok = exp_swap(other_tok.astype(jnp.bfloat16)).astype(jnp.float32)
    return join(my_tok, got_tok, first, 1)


def ctx_gather_blocks(rows, n_ctx, my_ctx):
    n_chip = n_ctx // 2
    my_chip = my_ctx // 2
    my_core = my_ctx % 2
    stack = [rows]
    for shift in range(1, n_chip):
        perm = [(i, ((i // 2 + shift) % n_chip) * 2 + i % 2) for i in range(n_ctx)]
        stack.append(lax.ppermute(rows, "ctx", perm=perm))
    own = jnp.stack(stack)
    partner = lax.ppermute(own, "ctx", perm=[(i, i ^ 1) for i in range(n_ctx)])
    shifts = jnp.arange(n_chip, dtype=jnp.int32)
    chips = (my_chip - shifts) % n_chip
    src_ctx = jnp.concatenate([chips * 2 + my_core, chips * 2 + (1 - my_core)])
    return jnp.concatenate([own, partner]), src_ctx


def local(
    query_states,
    key_states,
    value_states,
    residual,
    out_weight,
    norm_gain,
    gate_weight,
    up_weight,
    down_weight,
    routes,
    route_weights,
    prompt_lengths,
):
    n_ctx = lax.axis_size("ctx")
    my_ctx = lax.axis_index("ctx")
    tok_here = query_states.shape[1]
    feat_width = query_states.shape[2]
    heads_dev = feat_width // HD
    half_block = tok_here // 2
    score_scale = HD ** (-0.5)
    length = prompt_lengths[0]
    local_ids = jnp.arange(tok_here, dtype=jnp.int32)
    query_pos = row_positions(my_ctx * tok_here + local_ids, half_block, n_ctx)
    decode_pos = my_ctx * tok_here + local_ids
    query_three = query_states[0].reshape(tok_here, heads_dev, HD)
    run_max = jnp.full((heads_dev, tok_here), NEG, jnp.float32)
    kv_here = jnp.concatenate([key_states[0], value_states[0]], axis=1)
    kv_blocks, src_ctx = ctx_gather_blocks(kv_here, n_ctx, my_ctx)
    kv_all = kv_blocks.reshape(n_ctx * tok_here, 2 * feat_width)
    key_two = kv_all[:, :feat_width]
    value_two = kv_all[:, feat_width:]
    row_count = key_two.shape[0]
    row_ids = (src_ctx[:, None] * tok_here + local_ids[None, :]).reshape(row_count)
    key_pos = row_positions(row_ids, half_block, n_ctx)
    pick_rows = (decode_pos[:, None] == key_pos[None, :]).astype(jnp.bfloat16)
    kept_keys = jnp.dot(pick_rows, key_two, preferred_element_type=jnp.float32)
    kept_values = jnp.dot(pick_rows, value_two, preferred_element_type=jnp.float32)
    old_max = run_max
    key_heads = key_two.reshape(row_count, heads_dev, HD)
    value_heads = value_two.reshape(row_count, heads_dev, HD)
    logits = (
        jnp.einsum("qhd,khd->hqk", query_three, key_heads, preferred_element_type=jnp.float32)
        * score_scale
    )
    visible = (key_pos[None, :] <= query_pos[:, None]) & (key_pos[None, :] < length)
    logits = jnp.where(visible[None], logits, NEG)
    new_max = jnp.maximum(old_max, jnp.max(logits, axis=2))
    weights = jnp.where(visible[None], jnp.exp(logits - new_max[:, :, None]), 0.0)
    new_sum = jnp.sum(weights, axis=2)
    gained = jnp.einsum(
        "hqk,khd->hqd",
        weights.astype(jnp.bfloat16),
        value_heads,
        preferred_element_type=jnp.float32,
    )
    inner_state = (new_max, new_sum, gained)
    run_max, run_sum, run_out, kept_keys, kept_values = inner_state + (kept_keys, kept_values)
    mixed = (run_out / run_sum[:, :, None]).astype(jnp.bfloat16)
    mixed = jnp.transpose(mixed, (1, 0, 2)).reshape(tok_here, feat_width)
    out_parts = jnp.einsum(
        "tc,oc->to",
        mixed,
        lax.all_gather(out_weight, "ctx", axis=0, tiled=True),
        preferred_element_type=jnp.float32,
    )
    if lax.axis_size("exp") == 2:
        first_exp = lax.axis_index("exp") == 0
        residual_all = join(residual[0], exp_swap(residual[0]), first_exp, 0)
        head_all = out_parts + exp_swap(out_parts.astype(jnp.bfloat16)).astype(jnp.float32)
        stream_all = (residual_all.astype(jnp.float32) + head_all).astype(jnp.bfloat16)
        stream = halves(stream_all, first_exp, 0)[0]
        stream_f = stream_all.astype(jnp.float32)
    else:
        head_total = exp_reduce_rows(out_parts)
        stream = (residual[0].astype(jnp.float32) + head_total).astype(jnp.bfloat16)
        stream_f = stream.astype(jnp.float32)
    mean_sq = jnp.mean(stream_f * stream_f, axis=1, keepdims=True)
    normed = (stream_f * lax.rsqrt(mean_sq + EPS) * norm_gain).astype(jnp.bfloat16)
    capacity = min(tok_here, 2 * max(1, 3 * tok_here * TOP // (4 * n_ctx)))
    if lax.axis_size("exp") == 2:
        n_chip = n_ctx // 2

        def block_of(expert):
            other_core = (expert % 2 != my_ctx % 2).astype(jnp.int32)
            return other_core * n_chip + (expert // 2 - my_ctx // 2) % n_chip

        dispatch, combine = slot_tables(routes[0], route_weights[0], n_ctx, capacity, block_of)
        moe_rows = moe_column_halves(
            normed, dispatch, combine, gate_weight[0], up_weight[0], down_weight[0], n_ctx, capacity
        )
    else:
        dispatch, combine = slot_tables(routes[0], route_weights[0], n_ctx, capacity)
        moe_rows = moe_whole_rows(
            normed, dispatch, combine, gate_weight[0], up_weight[0], down_weight[0], n_ctx, capacity
        )
    layer_out = (stream.astype(jnp.float32) + moe_rows).astype(jnp.bfloat16)
    return (
        layer_out[None],
        kept_keys.astype(jnp.bfloat16)[None],
        kept_values.astype(jnp.bfloat16)[None],
    )


def solution(mesh):
    return jax.shard_map(
        local,
        mesh=mesh,
        in_specs=(
            P("req", "ctx", "exp"),
            P("req", "ctx", "exp"),
            P("req", "ctx", "exp"),
            P("req", ("ctx", "exp"), None),
            P("ctx", "exp"),
            P(),
            P("ctx", None, "exp"),
            P("ctx", None, "exp"),
            P("ctx", "exp", None),
            P("req", "ctx", None),
            P("req", "ctx", None),
            P("req"),
        ),
        out_specs=(P("req", ("ctx", "exp"), None), P("req", "ctx", "exp"), P("req", "ctx", "exp")),
        check_vma=False,
    )
```

```python
import jax
import jax.numpy as jnp
from jax import lax
from jax.sharding import PartitionSpec as P

D = 2048
HD = 128
TOP = 4


EPS = 1e-06
NEG = -1e30


def row_positions(row_ids, half_block, n_groups):
    block_ids = row_ids // half_block
    device = block_ids // 2
    target = jnp.where(block_ids % 2 == 0, device, 2 * n_groups - 1 - device)
    return target * half_block + row_ids % half_block


def slot_tables(route_block, weight_block, experts, capacity, block_of=None):
    tok_here, top_here = route_block.shape
    flat_ids = route_block.reshape(tok_here * top_here)
    hit_table = (flat_ids[:, None] == jnp.arange(experts, dtype=jnp.int32)[None, :]).astype(
        jnp.int32
    )
    before = jnp.cumsum(hit_table, axis=0) - hit_table
    slot_rank = jnp.sum(before * hit_table, axis=1)
    blocks = flat_ids if block_of is None else block_of(flat_ids)
    slot_index = blocks * capacity + slot_rank
    slot_match = (
        jnp.arange(experts * capacity, dtype=jnp.int32)[:, None] == slot_index[None, :]
    ).astype(jnp.float32)
    slot_match = slot_match.reshape(experts * capacity, tok_here, top_here)
    dispatch = jnp.sum(slot_match, axis=2)
    combine = jnp.transpose(jnp.sum(slot_match * weight_block[None, :, :], axis=2))
    return (dispatch, combine)


def expert_ffn(token_rows, gate_matrix, up_matrix, down_matrix):
    gate_act = jnp.dot(token_rows, gate_matrix, preferred_element_type=jnp.float32)
    up_act = jnp.dot(token_rows, up_matrix, preferred_element_type=jnp.float32)
    hidden = (jax.nn.silu(gate_act) * up_act).astype(jnp.bfloat16)
    return jnp.dot(hidden, down_matrix, preferred_element_type=jnp.float32)


def exp_swap(x):
    return lax.ppermute(x, "exp", perm=[(0, 1), (1, 0)])


def exp_reduce_rows(parts):
    if lax.axis_size("exp") != 2:
        return lax.psum_scatter(
            parts.astype(jnp.bfloat16), "exp", scatter_dimension=0, tiled=True
        ).astype(jnp.float32)
    half = parts.shape[0] // 2
    first = lax.axis_index("exp") == 0
    lower = parts[:half]
    upper = parts[half:]
    mine = jnp.where(first, lower, upper)
    theirs = jnp.where(first, upper, lower)
    got = exp_swap(theirs.astype(jnp.bfloat16))
    return mine + got.astype(jnp.float32)


def exp_gather_rows(rows):
    if lax.axis_size("exp") != 2:
        return lax.all_gather(rows, "exp", axis=0, tiled=True)
    got = exp_swap(rows)
    first = lax.axis_index("exp") == 0
    return jnp.where(
        first, jnp.concatenate([rows, got], axis=0), jnp.concatenate([got, rows], axis=0)
    )


def moe_whole_rows(normed, dispatch, combine, gate_matrix, up_matrix, down_matrix, n_ctx, capacity):
    all_normed = lax.all_gather(normed, "exp", axis=0, tiled=True)
    send_rows = jnp.dot(
        dispatch.astype(jnp.bfloat16), all_normed, preferred_element_type=jnp.float32
    ).astype(jnp.bfloat16)
    send_rows = send_rows.reshape(n_ctx, capacity, D)
    arrived = lax.all_to_all(send_rows, "ctx", split_axis=0, concat_axis=0, tiled=True)
    flat_rows = arrived.reshape(n_ctx * capacity, D)
    produced = expert_ffn(flat_rows, gate_matrix, up_matrix, down_matrix).reshape(
        n_ctx, capacity, D
    )
    served = lax.all_to_all(
        produced.astype(jnp.bfloat16), "ctx", split_axis=0, concat_axis=0, tiled=True
    )
    results = served.reshape(n_ctx * capacity, D).astype(jnp.float32)
    moe_part = jnp.dot(
        combine, results, precision=lax.Precision.HIGHEST, preferred_element_type=jnp.float32
    )
    return lax.psum_scatter(
        moe_part.astype(jnp.bfloat16), "exp", scatter_dimension=0, tiled=True
    ).astype(jnp.float32)


def halves(x, first, axis):
    size = x.shape[axis] // 2
    lower = lax.slice_in_dim(x, 0, size, axis=axis)
    upper = lax.slice_in_dim(x, size, 2 * size, axis=axis)
    return jnp.where(first, lower, upper), jnp.where(first, upper, lower)


def join(mine, theirs, first, axis):
    return jnp.where(
        first,
        jnp.concatenate([mine, theirs], axis=axis),
        jnp.concatenate([theirs, mine], axis=axis),
    )


def moe_column_halves(normed, dispatch, combine, gate_matrix, up_matrix, down_matrix, n_ctx, capacity):
    my_exp = lax.axis_index("exp")
    first = my_exp == 0
    half_d = normed.shape[1] // 2
    tokens_cols = halves(normed, first, 1)[0]
    tok_count = tokens_cols.shape[0]
    my_ctx = lax.axis_index("ctx")
    n_chip = n_ctx // 2
    my_chip = my_ctx // 2
    my_core = my_ctx % 2
    dispatch_parts = dispatch.reshape(2, n_chip, capacity, tok_count)
    full_d = normed.shape[1]
    near = jnp.dot(
        dispatch_parts[:, 0].reshape(2 * capacity, tok_count).astype(jnp.bfloat16),
        normed,
        preferred_element_type=jnp.float32,
    ).astype(jnp.bfloat16)
    near = near.reshape(2, capacity, full_d)
    far = jnp.dot(
        dispatch_parts[:, 1:].reshape(2 * (n_chip - 1) * capacity, tok_count).astype(jnp.bfloat16),
        tokens_cols,
        preferred_element_type=jnp.float32,
    ).astype(jnp.bfloat16)
    far = far.reshape(2, n_chip - 1, capacity, half_d)
    core_swap = [(i, i ^ 1) for i in range(n_ctx)]
    near_in = jnp.concatenate(
        [near[0], lax.ppermute(near[1], "ctx", perm=core_swap)], axis=0
    )
    far_pairs = jnp.stack([far[0], lax.ppermute(far[1], "ctx", perm=core_swap)], axis=1)
    arrived = [None]
    for shift in range(1, n_chip):
        perm = [(i, ((i // 2 + shift) % n_chip) * 2 + i % 2) for i in range(n_ctx)]
        arrived.append(lax.ppermute(far_pairs[shift - 1], "ctx", perm=perm))
    my_start = my_exp * half_d
    other_start = (1 - my_exp) * half_d
    gate_mine = lax.dynamic_slice_in_dim(gate_matrix, my_start, half_d, axis=0)
    gate_other = lax.dynamic_slice_in_dim(gate_matrix, other_start, half_d, axis=0)
    up_mine = lax.dynamic_slice_in_dim(up_matrix, my_start, half_d, axis=0)
    up_other = lax.dynamic_slice_in_dim(up_matrix, other_start, half_d, axis=0)
    down_other = lax.dynamic_slice_in_dim(down_matrix, other_start, half_d, axis=1)
    down_mine = lax.dynamic_slice_in_dim(down_matrix, my_start, half_d, axis=1)
    if n_chip <= 4:
        groups = [[0]] + [[k] for k in range(1, n_chip)]
    else:
        groups = [[0], list(range(1, n_chip // 2)), list(range(n_chip // 2, n_chip))]
    returned = [None] * n_chip
    returned_partner = [None] * n_chip
    for shifts in groups:
        if shifts == [0]:
            gate_act = jnp.dot(near_in, gate_matrix, preferred_element_type=jnp.float32)
            up_act = jnp.dot(near_in, up_matrix, preferred_element_type=jnp.float32)
        else:
            block = jnp.concatenate([arrived[k] for k in shifts], axis=0).reshape(-1, half_d)
            partner_cols = exp_swap(block)
            gate_act = jnp.dot(block, gate_mine, preferred_element_type=jnp.float32) + jnp.dot(
                partner_cols, gate_other, preferred_element_type=jnp.float32
            )
            up_act = jnp.dot(block, up_mine, preferred_element_type=jnp.float32) + jnp.dot(
                partner_cols, up_other, preferred_element_type=jnp.float32
            )
        hidden = (jax.nn.silu(gate_act) * up_act).astype(jnp.bfloat16)
        out_other = jnp.dot(hidden, down_other, preferred_element_type=jnp.float32)
        got_other = exp_swap(out_other.astype(jnp.bfloat16))
        out_mine = jnp.dot(hidden, down_mine, preferred_element_type=jnp.float32)
        summed = (out_mine + got_other.astype(jnp.float32)).astype(jnp.bfloat16)
        summed = summed.reshape(len(shifts), 2, capacity, half_d)
        for idx, shift in enumerate(shifts):
            if shift == 0:
                returned[shift] = summed[idx][0]
                returned_partner[shift] = lax.ppermute(summed[idx][1], "ctx", perm=core_swap)
            else:
                perm = [(i, ((i // 2 - shift) % n_chip) * 2 + i % 2) for i in range(n_ctx)]
                returned[shift] = lax.ppermute(summed[idx][0], "ctx", perm=perm)
                perm = [(i, ((i // 2 - shift) % n_chip) * 2 + 1 - i % 2) for i in range(n_ctx)]
                returned_partner[shift] = lax.ppermute(summed[idx][1], "ctx", perm=perm)
    served = jnp.stack([jnp.stack(returned), jnp.stack(returned_partner)])
    served = served.reshape(n_ctx * capacity, half_d)
    moe_half = jnp.dot(
        combine,
        served.astype(jnp.float32),
        precision=lax.Precision.HIGHEST,
        preferred_element_type=jnp.float32,
    )
    my_tok, other_tok = halves(moe_half, first, 0)
    got_tok = exp_swap(other_tok.astype(jnp.bfloat16)).astype(jnp.float32)
    return join(my_tok, got_tok, first, 1)


def ctx_gather_blocks(rows, n_ctx, my_ctx):
    n_chip = n_ctx // 2
    my_chip = my_ctx // 2
    my_core = my_ctx % 2
    stack = [rows]
    for shift in range(1, n_chip):
        perm = [(i, ((i // 2 + shift) % n_chip) * 2 + i % 2) for i in range(n_ctx)]
        stack.append(lax.ppermute(rows, "ctx", perm=perm))
    own = jnp.stack(stack)
    partner = lax.ppermute(own, "ctx", perm=[(i, i ^ 1) for i in range(n_ctx)])
    shifts = jnp.arange(n_chip, dtype=jnp.int32)
    chips = (my_chip - shifts) % n_chip
    src_ctx = jnp.concatenate([chips * 2 + my_core, chips * 2 + (1 - my_core)])
    return jnp.concatenate([own, partner]), src_ctx


def local(
    query_states,
    key_states,
    value_states,
    residual,
    out_weight,
    norm_gain,
    gate_weight,
    up_weight,
    down_weight,
    routes,
    route_weights,
    prompt_lengths,
):
    n_ctx = lax.axis_size("ctx")
    my_ctx = lax.axis_index("ctx")
    tok_here = query_states.shape[1]
    feat_width = query_states.shape[2]
    heads_dev = feat_width // HD
    half_block = tok_here // 2
    score_scale = HD ** (-0.5)
    length = prompt_lengths[0]
    local_ids = jnp.arange(tok_here, dtype=jnp.int32)
    query_pos = row_positions(my_ctx * tok_here + local_ids, half_block, n_ctx)
    decode_pos = my_ctx * tok_here + local_ids
    query_three = query_states[0].reshape(tok_here, heads_dev, HD)
    run_max = jnp.full((heads_dev, tok_here), NEG, jnp.float32)
    kv_here = jnp.concatenate([key_states[0], value_states[0]], axis=1)
    kv_blocks, src_ctx = ctx_gather_blocks(kv_here, n_ctx, my_ctx)
    kv_all = kv_blocks.reshape(n_ctx * tok_here, 2 * feat_width)
    key_two = kv_all[:, :feat_width]
    value_two = kv_all[:, feat_width:]
    row_count = key_two.shape[0]
    row_ids = (src_ctx[:, None] * tok_here + local_ids[None, :]).reshape(row_count)
    key_pos = row_positions(row_ids, half_block, n_ctx)
    pick_rows = (decode_pos[:, None] == key_pos[None, :]).astype(jnp.bfloat16)
    kept_keys = jnp.dot(pick_rows, key_two, preferred_element_type=jnp.float32)
    kept_values = jnp.dot(pick_rows, value_two, preferred_element_type=jnp.float32)
    old_max = run_max
    key_heads = key_two.reshape(row_count, heads_dev, HD)
    value_heads = value_two.reshape(row_count, heads_dev, HD)
    logits = (
        jnp.einsum("qhd,khd->hqk", query_three, key_heads, preferred_element_type=jnp.float32)
        * score_scale
    )
    visible = (key_pos[None, :] <= query_pos[:, None]) & (key_pos[None, :] < length)
    logits = jnp.where(visible[None], logits, NEG)
    new_max = jnp.maximum(old_max, jnp.max(logits, axis=2))
    weights = jnp.where(visible[None], jnp.exp(logits - new_max[:, :, None]), 0.0)
    new_sum = jnp.sum(weights, axis=2)
    gained = jnp.einsum(
        "hqk,khd->hqd",
        weights.astype(jnp.bfloat16),
        value_heads,
        preferred_element_type=jnp.float32,
    )
    inner_state = (new_max, new_sum, gained)
    run_max, run_sum, run_out, kept_keys, kept_values = inner_state + (kept_keys, kept_values)
    mixed = (run_out / run_sum[:, :, None]).astype(jnp.bfloat16)
    mixed = jnp.transpose(mixed, (1, 0, 2)).reshape(tok_here, feat_width)
    out_parts = jnp.einsum(
        "tc,oc->to",
        mixed,
        lax.all_gather(out_weight, "ctx", axis=0, tiled=True),
        preferred_element_type=jnp.float32,
    )
    if lax.axis_size("exp") == 2:
        first_exp = lax.axis_index("exp") == 0
        residual_all = join(residual[0], exp_swap(residual[0]), first_exp, 0)
        head_all = out_parts + exp_swap(out_parts.astype(jnp.bfloat16)).astype(jnp.float32)
        stream_all = (residual_all.astype(jnp.float32) + head_all).astype(jnp.bfloat16)
        stream = halves(stream_all, first_exp, 0)[0]
        stream_f = stream_all.astype(jnp.float32)
    else:
        head_total = exp_reduce_rows(out_parts)
        stream = (residual[0].astype(jnp.float32) + head_total).astype(jnp.bfloat16)
        stream_f = stream.astype(jnp.float32)
    mean_sq = jnp.mean(stream_f * stream_f, axis=1, keepdims=True)
    normed = (stream_f * lax.rsqrt(mean_sq + EPS) * norm_gain).astype(jnp.bfloat16)
    capacity = min(tok_here, 2 * max(1, 3 * tok_here * TOP // (4 * n_ctx)))
    if lax.axis_size("exp") == 2:
        n_chip = n_ctx // 2

        def block_of(expert):
            other_core = (expert % 2 != my_ctx % 2).astype(jnp.int32)
            return other_core * n_chip + (expert // 2 - my_ctx // 2) % n_chip

        dispatch, combine = slot_tables(routes[0], route_weights[0], n_ctx, capacity, block_of)
        moe_rows = moe_column_halves(
            normed, dispatch, combine, gate_weight[0], up_weight[0], down_weight[0], n_ctx, capacity
        )
    else:
        dispatch, combine = slot_tables(routes[0], route_weights[0], n_ctx, capacity)
        moe_rows = moe_whole_rows(
            normed, dispatch, combine, gate_weight[0], up_weight[0], down_weight[0], n_ctx, capacity
        )
    layer_out = (stream.astype(jnp.float32) + moe_rows).astype(jnp.bfloat16)
    return (
        layer_out[None],
        kept_keys.astype(jnp.bfloat16)[None],
        kept_values.astype(jnp.bfloat16)[None],
    )


def solution(mesh):
    return jax.shard_map(
        local,
        mesh=mesh,
        in_specs=(
            P("req", "ctx", "exp"),
            P("req", "ctx", "exp"),
            P("req", "ctx", "exp"),
            P("req", ("ctx", "exp"), None),
            P("ctx", "exp"),
            P(),
            P("ctx", None, "exp"),
            P("ctx", None, "exp"),
            P("ctx", "exp", None),
            P("req", "ctx", None),
            P("req", "ctx", None),
            P("req"),
        ),
        out_specs=(P("req", ("ctx", "exp"), None), P("req", "ctx", "exp"), P("req", "ctx", "exp")),
        check_vma=False,
    )
```

```python
import jax
import jax.numpy as jnp
from jax import lax
from jax.sharding import PartitionSpec as P

D = 2048
HD = 128
TOP = 4


EPS = 1e-06
NEG = -1e30


def row_positions(row_ids, half_block, n_groups):
    block_ids = row_ids // half_block
    device = block_ids // 2
    target = jnp.where(block_ids % 2 == 0, device, 2 * n_groups - 1 - device)
    return target * half_block + row_ids % half_block


def slot_tables(route_block, weight_block, experts, capacity, block_of=None):
    tok_here, top_here = route_block.shape
    flat_ids = route_block.reshape(tok_here * top_here)
    hit_table = (flat_ids[:, None] == jnp.arange(experts, dtype=jnp.int32)[None, :]).astype(
        jnp.int32
    )
    before = jnp.cumsum(hit_table, axis=0) - hit_table
    slot_rank = jnp.sum(before * hit_table, axis=1)
    blocks = flat_ids if block_of is None else block_of(flat_ids)
    slot_index = blocks * capacity + slot_rank
    slot_match = (
        jnp.arange(experts * capacity, dtype=jnp.int32)[:, None] == slot_index[None, :]
    ).astype(jnp.float32)
    slot_match = slot_match.reshape(experts * capacity, tok_here, top_here)
    dispatch = jnp.sum(slot_match, axis=2)
    combine = jnp.transpose(jnp.sum(slot_match * weight_block[None, :, :], axis=2))
    return (dispatch, combine)


def expert_ffn(token_rows, gate_matrix, up_matrix, down_matrix):
    gate_act = jnp.dot(token_rows, gate_matrix, preferred_element_type=jnp.float32)
    up_act = jnp.dot(token_rows, up_matrix, preferred_element_type=jnp.float32)
    hidden = (jax.nn.silu(gate_act) * up_act).astype(jnp.bfloat16)
    return jnp.dot(hidden, down_matrix, preferred_element_type=jnp.float32)


def exp_swap(x):
    return lax.ppermute(x, "exp", perm=[(0, 1), (1, 0)])


def exp_reduce_rows(parts):
    if lax.axis_size("exp") != 2:
        return lax.psum_scatter(
            parts.astype(jnp.bfloat16), "exp", scatter_dimension=0, tiled=True
        ).astype(jnp.float32)
    half = parts.shape[0] // 2
    first = lax.axis_index("exp") == 0
    lower = parts[:half]
    upper = parts[half:]
    mine = jnp.where(first, lower, upper)
    theirs = jnp.where(first, upper, lower)
    got = exp_swap(theirs.astype(jnp.bfloat16))
    return mine + got.astype(jnp.float32)


def exp_gather_rows(rows):
    if lax.axis_size("exp") != 2:
        return lax.all_gather(rows, "exp", axis=0, tiled=True)
    got = exp_swap(rows)
    first = lax.axis_index("exp") == 0
    return jnp.where(
        first, jnp.concatenate([rows, got], axis=0), jnp.concatenate([got, rows], axis=0)
    )


def moe_whole_rows(normed, dispatch, combine, gate_matrix, up_matrix, down_matrix, n_ctx, capacity):
    all_normed = lax.all_gather(normed, "exp", axis=0, tiled=True)
    send_rows = jnp.dot(
        dispatch.astype(jnp.bfloat16), all_normed, preferred_element_type=jnp.float32
    ).astype(jnp.bfloat16)
    send_rows = send_rows.reshape(n_ctx, capacity, D)
    arrived = lax.all_to_all(send_rows, "ctx", split_axis=0, concat_axis=0, tiled=True)
    flat_rows = arrived.reshape(n_ctx * capacity, D)
    produced = expert_ffn(flat_rows, gate_matrix, up_matrix, down_matrix).reshape(
        n_ctx, capacity, D
    )
    served = lax.all_to_all(
        produced.astype(jnp.bfloat16), "ctx", split_axis=0, concat_axis=0, tiled=True
    )
    results = served.reshape(n_ctx * capacity, D).astype(jnp.float32)
    moe_part = jnp.dot(
        combine, results, precision=lax.Precision.HIGHEST, preferred_element_type=jnp.float32
    )
    return lax.psum_scatter(
        moe_part.astype(jnp.bfloat16), "exp", scatter_dimension=0, tiled=True
    ).astype(jnp.float32)


def halves(x, first, axis):
    size = x.shape[axis] // 2
    lower = lax.slice_in_dim(x, 0, size, axis=axis)
    upper = lax.slice_in_dim(x, size, 2 * size, axis=axis)
    return jnp.where(first, lower, upper), jnp.where(first, upper, lower)


def join(mine, theirs, first, axis):
    return jnp.where(
        first,
        jnp.concatenate([mine, theirs], axis=axis),
        jnp.concatenate([theirs, mine], axis=axis),
    )


def moe_column_halves(normed, dispatch, combine, gate_matrix, up_matrix, down_matrix, n_ctx, capacity):
    my_exp = lax.axis_index("exp")
    first = my_exp == 0
    half_d = normed.shape[1] // 2
    tokens_cols = halves(normed, first, 1)[0]
    tok_count = tokens_cols.shape[0]
    my_ctx = lax.axis_index("ctx")
    n_chip = n_ctx // 2
    my_chip = my_ctx // 2
    my_core = my_ctx % 2
    dispatch_parts = dispatch.reshape(2, n_chip, capacity, tok_count)
    full_d = normed.shape[1]
    near = jnp.dot(
        dispatch_parts[:, 0].reshape(2 * capacity, tok_count).astype(jnp.bfloat16),
        normed,
        preferred_element_type=jnp.float32,
    ).astype(jnp.bfloat16)
    near = near.reshape(2, capacity, full_d)
    far = jnp.dot(
        dispatch_parts[:, 1:].reshape(2 * (n_chip - 1) * capacity, tok_count).astype(jnp.bfloat16),
        tokens_cols,
        preferred_element_type=jnp.float32,
    ).astype(jnp.bfloat16)
    far = far.reshape(2, n_chip - 1, capacity, half_d)
    core_swap = [(i, i ^ 1) for i in range(n_ctx)]
    near_in = jnp.concatenate(
        [near[0], lax.ppermute(near[1], "ctx", perm=core_swap)], axis=0
    )
    arrived = [None]
    for shift in range(1, n_chip):
        perm = [(i, ((i // 2 + shift) % n_chip) * 2 + i % 2) for i in range(n_ctx)]
        from_same = lax.ppermute(far[0][shift - 1], "ctx", perm=perm)
        perm = [(i, ((i // 2 + shift) % n_chip) * 2 + 1 - i % 2) for i in range(n_ctx)]
        from_other = lax.ppermute(far[1][shift - 1], "ctx", perm=perm)
        arrived.append(jnp.stack([from_same, from_other]))
    my_start = my_exp * half_d
    other_start = (1 - my_exp) * half_d
    gate_mine = lax.dynamic_slice_in_dim(gate_matrix, my_start, half_d, axis=0)
    gate_other = lax.dynamic_slice_in_dim(gate_matrix, other_start, half_d, axis=0)
    up_mine = lax.dynamic_slice_in_dim(up_matrix, my_start, half_d, axis=0)
    up_other = lax.dynamic_slice_in_dim(up_matrix, other_start, half_d, axis=0)
    down_other = lax.dynamic_slice_in_dim(down_matrix, other_start, half_d, axis=1)
    down_mine = lax.dynamic_slice_in_dim(down_matrix, my_start, half_d, axis=1)
    if n_chip <= 4:
        groups = [[0]] + [[k] for k in range(1, n_chip)]
    else:
        groups = [[0], list(range(1, n_chip // 2)), list(range(n_chip // 2, n_chip))]
    returned = [None] * n_chip
    returned_partner = [None] * n_chip
    for shifts in groups:
        if shifts == [0]:
            gate_act = jnp.dot(near_in, gate_matrix, preferred_element_type=jnp.float32)
            up_act = jnp.dot(near_in, up_matrix, preferred_element_type=jnp.float32)
        else:
            block = jnp.concatenate([arrived[k] for k in shifts], axis=0).reshape(-1, half_d)
            partner_cols = exp_swap(block)
            gate_act = jnp.dot(block, gate_mine, preferred_element_type=jnp.float32) + jnp.dot(
                partner_cols, gate_other, preferred_element_type=jnp.float32
            )
            up_act = jnp.dot(block, up_mine, preferred_element_type=jnp.float32) + jnp.dot(
                partner_cols, up_other, preferred_element_type=jnp.float32
            )
        hidden = (jax.nn.silu(gate_act) * up_act).astype(jnp.bfloat16)
        out_other = jnp.dot(hidden, down_other, preferred_element_type=jnp.float32)
        got_other = exp_swap(out_other.astype(jnp.bfloat16))
        out_mine = jnp.dot(hidden, down_mine, preferred_element_type=jnp.float32)
        summed = (out_mine + got_other.astype(jnp.float32)).astype(jnp.bfloat16)
        summed = summed.reshape(len(shifts), 2, capacity, half_d)
        for idx, shift in enumerate(shifts):
            if shift == 0:
                returned[shift] = summed[idx][0]
                returned_partner[shift] = lax.ppermute(summed[idx][1], "ctx", perm=core_swap)
            else:
                perm = [(i, ((i // 2 - shift) % n_chip) * 2 + i % 2) for i in range(n_ctx)]
                returned[shift] = lax.ppermute(summed[idx][0], "ctx", perm=perm)
                perm = [(i, ((i // 2 - shift) % n_chip) * 2 + 1 - i % 2) for i in range(n_ctx)]
                returned_partner[shift] = lax.ppermute(summed[idx][1], "ctx", perm=perm)
    served = jnp.stack([jnp.stack(returned), jnp.stack(returned_partner)])
    served = served.reshape(n_ctx * capacity, half_d)
    moe_half = jnp.dot(
        combine,
        served.astype(jnp.float32),
        precision=lax.Precision.HIGHEST,
        preferred_element_type=jnp.float32,
    )
    my_tok, other_tok = halves(moe_half, first, 0)
    got_tok = exp_swap(other_tok.astype(jnp.bfloat16)).astype(jnp.float32)
    return join(my_tok, got_tok, first, 1)


def ctx_gather_blocks(rows, n_ctx, my_ctx):
    n_chip = n_ctx // 2
    my_chip = my_ctx // 2
    my_core = my_ctx % 2
    stack = [rows]
    for shift in range(1, n_chip):
        perm = [(i, ((i // 2 + shift) % n_chip) * 2 + i % 2) for i in range(n_ctx)]
        stack.append(lax.ppermute(rows, "ctx", perm=perm))
    own = jnp.stack(stack)
    partner = lax.ppermute(own, "ctx", perm=[(i, i ^ 1) for i in range(n_ctx)])
    shifts = jnp.arange(n_chip, dtype=jnp.int32)
    chips = (my_chip - shifts) % n_chip
    src_ctx = jnp.concatenate([chips * 2 + my_core, chips * 2 + (1 - my_core)])
    return jnp.concatenate([own, partner]), src_ctx


def local(
    query_states,
    key_states,
    value_states,
    residual,
    out_weight,
    norm_gain,
    gate_weight,
    up_weight,
    down_weight,
    routes,
    route_weights,
    prompt_lengths,
):
    n_ctx = lax.axis_size("ctx")
    my_ctx = lax.axis_index("ctx")
    tok_here = query_states.shape[1]
    feat_width = query_states.shape[2]
    heads_dev = feat_width // HD
    half_block = tok_here // 2
    score_scale = HD ** (-0.5)
    length = prompt_lengths[0]
    local_ids = jnp.arange(tok_here, dtype=jnp.int32)
    query_pos = row_positions(my_ctx * tok_here + local_ids, half_block, n_ctx)
    decode_pos = my_ctx * tok_here + local_ids
    query_three = query_states[0].reshape(tok_here, heads_dev, HD)
    run_max = jnp.full((heads_dev, tok_here), NEG, jnp.float32)
    kv_here = jnp.concatenate([key_states[0], value_states[0]], axis=1)
    kv_blocks, src_ctx = ctx_gather_blocks(kv_here, n_ctx, my_ctx)
    kv_all = kv_blocks.reshape(n_ctx * tok_here, 2 * feat_width)
    key_two = kv_all[:, :feat_width]
    value_two = kv_all[:, feat_width:]
    row_count = key_two.shape[0]
    row_ids = (src_ctx[:, None] * tok_here + local_ids[None, :]).reshape(row_count)
    key_pos = row_positions(row_ids, half_block, n_ctx)
    pick_rows = (decode_pos[:, None] == key_pos[None, :]).astype(jnp.bfloat16)
    kept_keys = jnp.dot(pick_rows, key_two, preferred_element_type=jnp.float32)
    kept_values = jnp.dot(pick_rows, value_two, preferred_element_type=jnp.float32)
    old_max = run_max
    key_heads = key_two.reshape(row_count, heads_dev, HD)
    value_heads = value_two.reshape(row_count, heads_dev, HD)
    logits = (
        jnp.einsum("qhd,khd->hqk", query_three, key_heads, preferred_element_type=jnp.float32)
        * score_scale
    )
    visible = (key_pos[None, :] <= query_pos[:, None]) & (key_pos[None, :] < length)
    logits = jnp.where(visible[None], logits, NEG)
    new_max = jnp.maximum(old_max, jnp.max(logits, axis=2))
    weights = jnp.where(visible[None], jnp.exp(logits - new_max[:, :, None]), 0.0)
    new_sum = jnp.sum(weights, axis=2)
    gained = jnp.einsum(
        "hqk,khd->hqd",
        weights.astype(jnp.bfloat16),
        value_heads,
        preferred_element_type=jnp.float32,
    )
    inner_state = (new_max, new_sum, gained)
    run_max, run_sum, run_out, kept_keys, kept_values = inner_state + (kept_keys, kept_values)
    mixed = (run_out / run_sum[:, :, None]).astype(jnp.bfloat16)
    mixed = jnp.transpose(mixed, (1, 0, 2)).reshape(tok_here, feat_width)
    out_parts = jnp.einsum(
        "tc,oc->to",
        mixed,
        lax.all_gather(out_weight, "ctx", axis=0, tiled=True),
        preferred_element_type=jnp.float32,
    )
    if lax.axis_size("exp") == 2:
        first_exp = lax.axis_index("exp") == 0
        residual_all = join(residual[0], exp_swap(residual[0]), first_exp, 0)
        head_all = out_parts + exp_swap(out_parts.astype(jnp.bfloat16)).astype(jnp.float32)
        stream_all = (residual_all.astype(jnp.float32) + head_all).astype(jnp.bfloat16)
        stream = halves(stream_all, first_exp, 0)[0]
        stream_f = stream_all.astype(jnp.float32)
    else:
        head_total = exp_reduce_rows(out_parts)
        stream = (residual[0].astype(jnp.float32) + head_total).astype(jnp.bfloat16)
        stream_f = stream.astype(jnp.float32)
    mean_sq = jnp.mean(stream_f * stream_f, axis=1, keepdims=True)
    normed = (stream_f * lax.rsqrt(mean_sq + EPS) * norm_gain).astype(jnp.bfloat16)
    capacity = min(tok_here, 2 * max(1, 3 * tok_here * TOP // (4 * n_ctx)))
    if lax.axis_size("exp") == 2:
        n_chip = n_ctx // 2

        def block_of(expert):
            other_core = (expert % 2 != my_ctx % 2).astype(jnp.int32)
            return other_core * n_chip + (expert // 2 - my_ctx // 2) % n_chip

        dispatch, combine = slot_tables(routes[0], route_weights[0], n_ctx, capacity, block_of)
        moe_rows = moe_column_halves(
            normed, dispatch, combine, gate_weight[0], up_weight[0], down_weight[0], n_ctx, capacity
        )
    else:
        dispatch, combine = slot_tables(routes[0], route_weights[0], n_ctx, capacity)
        moe_rows = moe_whole_rows(
            normed, dispatch, combine, gate_weight[0], up_weight[0], down_weight[0], n_ctx, capacity
        )
    layer_out = (stream.astype(jnp.float32) + moe_rows).astype(jnp.bfloat16)
    return (
        layer_out[None],
        kept_keys.astype(jnp.bfloat16)[None],
        kept_values.astype(jnp.bfloat16)[None],
    )


def solution(mesh):
    return jax.shard_map(
        local,
        mesh=mesh,
        in_specs=(
            P("req", "ctx", "exp"),
            P("req", "ctx", "exp"),
            P("req", "ctx", "exp"),
            P("req", ("ctx", "exp"), None),
            P("ctx", "exp"),
            P(),
            P("ctx", None, "exp"),
            P("ctx", None, "exp"),
            P("ctx", "exp", None),
            P("req", "ctx", None),
            P("req", "ctx", None),
            P("req"),
        ),
        out_specs=(P("req", ("ctx", "exp"), None), P("req", "ctx", "exp"), P("req", "ctx", "exp")),
        check_vma=False,
    )
```

```python
import jax
import jax.numpy as jnp
from jax import lax
from jax.sharding import PartitionSpec as P

D = 2048
HD = 128
TOP = 4


EPS = 1e-06
NEG = -1e30


def row_positions(row_ids, half_block, n_groups):
    block_ids = row_ids // half_block
    device = block_ids // 2
    target = jnp.where(block_ids % 2 == 0, device, 2 * n_groups - 1 - device)
    return target * half_block + row_ids % half_block


def slot_tables(route_block, weight_block, experts, capacity, block_of=None):
    tok_here, top_here = route_block.shape
    flat_ids = route_block.reshape(tok_here * top_here)
    hit_table = (flat_ids[:, None] == jnp.arange(experts, dtype=jnp.int32)[None, :]).astype(
        jnp.int32
    )
    before = jnp.cumsum(hit_table, axis=0) - hit_table
    slot_rank = jnp.sum(before * hit_table, axis=1)
    blocks = flat_ids if block_of is None else block_of(flat_ids)
    slot_index = blocks * capacity + slot_rank
    slot_match = (
        jnp.arange(experts * capacity, dtype=jnp.int32)[:, None] == slot_index[None, :]
    ).astype(jnp.float32)
    slot_match = slot_match.reshape(experts * capacity, tok_here, top_here)
    dispatch = jnp.sum(slot_match, axis=2)
    combine = jnp.transpose(jnp.sum(slot_match * weight_block[None, :, :], axis=2))
    return (dispatch, combine)


def expert_ffn(token_rows, gate_matrix, up_matrix, down_matrix):
    gate_act = jnp.dot(token_rows, gate_matrix, preferred_element_type=jnp.float32)
    up_act = jnp.dot(token_rows, up_matrix, preferred_element_type=jnp.float32)
    hidden = (jax.nn.silu(gate_act) * up_act).astype(jnp.bfloat16)
    return jnp.dot(hidden, down_matrix, preferred_element_type=jnp.float32)


def exp_swap(x):
    return lax.ppermute(x, "exp", perm=[(0, 1), (1, 0)])


def exp_reduce_rows(parts):
    if lax.axis_size("exp") != 2:
        return lax.psum_scatter(
            parts.astype(jnp.bfloat16), "exp", scatter_dimension=0, tiled=True
        ).astype(jnp.float32)
    half = parts.shape[0] // 2
    first = lax.axis_index("exp") == 0
    lower = parts[:half]
    upper = parts[half:]
    mine = jnp.where(first, lower, upper)
    theirs = jnp.where(first, upper, lower)
    got = exp_swap(theirs.astype(jnp.bfloat16))
    return mine + got.astype(jnp.float32)


def exp_gather_rows(rows):
    if lax.axis_size("exp") != 2:
        return lax.all_gather(rows, "exp", axis=0, tiled=True)
    got = exp_swap(rows)
    first = lax.axis_index("exp") == 0
    return jnp.where(
        first, jnp.concatenate([rows, got], axis=0), jnp.concatenate([got, rows], axis=0)
    )


def moe_whole_rows(normed, dispatch, combine, gate_matrix, up_matrix, down_matrix, n_ctx, capacity):
    all_normed = lax.all_gather(normed, "exp", axis=0, tiled=True)
    send_rows = jnp.dot(
        dispatch.astype(jnp.bfloat16), all_normed, preferred_element_type=jnp.float32
    ).astype(jnp.bfloat16)
    send_rows = send_rows.reshape(n_ctx, capacity, D)
    arrived = lax.all_to_all(send_rows, "ctx", split_axis=0, concat_axis=0, tiled=True)
    flat_rows = arrived.reshape(n_ctx * capacity, D)
    produced = expert_ffn(flat_rows, gate_matrix, up_matrix, down_matrix).reshape(
        n_ctx, capacity, D
    )
    served = lax.all_to_all(
        produced.astype(jnp.bfloat16), "ctx", split_axis=0, concat_axis=0, tiled=True
    )
    results = served.reshape(n_ctx * capacity, D).astype(jnp.float32)
    moe_part = jnp.dot(
        combine, results, precision=lax.Precision.HIGHEST, preferred_element_type=jnp.float32
    )
    return lax.psum_scatter(
        moe_part.astype(jnp.bfloat16), "exp", scatter_dimension=0, tiled=True
    ).astype(jnp.float32)


def halves(x, first, axis):
    size = x.shape[axis] // 2
    lower = lax.slice_in_dim(x, 0, size, axis=axis)
    upper = lax.slice_in_dim(x, size, 2 * size, axis=axis)
    return jnp.where(first, lower, upper), jnp.where(first, upper, lower)


def join(mine, theirs, first, axis):
    return jnp.where(
        first,
        jnp.concatenate([mine, theirs], axis=axis),
        jnp.concatenate([theirs, mine], axis=axis),
    )


def moe_column_halves(normed, dispatch, combine, gate_matrix, up_matrix, down_matrix, n_ctx, capacity):
    my_exp = lax.axis_index("exp")
    first = my_exp == 0
    half_d = normed.shape[1] // 2
    tokens_cols = halves(normed, first, 1)[0]
    tok_count = tokens_cols.shape[0]
    my_ctx = lax.axis_index("ctx")
    n_chip = n_ctx // 2
    my_chip = my_ctx // 2
    my_core = my_ctx % 2
    dispatch_parts = dispatch.reshape(2, n_chip, capacity, tok_count)
    full_d = normed.shape[1]
    near = jnp.dot(
        dispatch_parts[:, 0].reshape(2 * capacity, tok_count).astype(jnp.bfloat16),
        normed,
        preferred_element_type=jnp.float32,
    ).astype(jnp.bfloat16)
    near = near.reshape(2, capacity, full_d)
    far = jnp.dot(
        dispatch_parts[:, 1:].reshape(2 * (n_chip - 1) * capacity, tok_count).astype(jnp.bfloat16),
        tokens_cols,
        preferred_element_type=jnp.float32,
    ).astype(jnp.bfloat16)
    far = far.reshape(2, n_chip - 1, capacity, half_d)
    core_swap = [(i, i ^ 1) for i in range(n_ctx)]
    near_in = jnp.concatenate(
        [near[0], lax.ppermute(near[1], "ctx", perm=core_swap)], axis=0
    )
    far_pairs = jnp.stack([far[0], lax.ppermute(far[1], "ctx", perm=core_swap)], axis=1)
    arrived = [None]
    for shift in range(1, n_chip):
        perm = [(i, ((i // 2 + shift) % n_chip) * 2 + i % 2) for i in range(n_ctx)]
        arrived.append(lax.ppermute(far_pairs[shift - 1], "ctx", perm=perm))
    my_start = my_exp * half_d
    other_start = (1 - my_exp) * half_d
    gate_mine = lax.dynamic_slice_in_dim(gate_matrix, my_start, half_d, axis=0)
    gate_other = lax.dynamic_slice_in_dim(gate_matrix, other_start, half_d, axis=0)
    up_mine = lax.dynamic_slice_in_dim(up_matrix, my_start, half_d, axis=0)
    up_other = lax.dynamic_slice_in_dim(up_matrix, other_start, half_d, axis=0)
    down_other = lax.dynamic_slice_in_dim(down_matrix, other_start, half_d, axis=1)
    down_mine = lax.dynamic_slice_in_dim(down_matrix, my_start, half_d, axis=1)
    if n_chip <= 4:
        groups = [[0]] + [[k] for k in range(1, n_chip)]
    else:
        groups = [[0], list(range(1, n_chip // 2)), list(range(n_chip // 2, n_chip))]
    returned = [None] * n_chip
    returned_partner = [None] * n_chip
    for shifts in groups:
        if shifts == [0]:
            gate_act = jnp.dot(near_in, gate_matrix, preferred_element_type=jnp.float32)
            up_act = jnp.dot(near_in, up_matrix, preferred_element_type=jnp.float32)
        else:
            block = jnp.concatenate([arrived[k] for k in shifts], axis=0).reshape(-1, half_d)
            partner_cols = exp_swap(block)
            gate_act = jnp.dot(block, gate_mine, preferred_element_type=jnp.float32) + jnp.dot(
                partner_cols, gate_other, preferred_element_type=jnp.float32
            )
            up_act = jnp.dot(block, up_mine, preferred_element_type=jnp.float32) + jnp.dot(
                partner_cols, up_other, preferred_element_type=jnp.float32
            )
        hidden = (jax.nn.silu(gate_act) * up_act).astype(jnp.bfloat16)
        out_other = jnp.dot(hidden, down_other, preferred_element_type=jnp.float32)
        got_other = exp_swap(out_other.astype(jnp.bfloat16))
        out_mine = jnp.dot(hidden, down_mine, preferred_element_type=jnp.float32)
        summed = (out_mine + got_other.astype(jnp.float32)).astype(jnp.bfloat16)
        summed = summed.reshape(len(shifts), 2, capacity, half_d)
        for idx, shift in enumerate(shifts):
            if shift == 0:
                returned[shift] = summed[idx][0]
                returned_partner[shift] = lax.ppermute(summed[idx][1], "ctx", perm=core_swap)
            else:
                perm = [(i, ((i // 2 - shift) % n_chip) * 2 + i % 2) for i in range(n_ctx)]
                returned[shift] = lax.ppermute(summed[idx][0], "ctx", perm=perm)
                perm = [(i, ((i // 2 - shift) % n_chip) * 2 + 1 - i % 2) for i in range(n_ctx)]
                returned_partner[shift] = lax.ppermute(summed[idx][1], "ctx", perm=perm)
    served = jnp.stack([jnp.stack(returned), jnp.stack(returned_partner)])
    served = served.reshape(n_ctx * capacity, half_d)
    weight_hi = combine.astype(jnp.bfloat16)
    weight_lo = (combine - weight_hi.astype(jnp.float32)).astype(jnp.bfloat16)
    moe_half = jnp.dot(weight_hi, served, preferred_element_type=jnp.float32) + jnp.dot(
        weight_lo, served, preferred_element_type=jnp.float32
    )
    my_tok, other_tok = halves(moe_half, first, 0)
    got_tok = exp_swap(other_tok.astype(jnp.bfloat16)).astype(jnp.float32)
    return join(my_tok, got_tok, first, 1)


def ctx_gather_blocks(rows, n_ctx, my_ctx):
    n_chip = n_ctx // 2
    my_chip = my_ctx // 2
    my_core = my_ctx % 2
    stack = [rows]
    for shift in range(1, n_chip):
        perm = [(i, ((i // 2 + shift) % n_chip) * 2 + i % 2) for i in range(n_ctx)]
        stack.append(lax.ppermute(rows, "ctx", perm=perm))
    own = jnp.stack(stack)
    partner = lax.ppermute(own, "ctx", perm=[(i, i ^ 1) for i in range(n_ctx)])
    shifts = jnp.arange(n_chip, dtype=jnp.int32)
    chips = (my_chip - shifts) % n_chip
    src_ctx = jnp.concatenate([chips * 2 + my_core, chips * 2 + (1 - my_core)])
    return jnp.concatenate([own, partner]), src_ctx


def local(
    query_states,
    key_states,
    value_states,
    residual,
    out_weight,
    norm_gain,
    gate_weight,
    up_weight,
    down_weight,
    routes,
    route_weights,
    prompt_lengths,
):
    n_ctx = lax.axis_size("ctx")
    my_ctx = lax.axis_index("ctx")
    tok_here = query_states.shape[1]
    feat_width = query_states.shape[2]
    heads_dev = feat_width // HD
    half_block = tok_here // 2
    score_scale = HD ** (-0.5)
    length = prompt_lengths[0]
    local_ids = jnp.arange(tok_here, dtype=jnp.int32)
    query_pos = row_positions(my_ctx * tok_here + local_ids, half_block, n_ctx)
    decode_pos = my_ctx * tok_here + local_ids
    query_three = query_states[0].reshape(tok_here, heads_dev, HD)
    run_max = jnp.full((heads_dev, tok_here), NEG, jnp.float32)
    kv_here = jnp.concatenate([key_states[0], value_states[0]], axis=1)
    kv_blocks, src_ctx = ctx_gather_blocks(kv_here, n_ctx, my_ctx)
    kv_all = kv_blocks.reshape(n_ctx * tok_here, 2 * feat_width)
    key_two = kv_all[:, :feat_width]
    value_two = kv_all[:, feat_width:]
    row_count = key_two.shape[0]
    row_ids = (src_ctx[:, None] * tok_here + local_ids[None, :]).reshape(row_count)
    key_pos = row_positions(row_ids, half_block, n_ctx)
    pick_rows = (decode_pos[:, None] == key_pos[None, :]).astype(jnp.bfloat16)
    kept_keys = jnp.dot(pick_rows, key_two, preferred_element_type=jnp.float32)
    kept_values = jnp.dot(pick_rows, value_two, preferred_element_type=jnp.float32)
    old_max = run_max
    key_heads = key_two.reshape(row_count, heads_dev, HD)
    value_heads = value_two.reshape(row_count, heads_dev, HD)
    logits = (
        jnp.einsum("qhd,khd->hqk", query_three, key_heads, preferred_element_type=jnp.float32)
        * score_scale
    )
    visible = (key_pos[None, :] <= query_pos[:, None]) & (key_pos[None, :] < length)
    logits = jnp.where(visible[None], logits, NEG)
    new_max = jnp.maximum(old_max, jnp.max(logits, axis=2))
    weights = jnp.where(visible[None], jnp.exp(logits - new_max[:, :, None]), 0.0)
    new_sum = jnp.sum(weights, axis=2)
    gained = jnp.einsum(
        "hqk,khd->hqd",
        weights.astype(jnp.bfloat16),
        value_heads,
        preferred_element_type=jnp.float32,
    )
    inner_state = (new_max, new_sum, gained)
    run_max, run_sum, run_out, kept_keys, kept_values = inner_state + (kept_keys, kept_values)
    mixed = (run_out / run_sum[:, :, None]).astype(jnp.bfloat16)
    mixed = jnp.transpose(mixed, (1, 0, 2)).reshape(tok_here, feat_width)
    out_parts = jnp.einsum(
        "tc,oc->to",
        mixed,
        lax.all_gather(out_weight, "ctx", axis=0, tiled=True),
        preferred_element_type=jnp.float32,
    )
    if lax.axis_size("exp") == 2:
        first_exp = lax.axis_index("exp") == 0
        residual_all = join(residual[0], exp_swap(residual[0]), first_exp, 0)
        head_all = out_parts + exp_swap(out_parts.astype(jnp.bfloat16)).astype(jnp.float32)
        stream_all = (residual_all.astype(jnp.float32) + head_all).astype(jnp.bfloat16)
        stream = halves(stream_all, first_exp, 0)[0]
        stream_f = stream_all.astype(jnp.float32)
    else:
        head_total = exp_reduce_rows(out_parts)
        stream = (residual[0].astype(jnp.float32) + head_total).astype(jnp.bfloat16)
        stream_f = stream.astype(jnp.float32)
    mean_sq = jnp.mean(stream_f * stream_f, axis=1, keepdims=True)
    normed = (stream_f * lax.rsqrt(mean_sq + EPS) * norm_gain).astype(jnp.bfloat16)
    capacity = min(tok_here, 2 * max(1, 3 * tok_here * TOP // (4 * n_ctx)))
    if lax.axis_size("exp") == 2:
        n_chip = n_ctx // 2

        def block_of(expert):
            other_core = (expert % 2 != my_ctx % 2).astype(jnp.int32)
            return other_core * n_chip + (expert // 2 - my_ctx // 2) % n_chip

        dispatch, combine = slot_tables(routes[0], route_weights[0], n_ctx, capacity, block_of)
        moe_rows = moe_column_halves(
            normed, dispatch, combine, gate_weight[0], up_weight[0], down_weight[0], n_ctx, capacity
        )
    else:
        dispatch, combine = slot_tables(routes[0], route_weights[0], n_ctx, capacity)
        moe_rows = moe_whole_rows(
            normed, dispatch, combine, gate_weight[0], up_weight[0], down_weight[0], n_ctx, capacity
        )
    layer_out = (stream.astype(jnp.float32) + moe_rows).astype(jnp.bfloat16)
    return (
        layer_out[None],
        kept_keys.astype(jnp.bfloat16)[None],
        kept_values.astype(jnp.bfloat16)[None],
    )


def solution(mesh):
    return jax.shard_map(
        local,
        mesh=mesh,
        in_specs=(
            P("req", "ctx", "exp"),
            P("req", "ctx", "exp"),
            P("req", "ctx", "exp"),
            P("req", ("ctx", "exp"), None),
            P("ctx", "exp"),
            P(),
            P("ctx", None, "exp"),
            P("ctx", None, "exp"),
            P("ctx", "exp", None),
            P("req", "ctx", None),
            P("req", "ctx", None),
            P("req"),
        ),
        out_specs=(P("req", ("ctx", "exp"), None), P("req", "ctx", "exp"), P("req", "ctx", "exp")),
        check_vma=False,
    )
```

```python
import jax
import jax.numpy as jnp
from jax import lax
from jax.sharding import PartitionSpec as P

D = 2048
HD = 128
TOP = 4


EPS = 1e-06
NEG = -1e30


def row_positions(row_ids, half_block, n_groups):
    block_ids = row_ids // half_block
    device = block_ids // 2
    target = jnp.where(block_ids % 2 == 0, device, 2 * n_groups - 1 - device)
    return target * half_block + row_ids % half_block


def slot_tables(route_block, weight_block, experts, capacity, block_of=None):
    tok_here, top_here = route_block.shape
    flat_ids = route_block.reshape(tok_here * top_here)
    hit_table = (flat_ids[:, None] == jnp.arange(experts, dtype=jnp.int32)[None, :]).astype(
        jnp.int32
    )
    before = jnp.cumsum(hit_table, axis=0) - hit_table
    slot_rank = jnp.sum(before * hit_table, axis=1)
    blocks = flat_ids if block_of is None else block_of(flat_ids)
    slot_index = blocks * capacity + slot_rank
    slot_match = (
        jnp.arange(experts * capacity, dtype=jnp.int32)[:, None] == slot_index[None, :]
    ).astype(jnp.float32)
    slot_match = slot_match.reshape(experts * capacity, tok_here, top_here)
    dispatch = jnp.sum(slot_match, axis=2)
    combine = jnp.transpose(jnp.sum(slot_match * weight_block[None, :, :], axis=2))
    return (dispatch, combine)


def expert_ffn(token_rows, gate_matrix, up_matrix, down_matrix):
    gate_act = jnp.dot(token_rows, gate_matrix, preferred_element_type=jnp.float32)
    up_act = jnp.dot(token_rows, up_matrix, preferred_element_type=jnp.float32)
    hidden = (jax.nn.silu(gate_act) * up_act).astype(jnp.bfloat16)
    return jnp.dot(hidden, down_matrix, preferred_element_type=jnp.float32)


def exp_swap(x):
    return lax.ppermute(x, "exp", perm=[(0, 1), (1, 0)])


def exp_reduce_rows(parts):
    if lax.axis_size("exp") != 2:
        return lax.psum_scatter(
            parts.astype(jnp.bfloat16), "exp", scatter_dimension=0, tiled=True
        ).astype(jnp.float32)
    half = parts.shape[0] // 2
    first = lax.axis_index("exp") == 0
    lower = parts[:half]
    upper = parts[half:]
    mine = jnp.where(first, lower, upper)
    theirs = jnp.where(first, upper, lower)
    got = exp_swap(theirs.astype(jnp.bfloat16))
    return mine + got.astype(jnp.float32)


def exp_gather_rows(rows):
    if lax.axis_size("exp") != 2:
        return lax.all_gather(rows, "exp", axis=0, tiled=True)
    got = exp_swap(rows)
    first = lax.axis_index("exp") == 0
    return jnp.where(
        first, jnp.concatenate([rows, got], axis=0), jnp.concatenate([got, rows], axis=0)
    )


def moe_whole_rows(normed, dispatch, combine, gate_matrix, up_matrix, down_matrix, n_ctx, capacity):
    all_normed = lax.all_gather(normed, "exp", axis=0, tiled=True)
    send_rows = jnp.dot(
        dispatch.astype(jnp.bfloat16), all_normed, preferred_element_type=jnp.float32
    ).astype(jnp.bfloat16)
    send_rows = send_rows.reshape(n_ctx, capacity, D)
    arrived = lax.all_to_all(send_rows, "ctx", split_axis=0, concat_axis=0, tiled=True)
    flat_rows = arrived.reshape(n_ctx * capacity, D)
    produced = expert_ffn(flat_rows, gate_matrix, up_matrix, down_matrix).reshape(
        n_ctx, capacity, D
    )
    served = lax.all_to_all(
        produced.astype(jnp.bfloat16), "ctx", split_axis=0, concat_axis=0, tiled=True
    )
    results = served.reshape(n_ctx * capacity, D).astype(jnp.float32)
    moe_part = jnp.dot(
        combine, results, precision=lax.Precision.HIGHEST, preferred_element_type=jnp.float32
    )
    return lax.psum_scatter(
        moe_part.astype(jnp.bfloat16), "exp", scatter_dimension=0, tiled=True
    ).astype(jnp.float32)


def halves(x, first, axis):
    size = x.shape[axis] // 2
    lower = lax.slice_in_dim(x, 0, size, axis=axis)
    upper = lax.slice_in_dim(x, size, 2 * size, axis=axis)
    return jnp.where(first, lower, upper), jnp.where(first, upper, lower)


def join(mine, theirs, first, axis):
    return jnp.where(
        first,
        jnp.concatenate([mine, theirs], axis=axis),
        jnp.concatenate([theirs, mine], axis=axis),
    )


def moe_column_halves(normed, dispatch, combine, gate_matrix, up_matrix, down_matrix, n_ctx, capacity):
    my_exp = lax.axis_index("exp")
    first = my_exp == 0
    half_d = normed.shape[1] // 2
    tokens_cols = halves(normed, first, 1)[0]
    tok_count = tokens_cols.shape[0]
    my_ctx = lax.axis_index("ctx")
    n_chip = n_ctx // 2
    my_chip = my_ctx // 2
    my_core = my_ctx % 2
    dispatch_parts = dispatch.reshape(2, n_chip, capacity, tok_count)
    full_d = normed.shape[1]
    near = jnp.dot(
        dispatch_parts[:, 0].reshape(2 * capacity, tok_count).astype(jnp.bfloat16),
        normed,
        preferred_element_type=jnp.float32,
    ).astype(jnp.bfloat16)
    near = near.reshape(2, capacity, full_d)
    far = jnp.dot(
        dispatch_parts[:, 1:].reshape(2 * (n_chip - 1) * capacity, tok_count).astype(jnp.bfloat16),
        tokens_cols,
        preferred_element_type=jnp.float32,
    ).astype(jnp.bfloat16)
    far = far.reshape(2, n_chip - 1, capacity, half_d)
    core_swap = [(i, i ^ 1) for i in range(n_ctx)]
    near_in = jnp.concatenate(
        [near[0], lax.ppermute(near[1], "ctx", perm=core_swap)], axis=0
    )
    far_pairs = jnp.stack([far[0], lax.ppermute(far[1], "ctx", perm=core_swap)], axis=1)
    arrived = [None]
    for shift in range(1, n_chip):
        perm = [(i, ((i // 2 + shift) % n_chip) * 2 + i % 2) for i in range(n_ctx)]
        arrived.append(lax.ppermute(far_pairs[shift - 1], "ctx", perm=perm))
    my_start = my_exp * half_d
    other_start = (1 - my_exp) * half_d
    gate_mine = lax.dynamic_slice_in_dim(gate_matrix, my_start, half_d, axis=0)
    gate_other = lax.dynamic_slice_in_dim(gate_matrix, other_start, half_d, axis=0)
    up_mine = lax.dynamic_slice_in_dim(up_matrix, my_start, half_d, axis=0)
    up_other = lax.dynamic_slice_in_dim(up_matrix, other_start, half_d, axis=0)
    down_other = lax.dynamic_slice_in_dim(down_matrix, other_start, half_d, axis=1)
    down_mine = lax.dynamic_slice_in_dim(down_matrix, my_start, half_d, axis=1)
    if n_chip <= 4:
        groups = [[0]] + [[k] for k in range(1, n_chip)]
    else:
        groups = [[0], list(range(1, n_chip // 2)), list(range(n_chip // 2, n_chip))]
    returned = [None] * n_chip
    returned_partner = [None] * n_chip
    for shifts in groups:
        if shifts == [0]:
            gate_act = jnp.dot(near_in, gate_matrix, preferred_element_type=jnp.float32)
            up_act = jnp.dot(near_in, up_matrix, preferred_element_type=jnp.float32)
        else:
            block = jnp.concatenate([arrived[k] for k in shifts], axis=0).reshape(-1, half_d)
            partner_cols = exp_swap(block)
            gate_act = jnp.dot(block, gate_mine, preferred_element_type=jnp.float32) + jnp.dot(
                partner_cols, gate_other, preferred_element_type=jnp.float32
            )
            up_act = jnp.dot(block, up_mine, preferred_element_type=jnp.float32) + jnp.dot(
                partner_cols, up_other, preferred_element_type=jnp.float32
            )
        hidden = (jax.nn.silu(gate_act) * up_act).astype(jnp.bfloat16)
        out_other = jnp.dot(hidden, down_other, preferred_element_type=jnp.float32)
        got_other = exp_swap(out_other.astype(jnp.bfloat16))
        out_mine = jnp.dot(hidden, down_mine, preferred_element_type=jnp.float32)
        summed = (out_mine + got_other.astype(jnp.float32)).astype(jnp.bfloat16)
        summed = summed.reshape(len(shifts), 2, capacity, half_d)
        for idx, shift in enumerate(shifts):
            if shift == 0:
                returned[shift] = summed[idx][0]
                returned_partner[shift] = lax.ppermute(summed[idx][1], "ctx", perm=core_swap)
            else:
                perm = [(i, ((i // 2 - shift) % n_chip) * 2 + i % 2) for i in range(n_ctx)]
                returned[shift] = lax.ppermute(summed[idx][0], "ctx", perm=perm)
                perm = [(i, ((i // 2 - shift) % n_chip) * 2 + 1 - i % 2) for i in range(n_ctx)]
                returned_partner[shift] = lax.ppermute(summed[idx][1], "ctx", perm=perm)
    served = jnp.stack([jnp.stack(returned), jnp.stack(returned_partner)])
    served = served.reshape(n_ctx * capacity, half_d)
    weight_hi = combine.astype(jnp.bfloat16)
    weight_lo = (combine - weight_hi.astype(jnp.float32)).astype(jnp.bfloat16)
    moe_half = jnp.dot(weight_hi, served, preferred_element_type=jnp.float32) + jnp.dot(
        weight_lo, served, preferred_element_type=jnp.float32
    )
    my_tok, other_tok = halves(moe_half, first, 0)
    got_tok = exp_swap(other_tok.astype(jnp.bfloat16)).astype(jnp.float32)
    return join(my_tok, got_tok, first, 1)


def ctx_gather_blocks(rows, n_ctx, my_ctx):
    n_chip = n_ctx // 2
    my_chip = my_ctx // 2
    my_core = my_ctx % 2
    stack = [rows]
    for shift in range(1, n_chip):
        perm = [(i, ((i // 2 + shift) % n_chip) * 2 + i % 2) for i in range(n_ctx)]
        stack.append(lax.ppermute(rows, "ctx", perm=perm))
    own = jnp.stack(stack)
    partner = lax.ppermute(own, "ctx", perm=[(i, i ^ 1) for i in range(n_ctx)])
    shifts = jnp.arange(n_chip, dtype=jnp.int32)
    chips = (my_chip - shifts) % n_chip
    src_ctx = jnp.concatenate([chips * 2 + my_core, chips * 2 + (1 - my_core)])
    return jnp.concatenate([own, partner]), src_ctx


def local(
    query_states,
    key_states,
    value_states,
    residual,
    out_weight,
    norm_gain,
    gate_weight,
    up_weight,
    down_weight,
    routes,
    route_weights,
    prompt_lengths,
):
    n_ctx = lax.axis_size("ctx")
    my_ctx = lax.axis_index("ctx")
    tok_here = query_states.shape[1]
    feat_width = query_states.shape[2]
    heads_dev = feat_width // HD
    half_block = tok_here // 2
    score_scale = HD ** (-0.5)
    length = prompt_lengths[0]
    local_ids = jnp.arange(tok_here, dtype=jnp.int32)
    query_pos = row_positions(my_ctx * tok_here + local_ids, half_block, n_ctx)
    decode_pos = my_ctx * tok_here + local_ids
    query_three = query_states[0].reshape(tok_here, heads_dev, HD)
    run_max = jnp.full((heads_dev, tok_here), NEG, jnp.float32)
    kv_here = jnp.concatenate([key_states[0], value_states[0]], axis=1)
    kv_blocks, src_ctx = ctx_gather_blocks(kv_here, n_ctx, my_ctx)
    kv_all = kv_blocks.reshape(n_ctx * tok_here, 2 * feat_width)
    key_two = kv_all[:, :feat_width]
    value_two = kv_all[:, feat_width:]
    row_count = key_two.shape[0]
    row_ids = (src_ctx[:, None] * tok_here + local_ids[None, :]).reshape(row_count)
    key_pos = row_positions(row_ids, half_block, n_ctx)
    pick_rows = (decode_pos[:, None] == key_pos[None, :]).astype(jnp.bfloat16)
    kept_keys = jnp.dot(pick_rows, key_two, preferred_element_type=jnp.float32)
    kept_values = jnp.dot(pick_rows, value_two, preferred_element_type=jnp.float32)
    old_max = run_max
    key_heads = key_two.reshape(row_count, heads_dev, HD)
    value_heads = value_two.reshape(row_count, heads_dev, HD)
    logits = (
        jnp.einsum("qhd,khd->hqk", query_three, key_heads, preferred_element_type=jnp.float32)
        * score_scale
    )
    visible = (key_pos[None, :] <= query_pos[:, None]) & (key_pos[None, :] < length)
    logits = jnp.where(visible[None], logits, NEG)
    new_max = jnp.maximum(old_max, jnp.max(logits, axis=2))
    weights = jnp.where(visible[None], jnp.exp(logits - new_max[:, :, None]), 0.0)
    new_sum = jnp.sum(weights, axis=2)
    gained = jnp.einsum(
        "hqk,khd->hqd",
        weights.astype(jnp.bfloat16),
        value_heads,
        preferred_element_type=jnp.float32,
    )
    inner_state = (new_max, new_sum, gained)
    run_max, run_sum, run_out, kept_keys, kept_values = inner_state + (kept_keys, kept_values)
    mixed = (run_out / run_sum[:, :, None]).astype(jnp.bfloat16)
    mixed = jnp.transpose(mixed, (1, 0, 2)).reshape(tok_here, feat_width)
    out_parts = jnp.einsum(
        "tc,oc->to",
        mixed,
        lax.all_gather(out_weight, "ctx", axis=0, tiled=True),
        preferred_element_type=jnp.float32,
    )
    if lax.axis_size("exp") == 2:
        first_exp = lax.axis_index("exp") == 0
        sent = jnp.concatenate([out_parts.astype(jnp.bfloat16), residual[0]], axis=0)
        got = exp_swap(sent)
        residual_all = join(residual[0], got[out_parts.shape[0]:], first_exp, 0)
        head_all = out_parts + got[: out_parts.shape[0]].astype(jnp.float32)
        stream_all = (residual_all.astype(jnp.float32) + head_all).astype(jnp.bfloat16)
        stream = halves(stream_all, first_exp, 0)[0]
        stream_f = stream_all.astype(jnp.float32)
    else:
        head_total = exp_reduce_rows(out_parts)
        stream = (residual[0].astype(jnp.float32) + head_total).astype(jnp.bfloat16)
        stream_f = stream.astype(jnp.float32)
    mean_sq = jnp.mean(stream_f * stream_f, axis=1, keepdims=True)
    normed = (stream_f * lax.rsqrt(mean_sq + EPS) * norm_gain).astype(jnp.bfloat16)
    capacity = min(tok_here, 2 * max(1, 3 * tok_here * TOP // (4 * n_ctx)))
    if lax.axis_size("exp") == 2:
        n_chip = n_ctx // 2

        def block_of(expert):
            other_core = (expert % 2 != my_ctx % 2).astype(jnp.int32)
            return other_core * n_chip + (expert // 2 - my_ctx // 2) % n_chip

        dispatch, combine = slot_tables(routes[0], route_weights[0], n_ctx, capacity, block_of)
        moe_rows = moe_column_halves(
            normed, dispatch, combine, gate_weight[0], up_weight[0], down_weight[0], n_ctx, capacity
        )
    else:
        dispatch, combine = slot_tables(routes[0], route_weights[0], n_ctx, capacity)
        moe_rows = moe_whole_rows(
            normed, dispatch, combine, gate_weight[0], up_weight[0], down_weight[0], n_ctx, capacity
        )
    layer_out = (stream.astype(jnp.float32) + moe_rows).astype(jnp.bfloat16)
    return (
        layer_out[None],
        kept_keys.astype(jnp.bfloat16)[None],
        kept_values.astype(jnp.bfloat16)[None],
    )


def solution(mesh):
    return jax.shard_map(
        local,
        mesh=mesh,
        in_specs=(
            P("req", "ctx", "exp"),
            P("req", "ctx", "exp"),
            P("req", "ctx", "exp"),
            P("req", ("ctx", "exp"), None),
            P("ctx", "exp"),
            P(),
            P("ctx", None, "exp"),
            P("ctx", None, "exp"),
            P("ctx", "exp", None),
            P("req", "ctx", None),
            P("req", "ctx", None),
            P("req"),
        ),
        out_specs=(P("req", ("ctx", "exp"), None), P("req", "ctx", "exp"), P("req", "ctx", "exp")),
        check_vma=False,
    )
```

```python
import jax
import jax.numpy as jnp
from jax import lax
from jax.sharding import PartitionSpec as P

D = 2048
HD = 128
TOP = 4


EPS = 1e-06
NEG = -1e30


def row_positions(row_ids, half_block, n_groups):
    block_ids = row_ids // half_block
    device = block_ids // 2
    target = jnp.where(block_ids % 2 == 0, device, 2 * n_groups - 1 - device)
    return target * half_block + row_ids % half_block


def slot_tables(route_block, weight_block, experts, capacity, block_of=None):
    tok_here, top_here = route_block.shape
    flat_ids = route_block.reshape(tok_here * top_here)
    hit_table = (flat_ids[:, None] == jnp.arange(experts, dtype=jnp.int32)[None, :]).astype(
        jnp.int32
    )
    before = jnp.cumsum(hit_table, axis=0) - hit_table
    slot_rank = jnp.sum(before * hit_table, axis=1)
    blocks = flat_ids if block_of is None else block_of(flat_ids)
    slot_index = blocks * capacity + slot_rank
    slot_match = (
        jnp.arange(experts * capacity, dtype=jnp.int32)[:, None] == slot_index[None, :]
    ).astype(jnp.float32)
    slot_match = slot_match.reshape(experts * capacity, tok_here, top_here)
    dispatch = jnp.sum(slot_match, axis=2)
    combine = jnp.transpose(jnp.sum(slot_match * weight_block[None, :, :], axis=2))
    return (dispatch, combine)


def expert_ffn(token_rows, gate_matrix, up_matrix, down_matrix):
    gate_act = jnp.dot(token_rows, gate_matrix, preferred_element_type=jnp.float32)
    up_act = jnp.dot(token_rows, up_matrix, preferred_element_type=jnp.float32)
    hidden = (jax.nn.silu(gate_act) * up_act).astype(jnp.bfloat16)
    return jnp.dot(hidden, down_matrix, preferred_element_type=jnp.float32)


def exp_swap(x):
    return lax.ppermute(x, "exp", perm=[(0, 1), (1, 0)])


def exp_reduce_rows(parts):
    if lax.axis_size("exp") != 2:
        return lax.psum_scatter(
            parts.astype(jnp.bfloat16), "exp", scatter_dimension=0, tiled=True
        ).astype(jnp.float32)
    half = parts.shape[0] // 2
    first = lax.axis_index("exp") == 0
    lower = parts[:half]
    upper = parts[half:]
    mine = jnp.where(first, lower, upper)
    theirs = jnp.where(first, upper, lower)
    got = exp_swap(theirs.astype(jnp.bfloat16))
    return mine + got.astype(jnp.float32)


def exp_gather_rows(rows):
    if lax.axis_size("exp") != 2:
        return lax.all_gather(rows, "exp", axis=0, tiled=True)
    got = exp_swap(rows)
    first = lax.axis_index("exp") == 0
    return jnp.where(
        first, jnp.concatenate([rows, got], axis=0), jnp.concatenate([got, rows], axis=0)
    )


def moe_whole_rows(normed, dispatch, combine, gate_matrix, up_matrix, down_matrix, n_ctx, capacity):
    all_normed = lax.all_gather(normed, "exp", axis=0, tiled=True)
    send_rows = jnp.dot(
        dispatch.astype(jnp.bfloat16), all_normed, preferred_element_type=jnp.float32
    ).astype(jnp.bfloat16)
    send_rows = send_rows.reshape(n_ctx, capacity, D)
    arrived = lax.all_to_all(send_rows, "ctx", split_axis=0, concat_axis=0, tiled=True)
    flat_rows = arrived.reshape(n_ctx * capacity, D)
    produced = expert_ffn(flat_rows, gate_matrix, up_matrix, down_matrix).reshape(
        n_ctx, capacity, D
    )
    served = lax.all_to_all(
        produced.astype(jnp.bfloat16), "ctx", split_axis=0, concat_axis=0, tiled=True
    )
    results = served.reshape(n_ctx * capacity, D).astype(jnp.float32)
    moe_part = jnp.dot(
        combine, results, precision=lax.Precision.HIGHEST, preferred_element_type=jnp.float32
    )
    return lax.psum_scatter(
        moe_part.astype(jnp.bfloat16), "exp", scatter_dimension=0, tiled=True
    ).astype(jnp.float32)


def halves(x, first, axis):
    size = x.shape[axis] // 2
    lower = lax.slice_in_dim(x, 0, size, axis=axis)
    upper = lax.slice_in_dim(x, size, 2 * size, axis=axis)
    return jnp.where(first, lower, upper), jnp.where(first, upper, lower)


def join(mine, theirs, first, axis):
    return jnp.where(
        first,
        jnp.concatenate([mine, theirs], axis=axis),
        jnp.concatenate([theirs, mine], axis=axis),
    )


def moe_column_halves(normed, dispatch, combine, gate_matrix, up_matrix, down_matrix, n_ctx, capacity):
    my_exp = lax.axis_index("exp")
    first = my_exp == 0
    half_d = normed.shape[1] // 2
    tokens_cols = halves(normed, first, 1)[0]
    tok_count = tokens_cols.shape[0]
    my_ctx = lax.axis_index("ctx")
    n_chip = n_ctx // 2
    my_chip = my_ctx // 2
    my_core = my_ctx % 2
    dispatch_parts = dispatch.reshape(2, n_chip, capacity, tok_count)
    full_d = normed.shape[1]
    near = jnp.dot(
        dispatch_parts[:, 0].reshape(2 * capacity, tok_count).astype(jnp.bfloat16),
        normed,
        preferred_element_type=jnp.float32,
    ).astype(jnp.bfloat16)
    near = near.reshape(2, capacity, full_d)
    far = jnp.dot(
        dispatch_parts[:, 1:].reshape(2 * (n_chip - 1) * capacity, tok_count).astype(jnp.bfloat16),
        tokens_cols,
        preferred_element_type=jnp.float32,
    ).astype(jnp.bfloat16)
    far = far.reshape(2, n_chip - 1, capacity, half_d)
    core_swap = [(i, i ^ 1) for i in range(n_ctx)]
    near_in = jnp.concatenate(
        [near[0], lax.ppermute(near[1], "ctx", perm=core_swap)], axis=0
    )
    far_pairs = jnp.stack([far[0], lax.ppermute(far[1], "ctx", perm=core_swap)], axis=1)
    arrived = [None]
    for shift in range(1, n_chip):
        perm = [(i, ((i // 2 + shift) % n_chip) * 2 + i % 2) for i in range(n_ctx)]
        arrived.append(lax.ppermute(far_pairs[shift - 1], "ctx", perm=perm))
    my_start = my_exp * half_d
    other_start = (1 - my_exp) * half_d
    gate_mine = lax.dynamic_slice_in_dim(gate_matrix, my_start, half_d, axis=0)
    gate_other = lax.dynamic_slice_in_dim(gate_matrix, other_start, half_d, axis=0)
    up_mine = lax.dynamic_slice_in_dim(up_matrix, my_start, half_d, axis=0)
    up_other = lax.dynamic_slice_in_dim(up_matrix, other_start, half_d, axis=0)
    down_other = lax.dynamic_slice_in_dim(down_matrix, other_start, half_d, axis=1)
    down_mine = lax.dynamic_slice_in_dim(down_matrix, my_start, half_d, axis=1)
    if n_chip <= 4:
        groups = [[0]] + [[k] for k in range(1, n_chip)]
    else:
        groups = [[0], list(range(1, n_chip // 2)), list(range(n_chip // 2, n_chip))]
    returned = [None] * n_chip
    returned_partner = [None] * n_chip
    for shifts in groups:
        if shifts == [0]:
            gate_act = jnp.dot(near_in, gate_matrix, preferred_element_type=jnp.float32)
            up_act = jnp.dot(near_in, up_matrix, preferred_element_type=jnp.float32)
        else:
            block = jnp.concatenate([arrived[k] for k in shifts], axis=0).reshape(-1, half_d)
            partner_cols = exp_swap(block)
            gate_act = jnp.dot(block, gate_mine, preferred_element_type=jnp.float32) + jnp.dot(
                partner_cols, gate_other, preferred_element_type=jnp.float32
            )
            up_act = jnp.dot(block, up_mine, preferred_element_type=jnp.float32) + jnp.dot(
                partner_cols, up_other, preferred_element_type=jnp.float32
            )
        hidden = (jax.nn.silu(gate_act) * up_act).astype(jnp.bfloat16)
        out_other = jnp.dot(hidden, down_other, preferred_element_type=jnp.float32)
        got_other = exp_swap(out_other.astype(jnp.bfloat16))
        out_mine = jnp.dot(hidden, down_mine, preferred_element_type=jnp.float32)
        summed = (out_mine + got_other.astype(jnp.float32)).astype(jnp.bfloat16)
        summed = summed.reshape(len(shifts), 2, capacity, half_d)
        for idx, shift in enumerate(shifts):
            if shift == 0:
                returned[shift] = summed[idx][0]
                returned_partner[shift] = lax.ppermute(summed[idx][1], "ctx", perm=core_swap)
            else:
                perm = [(i, ((i // 2 - shift) % n_chip) * 2 + i % 2) for i in range(n_ctx)]
                returned[shift] = lax.ppermute(summed[idx][0], "ctx", perm=perm)
                perm = [(i, ((i // 2 - shift) % n_chip) * 2 + 1 - i % 2) for i in range(n_ctx)]
                returned_partner[shift] = lax.ppermute(summed[idx][1], "ctx", perm=perm)
    served = jnp.stack([jnp.stack(returned), jnp.stack(returned_partner)])
    served = served.reshape(n_ctx * capacity, half_d)
    weight_hi = combine.astype(jnp.bfloat16)
    weight_lo = (combine - weight_hi.astype(jnp.float32)).astype(jnp.bfloat16)
    moe_half = jnp.dot(weight_hi, served, preferred_element_type=jnp.float32) + jnp.dot(
        weight_lo, served, preferred_element_type=jnp.float32
    )
    my_tok, other_tok = halves(moe_half, first, 0)
    got_tok = exp_swap(other_tok.astype(jnp.bfloat16)).astype(jnp.float32)
    return join(my_tok, got_tok, first, 1)


def ctx_gather_blocks(rows, n_ctx, my_ctx):
    n_chip = n_ctx // 2
    my_chip = my_ctx // 2
    my_core = my_ctx % 2
    stack = [rows]
    for shift in range(1, n_chip):
        perm = [(i, ((i // 2 + shift) % n_chip) * 2 + i % 2) for i in range(n_ctx)]
        stack.append(lax.ppermute(rows, "ctx", perm=perm))
    own = jnp.stack(stack)
    partner = lax.ppermute(own, "ctx", perm=[(i, i ^ 1) for i in range(n_ctx)])
    shifts = jnp.arange(n_chip, dtype=jnp.int32)
    chips = (my_chip - shifts) % n_chip
    src_ctx = jnp.concatenate([chips * 2 + my_core, chips * 2 + (1 - my_core)])
    return jnp.concatenate([own, partner]), src_ctx


def local(
    query_states,
    key_states,
    value_states,
    residual,
    out_weight,
    norm_gain,
    gate_weight,
    up_weight,
    down_weight,
    routes,
    route_weights,
    prompt_lengths,
):
    n_ctx = lax.axis_size("ctx")
    my_ctx = lax.axis_index("ctx")
    tok_here = query_states.shape[1]
    feat_width = query_states.shape[2]
    heads_dev = feat_width // HD
    half_block = tok_here // 2
    score_scale = HD ** (-0.5)
    length = prompt_lengths[0]
    local_ids = jnp.arange(tok_here, dtype=jnp.int32)
    query_pos = row_positions(my_ctx * tok_here + local_ids, half_block, n_ctx)
    decode_pos = my_ctx * tok_here + local_ids
    query_three = query_states[0].reshape(tok_here, heads_dev, HD)
    run_max = jnp.full((heads_dev, tok_here), NEG, jnp.float32)
    kv_here = jnp.concatenate([key_states[0], value_states[0]], axis=1)
    kv_blocks, src_ctx = ctx_gather_blocks(kv_here, n_ctx, my_ctx)
    kv_all = kv_blocks.reshape(n_ctx * tok_here, 2 * feat_width)
    key_two = kv_all[:, :feat_width]
    value_two = kv_all[:, feat_width:]
    row_count = key_two.shape[0]
    row_ids = (src_ctx[:, None] * tok_here + local_ids[None, :]).reshape(row_count)
    key_pos = row_positions(row_ids, half_block, n_ctx)
    pick_rows = (decode_pos[:, None] == key_pos[None, :]).astype(jnp.bfloat16)
    kept_keys = jnp.dot(pick_rows, key_two, preferred_element_type=jnp.float32)
    kept_values = jnp.dot(pick_rows, value_two, preferred_element_type=jnp.float32)
    old_max = run_max
    key_heads = key_two.reshape(row_count, heads_dev, HD)
    value_heads = value_two.reshape(row_count, heads_dev, HD)
    logits = (
        jnp.einsum("qhd,khd->hqk", query_three, key_heads, preferred_element_type=jnp.float32)
        * score_scale
    )
    visible = (key_pos[None, :] <= query_pos[:, None]) & (key_pos[None, :] < length)
    logits = jnp.where(visible[None], logits, NEG)
    new_max = jnp.maximum(old_max, jnp.max(logits, axis=2))
    weights = jnp.where(visible[None], jnp.exp(logits - new_max[:, :, None]), 0.0)
    new_sum = jnp.sum(weights, axis=2)
    gained = jnp.einsum(
        "hqk,khd->hqd",
        weights.astype(jnp.bfloat16),
        value_heads,
        preferred_element_type=jnp.float32,
    )
    inner_state = (new_max, new_sum, gained)
    run_max, run_sum, run_out, kept_keys, kept_values = inner_state + (kept_keys, kept_values)
    mixed = (run_out / run_sum[:, :, None]).astype(jnp.bfloat16)
    mixed = jnp.transpose(mixed, (1, 0, 2)).reshape(tok_here, feat_width)
    out_parts = jnp.einsum(
        "tc,oc->to",
        mixed,
        lax.all_gather(out_weight, "ctx", axis=0, tiled=True),
        preferred_element_type=jnp.float32,
    )
    if lax.axis_size("exp") == 2:
        first_exp = lax.axis_index("exp") == 0
        residual_all = join(residual[0], exp_swap(residual[0]), first_exp, 0)
        split = out_parts.shape[0] // 2
        head_parts = []
        for part in (out_parts[:split], out_parts[split:]):
            head_parts.append(part + exp_swap(part.astype(jnp.bfloat16)).astype(jnp.float32))
        head_all = jnp.concatenate(head_parts, axis=0)
        stream_all = (residual_all.astype(jnp.float32) + head_all).astype(jnp.bfloat16)
        stream = halves(stream_all, first_exp, 0)[0]
        stream_f = stream_all.astype(jnp.float32)
    else:
        head_total = exp_reduce_rows(out_parts)
        stream = (residual[0].astype(jnp.float32) + head_total).astype(jnp.bfloat16)
        stream_f = stream.astype(jnp.float32)
    mean_sq = jnp.mean(stream_f * stream_f, axis=1, keepdims=True)
    normed = (stream_f * lax.rsqrt(mean_sq + EPS) * norm_gain).astype(jnp.bfloat16)
    capacity = min(tok_here, 2 * max(1, 3 * tok_here * TOP // (4 * n_ctx)))
    if lax.axis_size("exp") == 2:
        n_chip = n_ctx // 2

        def block_of(expert):
            other_core = (expert % 2 != my_ctx % 2).astype(jnp.int32)
            return other_core * n_chip + (expert // 2 - my_ctx // 2) % n_chip

        dispatch, combine = slot_tables(routes[0], route_weights[0], n_ctx, capacity, block_of)
        moe_rows = moe_column_halves(
            normed, dispatch, combine, gate_weight[0], up_weight[0], down_weight[0], n_ctx, capacity
        )
    else:
        dispatch, combine = slot_tables(routes[0], route_weights[0], n_ctx, capacity)
        moe_rows = moe_whole_rows(
            normed, dispatch, combine, gate_weight[0], up_weight[0], down_weight[0], n_ctx, capacity
        )
    layer_out = (stream.astype(jnp.float32) + moe_rows).astype(jnp.bfloat16)
    return (
        layer_out[None],
        kept_keys.astype(jnp.bfloat16)[None],
        kept_values.astype(jnp.bfloat16)[None],
    )


def solution(mesh):
    return jax.shard_map(
        local,
        mesh=mesh,
        in_specs=(
            P("req", "ctx", "exp"),
            P("req", "ctx", "exp"),
            P("req", "ctx", "exp"),
            P("req", ("ctx", "exp"), None),
            P("ctx", "exp"),
            P(),
            P("ctx", None, "exp"),
            P("ctx", None, "exp"),
            P("ctx", "exp", None),
            P("req", "ctx", None),
            P("req", "ctx", None),
            P("req"),
        ),
        out_specs=(P("req", ("ctx", "exp"), None), P("req", "ctx", "exp"), P("req", "ctx", "exp")),
        check_vma=False,
    )
```

```python
import jax
import jax.numpy as jnp
from jax import lax
from jax.sharding import PartitionSpec as P

D = 2048
HD = 128
TOP = 4


EPS = 1e-06
NEG = -1e30


def row_positions(row_ids, half_block, n_groups):
    block_ids = row_ids // half_block
    device = block_ids // 2
    target = jnp.where(block_ids % 2 == 0, device, 2 * n_groups - 1 - device)
    return target * half_block + row_ids % half_block


def slot_tables(route_block, weight_block, experts, capacity, block_of=None):
    tok_here, top_here = route_block.shape
    flat_ids = route_block.reshape(tok_here * top_here)
    hit_table = (flat_ids[:, None] == jnp.arange(experts, dtype=jnp.int32)[None, :]).astype(
        jnp.int32
    )
    before = jnp.cumsum(hit_table, axis=0) - hit_table
    slot_rank = jnp.sum(before * hit_table, axis=1)
    blocks = flat_ids if block_of is None else block_of(flat_ids)
    slot_index = blocks * capacity + slot_rank
    slot_match = (
        jnp.arange(experts * capacity, dtype=jnp.int32)[:, None] == slot_index[None, :]
    ).astype(jnp.float32)
    slot_match = slot_match.reshape(experts * capacity, tok_here, top_here)
    dispatch = jnp.sum(slot_match, axis=2)
    combine = jnp.transpose(jnp.sum(slot_match * weight_block[None, :, :], axis=2))
    return (dispatch, combine)


def expert_ffn(token_rows, gate_matrix, up_matrix, down_matrix):
    gate_act = jnp.dot(token_rows, gate_matrix, preferred_element_type=jnp.float32)
    up_act = jnp.dot(token_rows, up_matrix, preferred_element_type=jnp.float32)
    hidden = (jax.nn.silu(gate_act) * up_act).astype(jnp.bfloat16)
    return jnp.dot(hidden, down_matrix, preferred_element_type=jnp.float32)


def exp_swap(x):
    return lax.ppermute(x, "exp", perm=[(0, 1), (1, 0)])


def exp_reduce_rows(parts):
    if lax.axis_size("exp") != 2:
        return lax.psum_scatter(
            parts.astype(jnp.bfloat16), "exp", scatter_dimension=0, tiled=True
        ).astype(jnp.float32)
    half = parts.shape[0] // 2
    first = lax.axis_index("exp") == 0
    lower = parts[:half]
    upper = parts[half:]
    mine = jnp.where(first, lower, upper)
    theirs = jnp.where(first, upper, lower)
    got = exp_swap(theirs.astype(jnp.bfloat16))
    return mine + got.astype(jnp.float32)


def exp_gather_rows(rows):
    if lax.axis_size("exp") != 2:
        return lax.all_gather(rows, "exp", axis=0, tiled=True)
    got = exp_swap(rows)
    first = lax.axis_index("exp") == 0
    return jnp.where(
        first, jnp.concatenate([rows, got], axis=0), jnp.concatenate([got, rows], axis=0)
    )


def moe_whole_rows(normed, dispatch, combine, gate_matrix, up_matrix, down_matrix, n_ctx, capacity):
    all_normed = lax.all_gather(normed, "exp", axis=0, tiled=True)
    send_rows = jnp.dot(
        dispatch.astype(jnp.bfloat16), all_normed, preferred_element_type=jnp.float32
    ).astype(jnp.bfloat16)
    send_rows = send_rows.reshape(n_ctx, capacity, D)
    arrived = lax.all_to_all(send_rows, "ctx", split_axis=0, concat_axis=0, tiled=True)
    flat_rows = arrived.reshape(n_ctx * capacity, D)
    produced = expert_ffn(flat_rows, gate_matrix, up_matrix, down_matrix).reshape(
        n_ctx, capacity, D
    )
    served = lax.all_to_all(
        produced.astype(jnp.bfloat16), "ctx", split_axis=0, concat_axis=0, tiled=True
    )
    results = served.reshape(n_ctx * capacity, D).astype(jnp.float32)
    moe_part = jnp.dot(
        combine, results, precision=lax.Precision.HIGHEST, preferred_element_type=jnp.float32
    )
    return lax.psum_scatter(
        moe_part.astype(jnp.bfloat16), "exp", scatter_dimension=0, tiled=True
    ).astype(jnp.float32)


def halves(x, first, axis):
    size = x.shape[axis] // 2
    lower = lax.slice_in_dim(x, 0, size, axis=axis)
    upper = lax.slice_in_dim(x, size, 2 * size, axis=axis)
    return jnp.where(first, lower, upper), jnp.where(first, upper, lower)


def join(mine, theirs, first, axis):
    return jnp.where(
        first,
        jnp.concatenate([mine, theirs], axis=axis),
        jnp.concatenate([theirs, mine], axis=axis),
    )


def moe_column_halves(normed, dispatch, combine, gate_matrix, up_matrix, down_matrix, n_ctx, capacity):
    my_exp = lax.axis_index("exp")
    first = my_exp == 0
    half_d = normed.shape[1] // 2
    tokens_cols = halves(normed, first, 1)[0]
    tok_count = tokens_cols.shape[0]
    my_ctx = lax.axis_index("ctx")
    n_chip = n_ctx // 2
    my_chip = my_ctx // 2
    my_core = my_ctx % 2
    dispatch_parts = dispatch.reshape(2, n_chip, capacity, tok_count)
    full_d = normed.shape[1]
    near = jnp.dot(
        dispatch_parts[:, 0].reshape(2 * capacity, tok_count).astype(jnp.bfloat16),
        normed,
        preferred_element_type=jnp.float32,
    ).astype(jnp.bfloat16)
    near = near.reshape(2, capacity, full_d)
    far = jnp.dot(
        dispatch_parts[:, 1:].reshape(2 * (n_chip - 1) * capacity, tok_count).astype(jnp.bfloat16),
        tokens_cols,
        preferred_element_type=jnp.float32,
    ).astype(jnp.bfloat16)
    far = far.reshape(2, n_chip - 1, capacity, half_d)
    core_swap = [(i, i ^ 1) for i in range(n_ctx)]
    near_in = jnp.concatenate(
        [near[0], lax.ppermute(near[1], "ctx", perm=core_swap)], axis=0
    )
    far_pairs = jnp.stack([far[0], lax.ppermute(far[1], "ctx", perm=core_swap)], axis=1)
    arrived = [None]
    for shift in range(1, n_chip):
        perm = [(i, ((i // 2 + shift) % n_chip) * 2 + i % 2) for i in range(n_ctx)]
        arrived.append(lax.ppermute(far_pairs[shift - 1], "ctx", perm=perm))
    my_start = my_exp * half_d
    other_start = (1 - my_exp) * half_d
    gate_mine = lax.dynamic_slice_in_dim(gate_matrix, my_start, half_d, axis=0)
    gate_other = lax.dynamic_slice_in_dim(gate_matrix, other_start, half_d, axis=0)
    up_mine = lax.dynamic_slice_in_dim(up_matrix, my_start, half_d, axis=0)
    up_other = lax.dynamic_slice_in_dim(up_matrix, other_start, half_d, axis=0)
    down_other = lax.dynamic_slice_in_dim(down_matrix, other_start, half_d, axis=1)
    down_mine = lax.dynamic_slice_in_dim(down_matrix, my_start, half_d, axis=1)
    if n_chip <= 4:
        groups = [[0]] + [[k] for k in range(1, n_chip)]
    else:
        groups = [[0], list(range(1, n_chip // 2)), list(range(n_chip // 2, n_chip))]
    returned = [None] * n_chip
    returned_partner = [None] * n_chip
    for shifts in groups:
        if shifts == [0]:
            gate_act = jnp.dot(near_in, gate_matrix, preferred_element_type=jnp.float32)
            up_act = jnp.dot(near_in, up_matrix, preferred_element_type=jnp.float32)
        else:
            block = jnp.concatenate([arrived[k] for k in shifts], axis=0).reshape(-1, half_d)
            partner_cols = exp_swap(block)
            gate_act = jnp.dot(block, gate_mine, preferred_element_type=jnp.float32) + jnp.dot(
                partner_cols, gate_other, preferred_element_type=jnp.float32
            )
            up_act = jnp.dot(block, up_mine, preferred_element_type=jnp.float32) + jnp.dot(
                partner_cols, up_other, preferred_element_type=jnp.float32
            )
        hidden = (jax.nn.silu(gate_act) * up_act).astype(jnp.bfloat16)
        out_other = jnp.dot(hidden, down_other, preferred_element_type=jnp.float32)
        got_other = exp_swap(out_other.astype(jnp.bfloat16))
        out_mine = jnp.dot(hidden, down_mine, preferred_element_type=jnp.float32)
        summed = (out_mine + got_other.astype(jnp.float32)).astype(jnp.bfloat16)
        summed = summed.reshape(len(shifts), 2, capacity, half_d)
        for idx, shift in enumerate(shifts):
            if shift == 0:
                returned[shift] = summed[idx][0]
                returned_partner[shift] = lax.ppermute(summed[idx][1], "ctx", perm=core_swap)
            else:
                perm = [(i, ((i // 2 - shift) % n_chip) * 2 + i % 2) for i in range(n_ctx)]
                returned[shift] = lax.ppermute(summed[idx][0], "ctx", perm=perm)
                perm = [(i, ((i // 2 - shift) % n_chip) * 2 + 1 - i % 2) for i in range(n_ctx)]
                returned_partner[shift] = lax.ppermute(summed[idx][1], "ctx", perm=perm)
    served = jnp.stack([jnp.stack(returned), jnp.stack(returned_partner)])
    served = served.reshape(n_ctx * capacity, half_d)
    weight_hi = combine.astype(jnp.bfloat16)
    weight_lo = (combine - weight_hi.astype(jnp.float32)).astype(jnp.bfloat16)
    quarter = half_d // 2
    mine_parts = []
    got_parts = []
    for cols in (served[:, :quarter], served[:, quarter:]):
        moe_part = jnp.dot(weight_hi, cols, preferred_element_type=jnp.float32) + jnp.dot(
            weight_lo, cols, preferred_element_type=jnp.float32
        )
        my_tok, other_tok = halves(moe_part, first, 0)
        mine_parts.append(my_tok)
        got_parts.append(exp_swap(other_tok.astype(jnp.bfloat16)).astype(jnp.float32))
    my_tok = jnp.concatenate(mine_parts, axis=1)
    got_tok = jnp.concatenate(got_parts, axis=1)
    return join(my_tok, got_tok, first, 1)


def ctx_gather_blocks(rows, n_ctx, my_ctx):
    n_chip = n_ctx // 2
    my_chip = my_ctx // 2
    my_core = my_ctx % 2
    stack = [rows]
    for shift in range(1, n_chip):
        perm = [(i, ((i // 2 + shift) % n_chip) * 2 + i % 2) for i in range(n_ctx)]
        stack.append(lax.ppermute(rows, "ctx", perm=perm))
    own = jnp.stack(stack)
    partner = lax.ppermute(own, "ctx", perm=[(i, i ^ 1) for i in range(n_ctx)])
    shifts = jnp.arange(n_chip, dtype=jnp.int32)
    chips = (my_chip - shifts) % n_chip
    src_ctx = jnp.concatenate([chips * 2 + my_core, chips * 2 + (1 - my_core)])
    return jnp.concatenate([own, partner]), src_ctx


def local(
    query_states,
    key_states,
    value_states,
    residual,
    out_weight,
    norm_gain,
    gate_weight,
    up_weight,
    down_weight,
    routes,
    route_weights,
    prompt_lengths,
):
    n_ctx = lax.axis_size("ctx")
    my_ctx = lax.axis_index("ctx")
    tok_here = query_states.shape[1]
    feat_width = query_states.shape[2]
    heads_dev = feat_width // HD
    half_block = tok_here // 2
    score_scale = HD ** (-0.5)
    length = prompt_lengths[0]
    local_ids = jnp.arange(tok_here, dtype=jnp.int32)
    query_pos = row_positions(my_ctx * tok_here + local_ids, half_block, n_ctx)
    decode_pos = my_ctx * tok_here + local_ids
    query_three = query_states[0].reshape(tok_here, heads_dev, HD)
    run_max = jnp.full((heads_dev, tok_here), NEG, jnp.float32)
    kv_here = jnp.concatenate([key_states[0], value_states[0]], axis=1)
    kv_blocks, src_ctx = ctx_gather_blocks(kv_here, n_ctx, my_ctx)
    kv_all = kv_blocks.reshape(n_ctx * tok_here, 2 * feat_width)
    key_two = kv_all[:, :feat_width]
    value_two = kv_all[:, feat_width:]
    row_count = key_two.shape[0]
    row_ids = (src_ctx[:, None] * tok_here + local_ids[None, :]).reshape(row_count)
    key_pos = row_positions(row_ids, half_block, n_ctx)
    pick_rows = (decode_pos[:, None] == key_pos[None, :]).astype(jnp.bfloat16)
    kept_keys = jnp.dot(pick_rows, key_two, preferred_element_type=jnp.float32)
    kept_values = jnp.dot(pick_rows, value_two, preferred_element_type=jnp.float32)
    old_max = run_max
    key_heads = key_two.reshape(row_count, heads_dev, HD)
    value_heads = value_two.reshape(row_count, heads_dev, HD)
    logits = (
        jnp.einsum("qhd,khd->hqk", query_three, key_heads, preferred_element_type=jnp.float32)
        * score_scale
    )
    visible = (key_pos[None, :] <= query_pos[:, None]) & (key_pos[None, :] < length)
    logits = jnp.where(visible[None], logits, NEG)
    new_max = jnp.maximum(old_max, jnp.max(logits, axis=2))
    weights = jnp.where(visible[None], jnp.exp(logits - new_max[:, :, None]), 0.0)
    new_sum = jnp.sum(weights, axis=2)
    gained = jnp.einsum(
        "hqk,khd->hqd",
        weights.astype(jnp.bfloat16),
        value_heads,
        preferred_element_type=jnp.float32,
    )
    inner_state = (new_max, new_sum, gained)
    run_max, run_sum, run_out, kept_keys, kept_values = inner_state + (kept_keys, kept_values)
    mixed = (run_out / run_sum[:, :, None]).astype(jnp.bfloat16)
    mixed = jnp.transpose(mixed, (1, 0, 2)).reshape(tok_here, feat_width)
    out_parts = jnp.einsum(
        "tc,oc->to",
        mixed,
        lax.all_gather(out_weight, "ctx", axis=0, tiled=True),
        preferred_element_type=jnp.float32,
    )
    if lax.axis_size("exp") == 2:
        first_exp = lax.axis_index("exp") == 0
        residual_all = join(residual[0], exp_swap(residual[0]), first_exp, 0)
        split = out_parts.shape[0] // 2
        head_parts = []
        for part in (out_parts[:split], out_parts[split:]):
            head_parts.append(part + exp_swap(part.astype(jnp.bfloat16)).astype(jnp.float32))
        head_all = jnp.concatenate(head_parts, axis=0)
        stream_all = (residual_all.astype(jnp.float32) + head_all).astype(jnp.bfloat16)
        stream = halves(stream_all, first_exp, 0)[0]
        stream_f = stream_all.astype(jnp.float32)
    else:
        head_total = exp_reduce_rows(out_parts)
        stream = (residual[0].astype(jnp.float32) + head_total).astype(jnp.bfloat16)
        stream_f = stream.astype(jnp.float32)
    mean_sq = jnp.mean(stream_f * stream_f, axis=1, keepdims=True)
    normed = (stream_f * lax.rsqrt(mean_sq + EPS) * norm_gain).astype(jnp.bfloat16)
    capacity = min(tok_here, 2 * max(1, 3 * tok_here * TOP // (4 * n_ctx)))
    if lax.axis_size("exp") == 2:
        n_chip = n_ctx // 2

        def block_of(expert):
            other_core = (expert % 2 != my_ctx % 2).astype(jnp.int32)
            return other_core * n_chip + (expert // 2 - my_ctx // 2) % n_chip

        dispatch, combine = slot_tables(routes[0], route_weights[0], n_ctx, capacity, block_of)
        moe_rows = moe_column_halves(
            normed, dispatch, combine, gate_weight[0], up_weight[0], down_weight[0], n_ctx, capacity
        )
    else:
        dispatch, combine = slot_tables(routes[0], route_weights[0], n_ctx, capacity)
        moe_rows = moe_whole_rows(
            normed, dispatch, combine, gate_weight[0], up_weight[0], down_weight[0], n_ctx, capacity
        )
    layer_out = (stream.astype(jnp.float32) + moe_rows).astype(jnp.bfloat16)
    return (
        layer_out[None],
        kept_keys.astype(jnp.bfloat16)[None],
        kept_values.astype(jnp.bfloat16)[None],
    )


def solution(mesh):
    return jax.shard_map(
        local,
        mesh=mesh,
        in_specs=(
            P("req", "ctx", "exp"),
            P("req", "ctx", "exp"),
            P("req", "ctx", "exp"),
            P("req", ("ctx", "exp"), None),
            P("ctx", "exp"),
            P(),
            P("ctx", None, "exp"),
            P("ctx", None, "exp"),
            P("ctx", "exp", None),
            P("req", "ctx", None),
            P("req", "ctx", None),
            P("req"),
        ),
        out_specs=(P("req", ("ctx", "exp"), None), P("req", "ctx", "exp"), P("req", "ctx", "exp")),
        check_vma=False,
    )
```
